32 devices in a mesh: req: 4 (over z), ctx: 8 (over y, x, core).
Axes of the slice: x: 2, y: 2, z: 4, core: 2. Of those that a mesh axis runs over, the one named last changes fastest.
Arguments:
- hidden_in: bfloat16 [4096, 2048], P(('req', 'ctx')), may hold values from -3 to 3
- queries: bfloat16 [4096, 1024], P(('req', 'ctx')), may hold values from -10 to 10
- span_keys: bfloat16 [4096, 1024], P(('req', 'ctx')), may hold values from -10 to 10
- span_values: bfloat16 [4096, 1024], P(('req', 'ctx')), may hold values from -6 to 6
- cache_keys: bfloat16 [6144, 1024], P(('req', 'ctx')), may hold values from -6 to 6
- cache_values: bfloat16 [6144, 1024], P(('req', 'ctx')), may hold values from -6 to 6
- cache_lengths: int32 [4], replicated, may hold values from 0 to 1536, as said below
- slot_request: int32 [4], replicated, may hold values from 0 to 3, each once
- out_weight: bfloat16 [1024, 2048], replicated, may hold values from -1.5 to 1.5
- norm_gain: float32 [2048], replicated, may hold values from 0.1 to 1.9
- expert_ids: int32 [4096, 8], P(('req', 'ctx')), may hold values from 0 to 15, all different within a row; in each aligned block of 128 rows (0 to 127, 128 to 255, ...) at most 128 rows name the same one
- expert_gates: float32 [4096, 8], P(('req', 'ctx')), may hold values from 0.05 to 0.5
- gate_proj: bfloat16 [16, 2048, 512], P('ctx'), may hold values from -0.125 to 0.125
- up_proj: bfloat16 [16, 2048, 512], P('ctx'), may hold values from -0.125 to 0.125
- down_proj: bfloat16 [16, 512, 2048], P('ctx'), may hold values from -0.25 to 0.25
Outputs:
- layer_out: bfloat16 [4096, 2048], P(('req', 'ctx'))
The draws below stay inside these ranges and needn't reach their ends.
Inputs may be any that keep to these rules, and one draw needn't show every extreme that they name: `cache_lengths`: some request has exactly 1536 cached positions.
All inputs are finite; a program needn't handle non-finite values.
Results may differ from the reference program's by a relative error of at most 0.015.
Values may be sent and summed in bfloat16 or wider, within the bound.
No kernel may reach another device: no remote copies, remote signals or barrier semaphores. Data moves between devices by JAX's collectives and lax.ppermute only.
A program may use at most 192 MiB of HBM per device.

```python
import math
import jax
import jax.numpy as jnp
import numpy as np
from jax import lax

D = 2048
HEAD_DIM = 128
TOPK = 8
HEADS = 8
FF_E = 512
TOK_DEV = 128
HQ = 1024
SPAN = 1024
CACHE = 1536
SLOTS = 4
EXPERTS = 16
CAP = 128
N_CTX = 8


def paired_fields(base_key):
    row_count = SLOTS * SPAN
    field_shape = (row_count, HQ)
    subkeys = jax.random.split(jax.random.fold_in(base_key, 97), 4)
    query_field = jnp.clip(jax.random.normal(subkeys[2], field_shape, jnp.float32), -6.0, 6.0)
    key_field = jnp.clip(jax.random.normal(subkeys[3], field_shape, jnp.float32), -6.0, 6.0)
    return (query_field, key_field)


def draw_queries(key, part):
    return paired_fields(key)[0].astype(jnp.bfloat16)


def draw_span_keys(key, part):
    return paired_fields(key)[1].astype(jnp.bfloat16)


def draw_cache_lengths(key, part):
    first_key, second_key = jax.random.split(jax.random.fold_in(key, 31))
    drawn = jax.random.randint(first_key, (SLOTS,), 0, CACHE + 1)
    chosen = jax.random.randint(second_key, (), 0, SLOTS)
    return jnp.where(jnp.arange(SLOTS) == chosen, CACHE, drawn).astype(jnp.int32)


def shard_levels(key, shape, cuts, low, high):
    level = 1.0
    for dim, parts in cuts:
        steps = jax.random.uniform(jax.random.fold_in(jax.random.fold_in(key, 6), dim), (parts,), jnp.float32, low / len(cuts), high / len(cuts))
        level = level * jnp.repeat(jnp.exp(steps), shape[dim] // parts).reshape((-1,) + (1,) * (len(shape) - 1 - dim))
    return level


def deal_out(own_key, own, number, rows, amount, top, most, lean):
    sequence = jax.random.permutation(own_key, amount)
    heavy_load, common = portions_of(amount, rows * top, most, lean, True), portions_of(amount, rows * top, most, lean, False)
    places = jnp.arange(amount)

    def named(lengths, rotation):
        used = int((lengths > 0).sum())
        fixed = max(1, used // 4)
        passed = fixed + (places - fixed + rotation * (used - fixed)) % max(1, amount - fixed)
        return jnp.zeros((amount,), jnp.int32).at[sequence[jnp.where(places < fixed, places, passed)]].set(jnp.asarray(lengths, jnp.int32))

    lengths = jnp.where(number % 4 == 0, named(heavy_load, number // 4), named(common, number - number // 4 - 1))
    mixed = jax.random.permutation(jax.random.fold_in(own, 3), amount)
    donor, sink = mixed[0:amount // 2 * 2:2], mixed[1:amount // 2 * 2:2]
    room = jnp.minimum(lengths[donor] - 1, most - lengths[sink]) // 2
    room = jnp.where((donor == sequence[0]) | (sink == sequence[0]) | (lengths[sink] == 0), 0, jnp.maximum(room, 0))
    passed = jax.random.randint(jax.random.fold_in(own, 4), (amount // 2,), 0, 1 << 20) % (room + 1)
    lengths = lengths.at[donor].add(-passed).at[sink].add(passed)
    labels = jnp.searchsorted(jnp.cumsum(lengths), jnp.arange(rows * top), side="right").astype(jnp.int32)
    listing = labels.reshape(top, rows).T
    listing = listing[jax.random.permutation(jax.random.fold_in(own, 1), rows)]
    rotation = jax.random.randint(jax.random.fold_in(own, 2), (rows, 1), 0, top)
    return jnp.take_along_axis(listing, (jnp.arange(top)[None, :] + rotation) % top, axis=1)


def portions_of(count, total, limit, skew, full):
    loads = [(1 << 20) // math.isqrt(grade ** skew) + 1 for grade in range(1, count + 1)]
    largest = limit if full else min(limit, max(-(-total // count), total * loads[0] // sum(loads)))
    least = 1 if total - largest >= count - 1 else 0
    holding, rest = [largest] + [least] * (count - 1), total - largest - least * (count - 1)
    while rest > 0:
        candidates = [i for i in range(1, count) if holding[i] < largest] or [i for i in range(1, count) if holding[i] < limit]
        pool, remaining = sum([loads[i] for i in candidates]), rest
        for i in candidates:
            extra = min(limit - holding[i], max(1, remaining * loads[i] // pool), rest)
            holding[i] = holding[i] + extra
            rest = rest - extra
    return np.array(holding)


def gaussian(rng, extent, width, reach, shards=(), kind=jnp.bfloat16):
    values = width * jax.random.normal(rng, extent, jnp.float32)
    if shards:
        values = values * shard_levels(rng, extent, shards, -0.22, 0.18)
    return jnp.clip(values, -reach, reach).astype(kind)


def setup_inputs(seed: int = 0) -> dict:
    arg_keys = jax.random.split(jax.random.key(seed), 16)
    hidden_in = gaussian(arg_keys[0], (SLOTS * SPAN, D), 0.5, 3.0, ((0, 32),))
    queries = draw_queries(jax.random.fold_in(arg_keys[15], 71), 0)
    span_keys = draw_span_keys(jax.random.fold_in(arg_keys[15], 71), 0)
    span_values = gaussian(arg_keys[3], (SLOTS * SPAN, HQ), 1.0, 6.0, ((0, 32),))
    cache_keys = gaussian(arg_keys[4], (SLOTS * CACHE, HQ), 1.0, 6.0, ((0, 32),))
    cache_values = gaussian(arg_keys[5], (SLOTS * CACHE, HQ), 1.0, 6.0, ((0, 32),))
    cache_lengths = draw_cache_lengths(jax.random.fold_in(arg_keys[15], 71), 0)
    slot_request = jax.random.permutation(arg_keys[7], SLOTS).astype(jnp.int32)
    out_weight = gaussian(arg_keys[8], (HQ, D), (max(HQ // 64, 1)) ** -0.5, 1.5)
    norm_gain = jnp.clip(1.0 + 0.18 * jax.random.normal(arg_keys[9], (D,), jnp.float32), 0.1, 1.9)
    expert_ids_keys = jax.random.split(jax.random.fold_in(arg_keys[10], 1), (SLOTS * SPAN) // TOK_DEV)
    expert_ids_turns = jax.random.permutation(jax.random.fold_in(arg_keys[10], 3), (SLOTS * SPAN) // TOK_DEV)
    expert_ids = jax.vmap(lambda own, number: deal_out(jax.random.fold_in(arg_keys[10], 2), own, number, TOK_DEV, EXPERTS, TOPK, CAP, 2))(expert_ids_keys, expert_ids_turns).reshape((SLOTS * SPAN, TOPK))
    expert_gates = jnp.clip(jnp.exp(math.log(0.5) - 2.3025851 * jax.random.uniform(arg_keys[11], (SLOTS * SPAN, TOPK), jnp.float32) ** shard_levels(arg_keys[11], (SLOTS * SPAN, TOPK), ((0, 32),), -0.2, 0.2)), 0.05, 0.5)
    gate_proj = gaussian(arg_keys[12], (EXPERTS, D, FF_E), D ** -0.5, 0.125, ((0, 8),))
    up_proj = gaussian(arg_keys[13], (EXPERTS, D, FF_E), D ** -0.5, 0.125, ((0, 8),))
    down_proj = gaussian(arg_keys[14], (EXPERTS, FF_E, D), FF_E ** -0.5, 0.25, ((0, 8),))
    return {"hidden_in": hidden_in, "queries": queries, "span_keys": span_keys, "span_values": span_values, "cache_keys": cache_keys, "cache_values": cache_values, "cache_lengths": cache_lengths, "slot_request": slot_request, "out_weight": out_weight, "norm_gain": norm_gain, "expert_ids": expert_ids, "expert_gates": expert_gates, "gate_proj": gate_proj, "up_proj": up_proj, "down_proj": down_proj}


def split_heads(matrix):
    return matrix.reshape(matrix.shape[0], HEADS, HEAD_DIM).transpose(1, 0, 2)

def attend_slot(operands):
    query_rows, span_k, span_v, stored_k, stored_v, cached_len = operands
    all_keys = jnp.concatenate([span_k, stored_k], 0)
    all_values = jnp.concatenate([span_v, stored_v], 0)
    positions = jnp.arange(all_keys.shape[0], dtype=jnp.int32)
    usable = (positions < SPAN) | (positions - SPAN < cached_len)
    scaling = 1.0 / math.sqrt(HEAD_DIM)

    def per_head(head_ops):
        head_q, head_k, head_v = head_ops
        scores = jnp.dot(head_q, head_k.T, preferred_element_type=jnp.float32) * scaling
        scores = jnp.where(usable[None, :], scores, -1e+30)
        peak = lax.optimization_barrier(jnp.max(scores, axis=1, keepdims=True))
        weights = jnp.where(usable[None, :], jnp.exp(scores - peak), 0.0)
        total = lax.optimization_barrier(jnp.sum(weights, axis=1, keepdims=True))
        summed = jnp.dot(weights.astype(jnp.bfloat16), head_v, preferred_element_type=jnp.float32)
        return (summed / total).astype(jnp.bfloat16)
    outputs = lax.map(per_head, (split_heads(query_rows), split_heads(all_keys), split_heads(all_values)))
    return outputs.transpose(1, 0, 2).reshape(SPAN, HQ)

def reference(hidden_in, queries, span_keys, span_values, cache_keys, cache_values, cache_lengths, slot_request, out_weight, norm_gain, expert_ids, expert_gates, gate_proj, up_proj, down_proj):
    slot_lengths = cache_lengths[slot_request]
    attended = lax.map(attend_slot, (queries.reshape(SLOTS, SPAN, HQ), span_keys.reshape(SLOTS, SPAN, HQ), span_values.reshape(SLOTS, SPAN, HQ), cache_keys.reshape(SLOTS, CACHE, HQ), cache_values.reshape(SLOTS, CACHE, HQ), slot_lengths))
    attended = attended.reshape(SLOTS * SPAN, HQ)
    residual = hidden_in.astype(jnp.float32) + jnp.dot(attended, out_weight, preferred_element_type=jnp.float32)
    mean_square = lax.optimization_barrier(jnp.mean(residual * residual, axis=1, keepdims=True))
    normed = (residual * lax.rsqrt(mean_square + 1e-06) * norm_gain).astype(jnp.bfloat16)
    token_total = SLOTS * SPAN
    flat_ids = expert_ids.reshape(-1)
    flat_gates = expert_gates.reshape(-1)
    source_token = jnp.arange(token_total * TOPK, dtype=jnp.int32) // TOPK
    capacity = SLOTS * N_CTX * CAP

    def one_expert(mixed, operands):
        expert_index, gate_w, up_w, down_w = operands
        chosen = (flat_ids == expert_index).astype(jnp.int32)
        order = jnp.cumsum(chosen) - 1
        target = jnp.where(chosen == 1, order, capacity)
        slot_token = jnp.zeros((capacity,), jnp.int32).at[target].set(source_token, mode='drop')
        slot_gate = jnp.zeros((capacity,), jnp.float32).at[target].set(flat_gates, mode='drop')
        gathered = normed[slot_token]
        gate_val = jnp.dot(gathered, gate_w, preferred_element_type=jnp.float32)
        up_val = jnp.dot(gathered, up_w, preferred_element_type=jnp.float32)
        activated = (jax.nn.silu(gate_val) * up_val).astype(jnp.bfloat16)
        produced = jnp.dot(activated, down_w, preferred_element_type=jnp.float32).astype(jnp.bfloat16)
        mixed = mixed.at[slot_token].add(slot_gate[:, None] * produced.astype(jnp.float32))
        return (mixed, None)
    mixed, unused = lax.scan(one_expert, residual, (jnp.arange(EXPERTS, dtype=jnp.int32), gate_proj, up_proj, down_proj))
    final = mixed.astype(jnp.bfloat16).reshape(SLOTS, SPAN, D)
    layer_out = jnp.zeros_like(final).at[slot_request].set(final)
    return layer_out.reshape(SLOTS * SPAN, D)
```

```python
import math

import jax
import jax.numpy as jnp
from jax import lax
from jax.sharding import PartitionSpec as P

HEAD_DIM = 128


def attend_gathered(queries, span_keys, span_values, cache_keys, cache_values, length):
    token_count, column_count = queries.shape
    head_count = column_count // HEAD_DIM
    cached_rows = cache_keys.shape[0]
    block_rows = token_count + cached_rows
    scaling = 1.0 / math.sqrt(HEAD_DIM)
    key_block = jnp.concatenate([span_keys, cache_keys], 0)
    value_block = jnp.concatenate([span_values, cache_values], 0)
    piece_keys = lax.all_gather(key_block, "ctx", axis=0, tiled=True)
    piece_values = lax.all_gather(value_block, "ctx", axis=0, tiled=True)
    piece_rows = piece_keys.shape[0]
    index = jnp.arange(piece_rows, dtype=jnp.int32)
    owner = index // block_rows
    within = index % block_rows
    usable = (within < token_count) | (owner * cached_rows + within - token_count < length)
    scores = (
        jnp.einsum(
            "thd,phd->htp",
            queries.reshape(token_count, head_count, HEAD_DIM),
            piece_keys.reshape(piece_rows, head_count, HEAD_DIM),
            preferred_element_type=jnp.float32,
        )
        * scaling
    )
    scores = jnp.where(usable[None, None, :], scores, -1e30)
    peak = jnp.max(scores, axis=2, keepdims=True)
    weights = jnp.where(usable[None, None, :], jnp.exp(scores - peak), 0.0)
    total = jnp.sum(weights, axis=2)
    accum = jnp.einsum(
        "htp,phd->htd",
        weights.astype(jnp.bfloat16),
        piece_values.reshape(piece_rows, head_count, HEAD_DIM),
        preferred_element_type=jnp.float32,
    )
    return (
        (accum / total[:, :, None])
        .transpose(1, 0, 2)
        .reshape(token_count, column_count)
        .astype(jnp.bfloat16)
    )


def attend_by_head(queries, span_keys, span_values, cache_keys, cache_values, length):
    token_count, column_count = queries.shape
    head_count = column_count // HEAD_DIM
    cached_rows = cache_keys.shape[0]
    ctx_count = lax.axis_size("ctx")
    local_heads = head_count // ctx_count
    width = local_heads * HEAD_DIM
    scaling = 1.0 / math.sqrt(HEAD_DIM)
    block_rows = token_count + cached_rows
    packed = jnp.concatenate(
        [queries, span_keys, cache_keys, span_values, cache_values], 0
    )
    packed_rows = packed.shape[0]
    packed = packed.reshape(packed_rows, ctx_count, width)
    got = lax.all_to_all(packed, "ctx", split_axis=1, concat_axis=0, tiled=True)
    got = got.reshape(ctx_count, packed_rows, local_heads, HEAD_DIM)
    query_all = got[:, :token_count].reshape(ctx_count * token_count, local_heads, HEAD_DIM)
    key_all = got[:, token_count : token_count + block_rows].reshape(
        ctx_count * block_rows, local_heads, HEAD_DIM
    )
    value_all = got[:, token_count + block_rows :].reshape(
        ctx_count * block_rows, local_heads, HEAD_DIM
    )
    piece_rows = ctx_count * block_rows
    index = jnp.arange(piece_rows, dtype=jnp.int32)
    owner = index // block_rows
    within = index % block_rows
    usable = (within < token_count) | (owner * cached_rows + within - token_count < length)
    scores = (
        jnp.einsum("thd,phd->htp", query_all, key_all, preferred_element_type=jnp.float32)
        * scaling
    )
    scores = jnp.where(usable[None, None, :], scores, -1e30)
    peak = jnp.max(scores, axis=2, keepdims=True)
    weights = jnp.where(usable[None, None, :], jnp.exp(scores - peak), 0.0)
    total = jnp.sum(weights, axis=2)
    accum = jnp.einsum(
        "htp,phd->thd",
        weights.astype(jnp.bfloat16),
        value_all,
        preferred_element_type=jnp.float32,
    )
    head_out = (accum / total.T[:, :, None]).astype(jnp.bfloat16)
    head_out = head_out.reshape(ctx_count, token_count, width)
    back = lax.all_to_all(head_out, "ctx", split_axis=0, concat_axis=0, tiled=True)
    return back.transpose(1, 0, 2).reshape(token_count, column_count)


def on_device(
    hidden_in,
    queries,
    span_keys,
    span_values,
    cache_keys,
    cache_values,
    cache_lengths,
    slot_request,
    out_weight,
    norm_gain,
    expert_ids,
    expert_gates,
    gate_proj,
    up_proj,
    down_proj,
):
    token_count, feature_width = hidden_in.shape
    column_count = queries.shape[1]
    head_count = column_count // HEAD_DIM
    ctx_count = lax.axis_size("ctx")
    slot_place = lax.axis_index("req")
    slot_count = slot_request.shape[0]
    slot_range = jnp.arange(slot_count, dtype=jnp.int32)
    request = jnp.sum(jnp.where(slot_range == slot_place, slot_request, 0))
    length = jnp.sum(jnp.where(slot_range == request, cache_lengths, 0))
    if head_count % ctx_count == 0:
        attended = attend_by_head(
            queries, span_keys, span_values, cache_keys, cache_values, length
        )
    else:
        attended = attend_gathered(
            queries, span_keys, span_values, cache_keys, cache_values, length
        )
    residual = hidden_in.astype(jnp.float32) + jnp.dot(
        attended, out_weight, preferred_element_type=jnp.float32
    )
    mean_square = jnp.mean(residual * residual, axis=1, keepdims=True)
    normed = (residual * lax.rsqrt(mean_square + 1e-06) * norm_gain).astype(jnp.bfloat16)

    local_experts = gate_proj.shape[0]
    normed_all = lax.all_gather(normed, "ctx", axis=0, tiled=True)
    ids_all = lax.all_gather(expert_ids, "ctx", axis=0, tiled=True)
    gates_all = lax.all_gather(expert_gates, "ctx", axis=0, tiled=True)
    first_expert = lax.axis_index("ctx") * local_experts
    moe = None
    for j in range(local_experts):
        weight = jnp.sum(jnp.where(ids_all == first_expert + j, gates_all, 0.0), axis=1)
        gate_val = jnp.dot(normed_all, gate_proj[j], preferred_element_type=jnp.float32)
        up_val = jnp.dot(normed_all, up_proj[j], preferred_element_type=jnp.float32)
        activated = (jax.nn.silu(gate_val) * up_val).astype(jnp.bfloat16)
        produced = jnp.dot(
            activated, down_proj[j], preferred_element_type=jnp.float32
        ).astype(jnp.bfloat16)
        term = weight[:, None] * produced.astype(jnp.float32)
        moe = term if moe is None else moe + term
    moe_rows = lax.psum_scatter(
        moe.astype(jnp.bfloat16), "ctx", scatter_dimension=0, tiled=True
    )
    final = (residual + moe_rows.astype(jnp.float32)).astype(jnp.bfloat16)

    source_slot = jnp.sum(jnp.where(slot_request == slot_place, slot_range, 0))
    piece = lax.all_gather(final, "req", axis=0, tiled=True)
    piece_rows = piece.shape[0]
    offset = source_slot * token_count
    inside = (offset >= 0) & (offset + token_count <= piece_rows)
    portion = lax.dynamic_slice_in_dim(
        piece, jnp.clip(offset, 0, piece_rows - token_count), token_count, 0
    )
    return jnp.where(inside, portion, jnp.zeros_like(final))


def solution(mesh):
    return jax.shard_map(
        on_device,
        mesh=mesh,
        in_specs=(
            P(("req", "ctx"), None),
            P(("req", "ctx"), None),
            P(("req", "ctx"), None),
            P(("req", "ctx"), None),
            P(("req", "ctx"), None),
            P(("req", "ctx"), None),
            P(),
            P(),
            P(),
            P(),
            P(("req", "ctx"), None),
            P(("req", "ctx"), None),
            P("ctx", None, None),
            P("ctx", None, None),
            P("ctx", None, None),
        ),
        out_specs=P(("req", "ctx"), None),
        check_vma=False,
    )
```

```python
import itertools
import math

import jax
import jax.numpy as jnp
from jax import lax
from jax.sharding import PartitionSpec as P

HEAD_DIM = 128


def attend_gathered(queries, span_keys, span_values, cache_keys, cache_values, length):
    token_count, column_count = queries.shape
    head_count = column_count // HEAD_DIM
    cached_rows = cache_keys.shape[0]
    block_rows = token_count + cached_rows
    scaling = 1.0 / math.sqrt(HEAD_DIM)
    key_block = jnp.concatenate([span_keys, cache_keys], 0)
    value_block = jnp.concatenate([span_values, cache_values], 0)
    piece_keys = lax.all_gather(key_block, "ctx", axis=0, tiled=True)
    piece_values = lax.all_gather(value_block, "ctx", axis=0, tiled=True)
    piece_rows = piece_keys.shape[0]
    index = jnp.arange(piece_rows, dtype=jnp.int32)
    owner = index // block_rows
    within = index % block_rows
    usable = (within < token_count) | (owner * cached_rows + within - token_count < length)
    scores = (
        jnp.einsum(
            "thd,phd->htp",
            queries.reshape(token_count, head_count, HEAD_DIM),
            piece_keys.reshape(piece_rows, head_count, HEAD_DIM),
            preferred_element_type=jnp.float32,
        )
        * scaling
    )
    scores = jnp.where(usable[None, None, :], scores, -1e30)
    peak = jnp.max(scores, axis=2, keepdims=True)
    weights = jnp.where(usable[None, None, :], jnp.exp(scores - peak), 0.0)
    total = jnp.sum(weights, axis=2)
    accum = jnp.einsum(
        "htp,phd->htd",
        weights.astype(jnp.bfloat16),
        piece_values.reshape(piece_rows, head_count, HEAD_DIM),
        preferred_element_type=jnp.float32,
    )
    return (
        (accum / total[:, :, None])
        .transpose(1, 0, 2)
        .reshape(token_count, column_count)
        .astype(jnp.bfloat16)
    )


def attend_by_head(queries, span_keys, span_values, cache_keys, cache_values, length, extra):
    token_count, column_count = queries.shape
    head_count = column_count // HEAD_DIM
    cached_rows = cache_keys.shape[0]
    ctx_count = lax.axis_size("ctx")
    local_heads = head_count // ctx_count
    width = local_heads * HEAD_DIM
    scaling = 1.0 / math.sqrt(HEAD_DIM)
    block_rows = token_count + cached_rows
    packed = jnp.concatenate(
        [queries, span_keys, cache_keys, span_values, cache_values], 0
    )
    base_rows = packed.shape[0]
    packed = jnp.concatenate([packed.reshape(base_rows, ctx_count, width), extra], 0)
    packed_rows = packed.shape[0]
    got = lax.all_to_all(packed, "ctx", split_axis=1, concat_axis=0, tiled=True)
    got = got.reshape(ctx_count, packed_rows, local_heads, HEAD_DIM)
    query_all = got[:, :token_count].reshape(ctx_count * token_count, local_heads, HEAD_DIM)
    key_all = got[:, token_count : token_count + block_rows].reshape(
        ctx_count * block_rows, local_heads, HEAD_DIM
    )
    extra_got = got[:, base_rows:]
    value_all = got[:, token_count + block_rows : base_rows].reshape(
        ctx_count * block_rows, local_heads, HEAD_DIM
    )
    piece_rows = ctx_count * block_rows
    index = jnp.arange(piece_rows, dtype=jnp.int32)
    owner = index // block_rows
    within = index % block_rows
    usable = (within < token_count) | (owner * cached_rows + within - token_count < length)
    scores = (
        jnp.einsum("thd,phd->htp", query_all, key_all, preferred_element_type=jnp.float32)
        * scaling
    )
    scores = jnp.where(usable[None, None, :], scores, -1e30)
    peak = jnp.max(scores, axis=2, keepdims=True)
    weights = jnp.where(usable[None, None, :], jnp.exp(scores - peak), 0.0)
    total = jnp.sum(weights, axis=2)
    accum = jnp.einsum(
        "htp,phd->thd",
        weights.astype(jnp.bfloat16),
        value_all,
        preferred_element_type=jnp.float32,
    )
    head_out = (accum / total.T[:, :, None]).astype(jnp.bfloat16)
    head_out = head_out.reshape(ctx_count, token_count, width)
    back = lax.all_to_all(head_out, "ctx", split_axis=0, concat_axis=0, tiled=True)
    return back.transpose(1, 0, 2).reshape(token_count, column_count), extra_got


def on_device(
    hidden_in,
    queries,
    span_keys,
    span_values,
    cache_keys,
    cache_values,
    cache_lengths,
    slot_request,
    out_weight,
    norm_gain,
    expert_ids,
    expert_gates,
    gate_proj,
    up_proj,
    down_proj,
):
    token_count, feature_width = hidden_in.shape
    column_count = queries.shape[1]
    head_count = column_count // HEAD_DIM
    ctx_count = lax.axis_size("ctx")
    slot_place = lax.axis_index("req")
    slot_count = slot_request.shape[0]
    slot_range = jnp.arange(slot_count, dtype=jnp.int32)
    request = jnp.sum(jnp.where(slot_range == slot_place, slot_request, 0))
    length = jnp.sum(jnp.where(slot_range == request, cache_lengths, 0))
    local_experts = gate_proj.shape[0]
    expert_total = local_experts * ctx_count
    gate_matrix = jnp.sum(
        jnp.where(
            expert_ids[:, :, None] == jnp.arange(expert_total, dtype=jnp.int32)[None, None, :],
            expert_gates[:, :, None],
            0.0,
        ),
        axis=1,
    )
    first_expert = lax.axis_index("ctx") * local_experts
    if head_count % ctx_count == 0:
        width = column_count // ctx_count
        high = lax.reduce_precision(gate_matrix, exponent_bits=8, mantissa_bits=7)
        rest = gate_matrix - high
        middle = lax.reduce_precision(rest, exponent_bits=8, mantissa_bits=7)
        low = rest - middle
        parts = jnp.stack([high, middle, low], -1).astype(jnp.bfloat16)
        parts = parts.reshape(token_count, ctx_count, local_experts * 3)
        parts = parts.transpose(1, 0, 2).reshape(ctx_count, -1)
        part_len = parts.shape[1]
        part_rows = -(-part_len // width)
        parts = jnp.pad(parts, ((0, 0), (0, part_rows * width - part_len)))
        parts = parts.reshape(ctx_count, part_rows, width).transpose(1, 0, 2)
        attended, parts_got = attend_by_head(
            queries, span_keys, span_values, cache_keys, cache_values, length, parts
        )
        parts_got = parts_got.reshape(ctx_count, part_rows * width)[:, :part_len]
        parts_got = parts_got.reshape(ctx_count * token_count, local_experts, 3).astype(
            jnp.float32
        )
        local_gates = (parts_got[:, :, 0] + parts_got[:, :, 1]) + parts_got[:, :, 2]
    else:
        attended = attend_gathered(
            queries, span_keys, span_values, cache_keys, cache_values, length
        )
        local_gates = lax.all_gather(
            lax.dynamic_slice_in_dim(gate_matrix, first_expert, local_experts, 1),
            "ctx",
            axis=0,
            tiled=True,
        )
    residual = hidden_in.astype(jnp.float32) + jnp.dot(
        attended, out_weight, preferred_element_type=jnp.float32
    )
    mean_square = jnp.mean(residual * residual, axis=1, keepdims=True)
    normed = (residual * lax.rsqrt(mean_square + 1e-06) * norm_gain).astype(jnp.bfloat16)

    normed_all = lax.all_gather(normed, "ctx", axis=0, tiled=True)
    moe = None
    for j in range(local_experts):
        weight = local_gates[:, j]
        gate_val = jnp.dot(normed_all, gate_proj[j], preferred_element_type=jnp.float32)
        up_val = jnp.dot(normed_all, up_proj[j], preferred_element_type=jnp.float32)
        activated = (jax.nn.silu(gate_val) * up_val).astype(jnp.bfloat16)
        produced = jnp.dot(
            activated, down_proj[j], preferred_element_type=jnp.float32
        ).astype(jnp.bfloat16)
        term = weight[:, None] * produced.astype(jnp.float32)
        moe = term if moe is None else moe + term
    moe_rows = lax.psum_scatter(
        moe.astype(jnp.bfloat16), "ctx", scatter_dimension=0, tiled=True
    )
    final = (residual + moe_rows.astype(jnp.float32)).astype(jnp.bfloat16)

    return route_to_request(final, slot_request)


def route_to_request(final, slot_request):
    slot_count = slot_request.shape[0]
    token_count = final.shape[0]
    slot_range = jnp.arange(slot_count, dtype=jnp.int32)
    if slot_count <= 4:
        orders = list(itertools.permutations(range(slot_count)))
        table = jnp.array(orders, jnp.int32)
        match = jnp.all(table == slot_request[None, :], axis=1)
        choice = jnp.sum(jnp.where(match, jnp.arange(len(orders), dtype=jnp.int32), 0))

        def mover(order):
            pairs = [(g, order[g]) for g in range(slot_count)]
            if all(a == b for a, b in pairs):
                return lambda rows: rows
            return lambda rows: lax.ppermute(rows, "req", pairs)

        return lax.switch(choice, [mover(order) for order in orders], final)
    slot_place = lax.axis_index("req")
    source_slot = jnp.sum(jnp.where(slot_request == slot_place, slot_range, 0))
    piece = lax.all_gather(final, "req", axis=0, tiled=True)
    piece_rows = piece.shape[0]
    offset = source_slot * token_count
    inside = (offset >= 0) & (offset + token_count <= piece_rows)
    portion = lax.dynamic_slice_in_dim(
        piece, jnp.clip(offset, 0, piece_rows - token_count), token_count, 0
    )
    return jnp.where(inside, portion, jnp.zeros_like(final))


def solution(mesh):
    return jax.shard_map(
        on_device,
        mesh=mesh,
        in_specs=(
            P(("req", "ctx"), None),
            P(("req", "ctx"), None),
            P(("req", "ctx"), None),
            P(("req", "ctx"), None),
            P(("req", "ctx"), None),
            P(("req", "ctx"), None),
            P(),
            P(),
            P(),
            P(),
            P(("req", "ctx"), None),
            P(("req", "ctx"), None),
            P("ctx", None, None),
            P("ctx", None, None),
            P("ctx", None, None),
        ),
        out_specs=P(("req", "ctx"), None),
        check_vma=False,
    )
```

```python
import itertools
import math

import jax
import jax.numpy as jnp
from jax import lax
from jax.sharding import PartitionSpec as P

HEAD_DIM = 128


def attend_gathered(queries, span_keys, span_values, cache_keys, cache_values, length):
    token_count, column_count = queries.shape
    head_count = column_count // HEAD_DIM
    cached_rows = cache_keys.shape[0]
    block_rows = token_count + cached_rows
    scaling = 1.0 / math.sqrt(HEAD_DIM)
    key_block = jnp.concatenate([span_keys, cache_keys], 0)
    value_block = jnp.concatenate([span_values, cache_values], 0)
    piece_keys = lax.all_gather(key_block, "ctx", axis=0, tiled=True)
    piece_values = lax.all_gather(value_block, "ctx", axis=0, tiled=True)
    piece_rows = piece_keys.shape[0]
    index = jnp.arange(piece_rows, dtype=jnp.int32)
    owner = index // block_rows
    within = index % block_rows
    usable = (within < token_count) | (owner * cached_rows + within - token_count < length)
    scores = (
        jnp.einsum(
            "thd,phd->htp",
            queries.reshape(token_count, head_count, HEAD_DIM),
            piece_keys.reshape(piece_rows, head_count, HEAD_DIM),
            preferred_element_type=jnp.float32,
        )
        * scaling
    )
    scores = jnp.where(usable[None, None, :], scores, -1e30)
    peak = jnp.max(scores, axis=2, keepdims=True)
    weights = jnp.where(usable[None, None, :], jnp.exp(scores - peak), 0.0)
    total = jnp.sum(weights, axis=2)
    accum = jnp.einsum(
        "htp,phd->htd",
        weights.astype(jnp.bfloat16),
        piece_values.reshape(piece_rows, head_count, HEAD_DIM),
        preferred_element_type=jnp.float32,
    )
    return (
        (accum / total[:, :, None])
        .transpose(1, 0, 2)
        .reshape(token_count, column_count)
        .astype(jnp.bfloat16)
    )


def attend_by_head(queries, span_keys, span_values, cache_keys, cache_values, length, extra):
    token_count, column_count = queries.shape
    head_count = column_count // HEAD_DIM
    cached_rows = cache_keys.shape[0]
    ctx_count = lax.axis_size("ctx")
    local_heads = head_count // ctx_count
    width = local_heads * HEAD_DIM
    scaling = 1.0 / math.sqrt(HEAD_DIM)
    block_rows = token_count + cached_rows
    packed = jnp.concatenate(
        [queries, span_keys, cache_keys, span_values, cache_values], 0
    )
    base_rows = packed.shape[0]
    packed = jnp.concatenate([packed.reshape(base_rows, ctx_count, width), extra], 0)
    packed_rows = packed.shape[0]
    got = lax.all_to_all(packed, "ctx", split_axis=1, concat_axis=0, tiled=True)
    got = got.reshape(ctx_count, packed_rows, local_heads, HEAD_DIM)
    query_all = got[:, :token_count].reshape(ctx_count * token_count, local_heads, HEAD_DIM)
    key_all = got[:, token_count : token_count + block_rows].reshape(
        ctx_count * block_rows, local_heads, HEAD_DIM
    )
    extra_got = got[:, base_rows:]
    value_all = got[:, token_count + block_rows : base_rows].reshape(
        ctx_count * block_rows, local_heads, HEAD_DIM
    )
    piece_rows = ctx_count * block_rows
    index = jnp.arange(piece_rows, dtype=jnp.int32)
    owner = index // block_rows
    within = index % block_rows
    usable = (within < token_count) | (owner * cached_rows + within - token_count < length)
    scores = (
        jnp.einsum("thd,phd->htp", query_all, key_all, preferred_element_type=jnp.float32)
        * scaling
    )
    scores = jnp.where(usable[None, None, :], scores, -1e30)
    peak = jnp.max(scores, axis=2, keepdims=True)
    weights = jnp.where(usable[None, None, :], jnp.exp(scores - peak), 0.0)
    total = jnp.sum(weights, axis=2)
    accum = jnp.einsum(
        "htp,phd->thd",
        weights.astype(jnp.bfloat16),
        value_all,
        preferred_element_type=jnp.float32,
    )
    head_out = (accum / total.T[:, :, None]).astype(jnp.bfloat16)
    head_out = head_out.reshape(ctx_count, token_count, width)
    back = lax.all_to_all(head_out, "ctx", split_axis=0, concat_axis=0, tiled=True)
    return back.transpose(1, 0, 2).reshape(token_count, column_count), extra_got


def on_device(
    hidden_in,
    queries,
    span_keys,
    span_values,
    cache_keys,
    cache_values,
    cache_lengths,
    slot_request,
    out_weight,
    norm_gain,
    expert_ids,
    expert_gates,
    gate_proj,
    up_proj,
    down_proj,
):
    token_count, feature_width = hidden_in.shape
    column_count = queries.shape[1]
    head_count = column_count // HEAD_DIM
    ctx_count = lax.axis_size("ctx")
    slot_place = lax.axis_index("req")
    slot_count = slot_request.shape[0]
    slot_range = jnp.arange(slot_count, dtype=jnp.int32)
    request = jnp.sum(jnp.where(slot_range == slot_place, slot_request, 0))
    length = jnp.sum(jnp.where(slot_range == request, cache_lengths, 0))
    local_experts = gate_proj.shape[0]
    expert_total = local_experts * ctx_count
    gate_matrix = jnp.sum(
        jnp.where(
            expert_ids[:, :, None] == jnp.arange(expert_total, dtype=jnp.int32)[None, None, :],
            expert_gates[:, :, None],
            0.0,
        ),
        axis=1,
    )
    first_expert = lax.axis_index("ctx") * local_experts
    if head_count % ctx_count == 0:
        width = column_count // ctx_count
        high = lax.reduce_precision(gate_matrix, exponent_bits=8, mantissa_bits=7)
        rest = gate_matrix - high
        middle = lax.reduce_precision(rest, exponent_bits=8, mantissa_bits=7)
        low = rest - middle
        parts = jnp.stack([high, middle, low], -1).astype(jnp.bfloat16)
        parts = parts.reshape(token_count, ctx_count, local_experts * 3)
        parts = parts.transpose(1, 0, 2).reshape(ctx_count, -1)
        part_len = parts.shape[1]
        part_rows = -(-part_len // width)
        parts = jnp.pad(parts, ((0, 0), (0, part_rows * width - part_len)))
        parts = parts.reshape(ctx_count, part_rows, width).transpose(1, 0, 2)
        attended, parts_got = attend_by_head(
            queries, span_keys, span_values, cache_keys, cache_values, length, parts
        )
        parts_got = parts_got.reshape(ctx_count, part_rows * width)[:, :part_len]
        parts_got = parts_got.reshape(ctx_count * token_count, local_experts, 3).astype(
            jnp.float32
        )
        local_gates = (parts_got[:, :, 0] + parts_got[:, :, 1]) + parts_got[:, :, 2]
    else:
        attended = attend_gathered(
            queries, span_keys, span_values, cache_keys, cache_values, length
        )
        local_gates = lax.all_gather(
            lax.dynamic_slice_in_dim(gate_matrix, first_expert, local_experts, 1),
            "ctx",
            axis=0,
            tiled=True,
        )
    residual = hidden_in.astype(jnp.float32) + jnp.dot(
        attended, out_weight, preferred_element_type=jnp.float32
    )
    mean_square = jnp.mean(residual * residual, axis=1, keepdims=True)
    normed = (residual * lax.rsqrt(mean_square + 1e-06) * norm_gain).astype(jnp.bfloat16)

    def experts_on(rows, gates):
        moe = None
        for j in range(local_experts):
            gate_val = jnp.dot(rows, gate_proj[j], preferred_element_type=jnp.float32)
            up_val = jnp.dot(rows, up_proj[j], preferred_element_type=jnp.float32)
            activated = (jax.nn.silu(gate_val) * up_val).astype(jnp.bfloat16)
            produced = jnp.dot(
                activated, down_proj[j], preferred_element_type=jnp.float32
            ).astype(jnp.bfloat16)
            term = gates[:, j : j + 1] * produced.astype(jnp.float32)
            moe = term if moe is None else moe + term
        return moe

    if ctx_count & (ctx_count - 1) == 0 and ctx_count > 1 and token_count % 2 == 0:
        me = lax.axis_index("ctx")
        half_rows = token_count // 2
        gate_blocks = local_gates.reshape(ctx_count, token_count, local_experts)
        moe_halves = []
        for half, order in enumerate(xor_orders(ctx_count)):
            rows = normed[half * half_rows : (half + 1) * half_rows]
            held = gather_xor(rows, order, ctx_count)
            sources = jnp.array(relative_masks(order), jnp.int32) ^ me
            gates = jnp.take(
                gate_blocks[:, half * half_rows : (half + 1) * half_rows], sources, axis=0
            ).reshape(ctx_count * half_rows, local_experts)
            part = experts_on(held.reshape(ctx_count * half_rows, feature_width), gates)
            part = part.reshape(ctx_count, half_rows, feature_width)
            moe_halves.append(reduce_xor(part, order, ctx_count))
        moe_rows = jnp.concatenate(moe_halves, 0)
    else:
        normed_all = lax.all_gather(normed, "ctx", axis=0, tiled=True)
        moe = experts_on(normed_all, local_gates)
        moe_rows = lax.psum_scatter(
            moe.astype(jnp.bfloat16), "ctx", scatter_dimension=0, tiled=True
        ).astype(jnp.float32)
    final = (residual + moe_rows).astype(jnp.bfloat16)

    return route_to_request(final, slot_request)


def xor_orders(ctx_count):
    bits = ctx_count.bit_length() - 1
    first = list(range(bits - 1, -1, -1))
    second = list(first)
    if bits >= 3:
        second[0], second[1] = second[1], second[0]
    return [first, second]


def relative_masks(order):
    return [
        sum(((f >> step) & 1) << bit for step, bit in enumerate(order))
        for f in range(1 << len(order))
    ]


def swap(rows, mask, ctx_count):
    return lax.ppermute(rows, "ctx", [(c, c ^ mask) for c in range(ctx_count)])


def gather_xor(rows, order, ctx_count):
    held = rows[None]
    for bit in order:
        held = jnp.concatenate([held, swap(held, 1 << bit, ctx_count)], 0)
    return held


def reduce_xor(part, order, ctx_count):
    total = part
    for bit in reversed(order):
        half = total.shape[0] // 2
        sent = swap(total[half:].astype(jnp.bfloat16), 1 << bit, ctx_count)
        total = total[:half] + sent.astype(jnp.float32)
    return total[0]


def route_to_request(final, slot_request):
    slot_count = slot_request.shape[0]
    token_count = final.shape[0]
    slot_range = jnp.arange(slot_count, dtype=jnp.int32)
    if slot_count <= 4:
        orders = list(itertools.permutations(range(slot_count)))
        table = jnp.array(orders, jnp.int32)
        match = jnp.all(table == slot_request[None, :], axis=1)
        choice = jnp.sum(jnp.where(match, jnp.arange(len(orders), dtype=jnp.int32), 0))

        def mover(order):
            pairs = [(g, order[g]) for g in range(slot_count)]
            if all(a == b for a, b in pairs):
                return lambda rows: rows
            return lambda rows: lax.ppermute(rows, "req", pairs)

        return lax.switch(choice, [mover(order) for order in orders], final)
    slot_place = lax.axis_index("req")
    source_slot = jnp.sum(jnp.where(slot_request == slot_place, slot_range, 0))
    piece = lax.all_gather(final, "req", axis=0, tiled=True)
    piece_rows = piece.shape[0]
    offset = source_slot * token_count
    inside = (offset >= 0) & (offset + token_count <= piece_rows)
    portion = lax.dynamic_slice_in_dim(
        piece, jnp.clip(offset, 0, piece_rows - token_count), token_count, 0
    )
    return jnp.where(inside, portion, jnp.zeros_like(final))


def solution(mesh):
    return jax.shard_map(
        on_device,
        mesh=mesh,
        in_specs=(
            P(("req", "ctx"), None),
            P(("req", "ctx"), None),
            P(("req", "ctx"), None),
            P(("req", "ctx"), None),
            P(("req", "ctx"), None),
            P(("req", "ctx"), None),
            P(),
            P(),
            P(),
            P(),
            P(("req", "ctx"), None),
            P(("req", "ctx"), None),
            P("ctx", None, None),
            P("ctx", None, None),
            P("ctx", None, None),
        ),
        out_specs=P(("req", "ctx"), None),
        check_vma=False,
    )
```

```python
import itertools
import math

import jax
import jax.numpy as jnp
from jax import lax
from jax.sharding import PartitionSpec as P

HEAD_DIM = 128


def attend_gathered(queries, span_keys, span_values, cache_keys, cache_values, length):
    token_count, column_count = queries.shape
    head_count = column_count // HEAD_DIM
    cached_rows = cache_keys.shape[0]
    block_rows = token_count + cached_rows
    scaling = 1.0 / math.sqrt(HEAD_DIM)
    key_block = jnp.concatenate([span_keys, cache_keys], 0)
    value_block = jnp.concatenate([span_values, cache_values], 0)
    piece_keys = lax.all_gather(key_block, "ctx", axis=0, tiled=True)
    piece_values = lax.all_gather(value_block, "ctx", axis=0, tiled=True)
    piece_rows = piece_keys.shape[0]
    index = jnp.arange(piece_rows, dtype=jnp.int32)
    owner = index // block_rows
    within = index % block_rows
    usable = (within < token_count) | (owner * cached_rows + within - token_count < length)
    scores = (
        jnp.einsum(
            "thd,phd->htp",
            queries.reshape(token_count, head_count, HEAD_DIM),
            piece_keys.reshape(piece_rows, head_count, HEAD_DIM),
            preferred_element_type=jnp.float32,
        )
        * scaling
    )
    scores = jnp.where(usable[None, None, :], scores, -1e30)
    peak = jnp.max(scores, axis=2, keepdims=True)
    weights = jnp.where(usable[None, None, :], jnp.exp(scores - peak), 0.0)
    total = jnp.sum(weights, axis=2)
    accum = jnp.einsum(
        "htp,phd->htd",
        weights.astype(jnp.bfloat16),
        piece_values.reshape(piece_rows, head_count, HEAD_DIM),
        preferred_element_type=jnp.float32,
    )
    return (
        (accum / total[:, :, None])
        .transpose(1, 0, 2)
        .reshape(token_count, column_count)
        .astype(jnp.bfloat16)
    )


def attend_by_head(queries, span_keys, span_values, cache_keys, cache_values, length, extra):
    token_count, column_count = queries.shape
    head_count = column_count // HEAD_DIM
    cached_rows = cache_keys.shape[0]
    ctx_count = lax.axis_size("ctx")
    local_heads = head_count // ctx_count
    width = local_heads * HEAD_DIM
    scaling = 1.0 / math.sqrt(HEAD_DIM)
    block_rows = token_count + cached_rows
    packed = jnp.concatenate(
        [queries, span_keys, cache_keys, span_values, cache_values], 0
    )
    base_rows = packed.shape[0]
    packed = jnp.concatenate([packed.reshape(base_rows, ctx_count, width), extra], 0)
    packed_rows = packed.shape[0]
    got = lax.all_to_all(packed, "ctx", split_axis=1, concat_axis=0, tiled=True)
    got = got.reshape(ctx_count, packed_rows, local_heads, HEAD_DIM)
    query_all = got[:, :token_count].reshape(ctx_count * token_count, local_heads, HEAD_DIM)
    key_all = got[:, token_count : token_count + block_rows].reshape(
        ctx_count * block_rows, local_heads, HEAD_DIM
    )
    extra_got = got[:, base_rows:]
    value_all = got[:, token_count + block_rows : base_rows].reshape(
        ctx_count * block_rows, local_heads, HEAD_DIM
    )
    piece_rows = ctx_count * block_rows
    index = jnp.arange(piece_rows, dtype=jnp.int32)
    owner = index // block_rows
    within = index % block_rows
    usable = (within < token_count) | (owner * cached_rows + within - token_count < length)
    scores = (
        jnp.einsum("thd,phd->htp", query_all, key_all, preferred_element_type=jnp.float32)
        * scaling
    )
    scores = jnp.where(usable[None, None, :], scores, -1e30)
    peak = jnp.max(scores, axis=2, keepdims=True)
    weights = jnp.where(usable[None, None, :], jnp.exp(scores - peak), 0.0)
    total = jnp.sum(weights, axis=2)
    accum = jnp.einsum(
        "htp,phd->thd",
        weights.astype(jnp.bfloat16),
        value_all,
        preferred_element_type=jnp.float32,
    )
    head_out = (accum / total.T[:, :, None]).astype(jnp.bfloat16)
    head_out = head_out.reshape(ctx_count, token_count, width)
    back = lax.all_to_all(head_out, "ctx", split_axis=0, concat_axis=0, tiled=True)
    return back.transpose(1, 0, 2).reshape(token_count, column_count), extra_got


def on_device(
    hidden_in,
    queries,
    span_keys,
    span_values,
    cache_keys,
    cache_values,
    cache_lengths,
    slot_request,
    out_weight,
    norm_gain,
    expert_ids,
    expert_gates,
    gate_proj,
    up_proj,
    down_proj,
):
    token_count, feature_width = hidden_in.shape
    column_count = queries.shape[1]
    head_count = column_count // HEAD_DIM
    ctx_count = lax.axis_size("ctx")
    slot_place = lax.axis_index("req")
    slot_count = slot_request.shape[0]
    slot_range = jnp.arange(slot_count, dtype=jnp.int32)
    request = jnp.sum(jnp.where(slot_range == slot_place, slot_request, 0))
    length = jnp.sum(jnp.where(slot_range == request, cache_lengths, 0))
    local_experts = gate_proj.shape[0]
    expert_total = local_experts * ctx_count
    gate_matrix = jnp.sum(
        jnp.where(
            expert_ids[:, :, None] == jnp.arange(expert_total, dtype=jnp.int32)[None, None, :],
            expert_gates[:, :, None],
            0.0,
        ),
        axis=1,
    )
    first_expert = lax.axis_index("ctx") * local_experts
    if head_count % ctx_count == 0:
        width = column_count // ctx_count
        high = lax.reduce_precision(gate_matrix, exponent_bits=8, mantissa_bits=7)
        rest = gate_matrix - high
        middle = lax.reduce_precision(rest, exponent_bits=8, mantissa_bits=7)
        low = rest - middle
        parts = jnp.stack([high, middle, low], -1).astype(jnp.bfloat16)
        parts = parts.reshape(token_count, ctx_count, local_experts * 3)
        parts = parts.transpose(1, 0, 2).reshape(ctx_count, -1)
        part_len = parts.shape[1]
        part_rows = -(-part_len // width)
        parts = jnp.pad(parts, ((0, 0), (0, part_rows * width - part_len)))
        parts = parts.reshape(ctx_count, part_rows, width).transpose(1, 0, 2)
        attended, parts_got = attend_by_head(
            queries, span_keys, span_values, cache_keys, cache_values, length, parts
        )
        parts_got = parts_got.reshape(ctx_count, part_rows * width)[:, :part_len]
        parts_got = parts_got.reshape(ctx_count * token_count, local_experts, 3).astype(
            jnp.float32
        )
        local_gates = (parts_got[:, :, 0] + parts_got[:, :, 1]) + parts_got[:, :, 2]
    else:
        attended = attend_gathered(
            queries, span_keys, span_values, cache_keys, cache_values, length
        )
        local_gates = lax.all_gather(
            lax.dynamic_slice_in_dim(gate_matrix, first_expert, local_experts, 1),
            "ctx",
            axis=0,
            tiled=True,
        )
    residual = hidden_in.astype(jnp.float32) + jnp.dot(
        attended, out_weight, preferred_element_type=jnp.float32
    )
    mean_square = jnp.mean(residual * residual, axis=1, keepdims=True)
    normed = (residual * lax.rsqrt(mean_square + 1e-06) * norm_gain).astype(jnp.bfloat16)

    def experts_on(rows, gates):
        moe = None
        for j in range(local_experts):
            gate_val = jnp.dot(rows, gate_proj[j], preferred_element_type=jnp.float32)
            up_val = jnp.dot(rows, up_proj[j], preferred_element_type=jnp.float32)
            activated = (jax.nn.silu(gate_val) * up_val).astype(jnp.bfloat16)
            activated = lax.optimization_barrier(activated)
            produced = jnp.dot(
                activated, down_proj[j], preferred_element_type=jnp.float32
            ).astype(jnp.bfloat16)
            term = gates[:, j : j + 1] * produced.astype(jnp.float32)
            moe = term if moe is None else moe + term
        return moe

    if ctx_count & (ctx_count - 1) == 0 and ctx_count > 1 and token_count % 2 == 0:
        me = lax.axis_index("ctx")
        half_rows = token_count // 2
        gate_blocks = local_gates.reshape(ctx_count, token_count, local_experts)
        moe_halves = []
        for half, order in enumerate(xor_orders(ctx_count)):
            rows = normed[half * half_rows : (half + 1) * half_rows]
            held = gather_xor(rows, order, ctx_count)
            sources = jnp.array(relative_masks(order), jnp.int32) ^ me
            gates = jnp.take(
                gate_blocks[:, half * half_rows : (half + 1) * half_rows], sources, axis=0
            ).reshape(ctx_count * half_rows, local_experts)
            part = experts_on(held.reshape(ctx_count * half_rows, feature_width), gates)
            part = part.reshape(ctx_count, half_rows, feature_width)
            moe_halves.append(reduce_xor(part, order, ctx_count))
        moe_rows = jnp.concatenate(moe_halves, 0)
    else:
        normed_all = lax.all_gather(normed, "ctx", axis=0, tiled=True)
        moe = experts_on(normed_all, local_gates)
        moe_rows = lax.psum_scatter(
            moe.astype(jnp.bfloat16), "ctx", scatter_dimension=0, tiled=True
        ).astype(jnp.float32)
    final = (residual + moe_rows).astype(jnp.bfloat16)

    return route_to_request(final, slot_request)


def xor_orders(ctx_count):
    bits = ctx_count.bit_length() - 1
    first = list(range(bits - 1, -1, -1))
    second = list(first)
    if bits >= 3:
        second[0], second[1] = second[1], second[0]
    return [first, second]


def relative_masks(order):
    return [
        sum(((f >> step) & 1) << bit for step, bit in enumerate(order))
        for f in range(1 << len(order))
    ]


def swap(rows, mask, ctx_count):
    return lax.ppermute(rows, "ctx", [(c, c ^ mask) for c in range(ctx_count)])


def gather_xor(rows, order, ctx_count):
    held = rows[None]
    for bit in order:
        held = jnp.concatenate([held, swap(held, 1 << bit, ctx_count)], 0)
    return held


def reduce_xor(part, order, ctx_count):
    total = part
    for bit in reversed(order):
        half = total.shape[0] // 2
        sent = swap(total[half:].astype(jnp.bfloat16), 1 << bit, ctx_count)
        total = total[:half] + sent.astype(jnp.float32)
    return total[0]


def route_to_request(final, slot_request):
    slot_count = slot_request.shape[0]
    token_count = final.shape[0]
    slot_range = jnp.arange(slot_count, dtype=jnp.int32)
    if slot_count <= 4:
        orders = list(itertools.permutations(range(slot_count)))
        table = jnp.array(orders, jnp.int32)
        match = jnp.all(table == slot_request[None, :], axis=1)
        choice = jnp.sum(jnp.where(match, jnp.arange(len(orders), dtype=jnp.int32), 0))

        def mover(order):
            pairs = [(g, order[g]) for g in range(slot_count)]
            if all(a == b for a, b in pairs):
                return lambda rows: rows
            return lambda rows: lax.ppermute(rows, "req", pairs)

        return lax.switch(choice, [mover(order) for order in orders], final)
    slot_place = lax.axis_index("req")
    source_slot = jnp.sum(jnp.where(slot_request == slot_place, slot_range, 0))
    piece = lax.all_gather(final, "req", axis=0, tiled=True)
    piece_rows = piece.shape[0]
    offset = source_slot * token_count
    inside = (offset >= 0) & (offset + token_count <= piece_rows)
    portion = lax.dynamic_slice_in_dim(
        piece, jnp.clip(offset, 0, piece_rows - token_count), token_count, 0
    )
    return jnp.where(inside, portion, jnp.zeros_like(final))


def solution(mesh):
    return jax.shard_map(
        on_device,
        mesh=mesh,
        in_specs=(
            P(("req", "ctx"), None),
            P(("req", "ctx"), None),
            P(("req", "ctx"), None),
            P(("req", "ctx"), None),
            P(("req", "ctx"), None),
            P(("req", "ctx"), None),
            P(),
            P(),
            P(),
            P(),
            P(("req", "ctx"), None),
            P(("req", "ctx"), None),
            P("ctx", None, None),
            P("ctx", None, None),
            P("ctx", None, None),
        ),
        out_specs=P(("req", "ctx"), None),
        check_vma=False,
    )
```

```python
import itertools
import math

import jax
import jax.numpy as jnp
from jax import lax
from jax.sharding import PartitionSpec as P

HEAD_DIM = 128


def attend_gathered(queries, span_keys, span_values, cache_keys, cache_values, length):
    token_count, column_count = queries.shape
    head_count = column_count // HEAD_DIM
    cached_rows = cache_keys.shape[0]
    block_rows = token_count + cached_rows
    scaling = 1.0 / math.sqrt(HEAD_DIM)
    key_block = jnp.concatenate([span_keys, cache_keys], 0)
    value_block = jnp.concatenate([span_values, cache_values], 0)
    piece_keys = lax.all_gather(key_block, "ctx", axis=0, tiled=True)
    piece_values = lax.all_gather(value_block, "ctx", axis=0, tiled=True)
    piece_rows = piece_keys.shape[0]
    index = jnp.arange(piece_rows, dtype=jnp.int32)
    owner = index // block_rows
    within = index % block_rows
    usable = (within < token_count) | (owner * cached_rows + within - token_count < length)
    scores = (
        jnp.einsum(
            "thd,phd->htp",
            queries.reshape(token_count, head_count, HEAD_DIM),
            piece_keys.reshape(piece_rows, head_count, HEAD_DIM),
            preferred_element_type=jnp.float32,
        )
        * scaling
    )
    scores = jnp.where(usable[None, None, :], scores, -1e30)
    peak = jnp.max(scores, axis=2, keepdims=True)
    weights = jnp.where(usable[None, None, :], jnp.exp(scores - peak), 0.0)
    total = jnp.sum(weights, axis=2)
    accum = jnp.einsum(
        "htp,phd->htd",
        weights.astype(jnp.bfloat16),
        piece_values.reshape(piece_rows, head_count, HEAD_DIM),
        preferred_element_type=jnp.float32,
    )
    return (
        (accum / total[:, :, None])
        .transpose(1, 0, 2)
        .reshape(token_count, column_count)
        .astype(jnp.bfloat16)
    )


def attend_by_head(queries, span_keys, span_values, cache_keys, cache_values, length, extra):
    token_count, column_count = queries.shape
    head_count = column_count // HEAD_DIM
    cached_rows = cache_keys.shape[0]
    ctx_count = lax.axis_size("ctx")
    local_heads = head_count // ctx_count
    width = local_heads * HEAD_DIM
    scaling = 1.0 / math.sqrt(HEAD_DIM)
    block_rows = token_count + cached_rows
    packed = jnp.concatenate(
        [queries, span_keys, cache_keys, span_values, cache_values], 0
    )
    base_rows = packed.shape[0]
    packed = jnp.concatenate([packed.reshape(base_rows, ctx_count, width), extra], 0)
    packed_rows = packed.shape[0]
    got = lax.all_to_all(packed, "ctx", split_axis=1, concat_axis=0, tiled=True)
    got = got.reshape(ctx_count, packed_rows, local_heads, HEAD_DIM)
    query_all = got[:, :token_count].reshape(ctx_count * token_count, local_heads, HEAD_DIM)
    key_all = got[:, token_count : token_count + block_rows].reshape(
        ctx_count * block_rows, local_heads, HEAD_DIM
    )
    extra_got = got[:, base_rows:]
    value_all = got[:, token_count + block_rows : base_rows].reshape(
        ctx_count * block_rows, local_heads, HEAD_DIM
    )
    piece_rows = ctx_count * block_rows
    index = jnp.arange(piece_rows, dtype=jnp.int32)
    owner = index // block_rows
    within = index % block_rows
    usable = (within < token_count) | (owner * cached_rows + within - token_count < length)
    scores = (
        jnp.einsum("thd,phd->htp", query_all, key_all, preferred_element_type=jnp.float32)
        * scaling
    )
    scores = jnp.where(usable[None, None, :], scores, -1e30)
    peak = jnp.max(scores, axis=2, keepdims=True)
    weights = jnp.where(usable[None, None, :], jnp.exp(scores - peak), 0.0)
    total = jnp.sum(weights, axis=2)
    accum = jnp.einsum(
        "htp,phd->thd",
        weights.astype(jnp.bfloat16),
        value_all,
        preferred_element_type=jnp.float32,
    )
    head_out = (accum / total.T[:, :, None]).astype(jnp.bfloat16)
    head_out = head_out.reshape(ctx_count, token_count, width)
    back = lax.all_to_all(head_out, "ctx", split_axis=0, concat_axis=0, tiled=True)
    return back.transpose(1, 0, 2).reshape(token_count, column_count), extra_got


def on_device(
    hidden_in,
    queries,
    span_keys,
    span_values,
    cache_keys,
    cache_values,
    cache_lengths,
    slot_request,
    out_weight,
    norm_gain,
    expert_ids,
    expert_gates,
    gate_proj,
    up_proj,
    down_proj,
):
    token_count, feature_width = hidden_in.shape
    column_count = queries.shape[1]
    head_count = column_count // HEAD_DIM
    ctx_count = lax.axis_size("ctx")
    slot_place = lax.axis_index("req")
    slot_count = slot_request.shape[0]
    slot_range = jnp.arange(slot_count, dtype=jnp.int32)
    request = jnp.sum(jnp.where(slot_range == slot_place, slot_request, 0))
    length = jnp.sum(jnp.where(slot_range == request, cache_lengths, 0))
    local_experts = gate_proj.shape[0]
    expert_total = local_experts * ctx_count
    gate_matrix = jnp.sum(
        jnp.where(
            expert_ids[:, :, None] == jnp.arange(expert_total, dtype=jnp.int32)[None, None, :],
            expert_gates[:, :, None],
            0.0,
        ),
        axis=1,
    )
    first_expert = lax.axis_index("ctx") * local_experts
    if head_count % ctx_count == 0:
        width = column_count // ctx_count
        high = lax.reduce_precision(gate_matrix, exponent_bits=8, mantissa_bits=7)
        rest = gate_matrix - high
        middle = lax.reduce_precision(rest, exponent_bits=8, mantissa_bits=7)
        low = rest - middle
        parts = jnp.stack([high, middle, low], -1).astype(jnp.bfloat16)
        parts = parts.reshape(token_count, ctx_count, local_experts * 3)
        parts = parts.transpose(1, 0, 2).reshape(ctx_count, -1)
        part_len = parts.shape[1]
        part_rows = -(-part_len // width)
        parts = jnp.pad(parts, ((0, 0), (0, part_rows * width - part_len)))
        parts = parts.reshape(ctx_count, part_rows, width).transpose(1, 0, 2)
        attended, parts_got = attend_by_head(
            queries, span_keys, span_values, cache_keys, cache_values, length, parts
        )
        parts_got = parts_got.reshape(ctx_count, part_rows * width)[:, :part_len]
        parts_got = parts_got.reshape(ctx_count * token_count, local_experts, 3).astype(
            jnp.float32
        )
        local_gates = (parts_got[:, :, 0] + parts_got[:, :, 1]) + parts_got[:, :, 2]
    else:
        attended = attend_gathered(
            queries, span_keys, span_values, cache_keys, cache_values, length
        )
        local_gates = lax.all_gather(
            lax.dynamic_slice_in_dim(gate_matrix, first_expert, local_experts, 1),
            "ctx",
            axis=0,
            tiled=True,
        )
    residual = hidden_in.astype(jnp.float32) + jnp.dot(
        attended, out_weight, preferred_element_type=jnp.float32
    )
    mean_square = jnp.mean(residual * residual, axis=1, keepdims=True)
    normed = (residual * lax.rsqrt(mean_square + 1e-06) * norm_gain).astype(jnp.bfloat16)

    def experts_on(rows, gates):
        moe = None
        for j in range(local_experts):
            gate_val = jnp.dot(rows, gate_proj[j], preferred_element_type=jnp.float32)
            up_val = jnp.dot(rows, up_proj[j], preferred_element_type=jnp.float32)
            activated = (jax.nn.silu(gate_val) * up_val).astype(jnp.bfloat16)
            activated = lax.optimization_barrier(activated)
            produced = jnp.dot(
                activated, down_proj[j], preferred_element_type=jnp.float32
            ).astype(jnp.bfloat16)
            term = gates[:, j : j + 1] * produced.astype(jnp.float32)
            moe = term if moe is None else moe + term
        return moe

    if ctx_count & (ctx_count - 1) == 0 and ctx_count > 1 and token_count % 2 == 0:
        me = lax.axis_index("ctx")
        half_rows = token_count // 2
        gate_blocks = local_gates.reshape(ctx_count, token_count, local_experts)
        orders = xor_orders(ctx_count)
        helds = gather_xor(
            [normed[h * half_rows : (h + 1) * half_rows] for h in range(2)], orders, ctx_count
        )
        parts = []
        for half, order in enumerate(orders):
            sources = jnp.array(relative_masks(order), jnp.int32) ^ me
            gates = jnp.take(
                gate_blocks[:, half * half_rows : (half + 1) * half_rows], sources, axis=0
            ).reshape(ctx_count * half_rows, local_experts)
            part = experts_on(helds[half].reshape(ctx_count * half_rows, feature_width), gates)
            parts.append(part.reshape(ctx_count, half_rows, feature_width))
        moe_halves = reduce_xor(parts, orders, ctx_count)
        moe_rows = jnp.concatenate(moe_halves, 0)
    else:
        normed_all = lax.all_gather(normed, "ctx", axis=0, tiled=True)
        moe = experts_on(normed_all, local_gates)
        moe_rows = lax.psum_scatter(
            moe.astype(jnp.bfloat16), "ctx", scatter_dimension=0, tiled=True
        ).astype(jnp.float32)
    final = (residual + moe_rows).astype(jnp.bfloat16)

    return route_to_request(final, slot_request)


def xor_orders(ctx_count):
    bits = ctx_count.bit_length() - 1
    first = list(range(bits - 1, -1, -1))
    second = list(first)
    if bits >= 3:
        second[0], second[1] = second[1], second[0]
    return [first, second]


def relative_masks(order):
    return [
        sum(((f >> step) & 1) << bit for step, bit in enumerate(order))
        for f in range(1 << len(order))
    ]


def swap(rows, mask, ctx_count):
    return lax.ppermute(rows, "ctx", [(c, c ^ mask) for c in range(ctx_count)])


def gather_xor(rows_list, orders, ctx_count):
    helds = [rows[None] for rows in rows_list]
    for step in range(len(orders[0])):
        helds = [
            jnp.concatenate([held, swap(held, 1 << order[step], ctx_count)], 0)
            for held, order in zip(helds, orders)
        ]
        helds = list(lax.optimization_barrier(tuple(helds)))
    return helds


def reduce_xor(parts, orders, ctx_count):
    totals = parts
    for step in reversed(range(len(orders[0]))):
        half = totals[0].shape[0] // 2
        sents = [
            swap(total[half:].astype(jnp.bfloat16), 1 << order[step], ctx_count)
            for total, order in zip(totals, orders)
        ]
        totals = [total[:half] + sent.astype(jnp.float32) for total, sent in zip(totals, sents)]
        totals = list(lax.optimization_barrier(tuple(totals)))
    return [total[0] for total in totals]


def route_to_request(final, slot_request):
    slot_count = slot_request.shape[0]
    token_count = final.shape[0]
    slot_range = jnp.arange(slot_count, dtype=jnp.int32)
    if slot_count <= 4:
        orders = list(itertools.permutations(range(slot_count)))
        table = jnp.array(orders, jnp.int32)
        match = jnp.all(table == slot_request[None, :], axis=1)
        choice = jnp.sum(jnp.where(match, jnp.arange(len(orders), dtype=jnp.int32), 0))

        def mover(order):
            pairs = [(g, order[g]) for g in range(slot_count)]
            if all(a == b for a, b in pairs):
                return lambda rows: rows
            return lambda rows: lax.ppermute(rows, "req", pairs)

        return lax.switch(choice, [mover(order) for order in orders], final)
    slot_place = lax.axis_index("req")
    source_slot = jnp.sum(jnp.where(slot_request == slot_place, slot_range, 0))
    piece = lax.all_gather(final, "req", axis=0, tiled=True)
    piece_rows = piece.shape[0]
    offset = source_slot * token_count
    inside = (offset >= 0) & (offset + token_count <= piece_rows)
    portion = lax.dynamic_slice_in_dim(
        piece, jnp.clip(offset, 0, piece_rows - token_count), token_count, 0
    )
    return jnp.where(inside, portion, jnp.zeros_like(final))


def solution(mesh):
    return jax.shard_map(
        on_device,
        mesh=mesh,
        in_specs=(
            P(("req", "ctx"), None),
            P(("req", "ctx"), None),
            P(("req", "ctx"), None),
            P(("req", "ctx"), None),
            P(("req", "ctx"), None),
            P(("req", "ctx"), None),
            P(),
            P(),
            P(),
            P(),
            P(("req", "ctx"), None),
            P(("req", "ctx"), None),
            P("ctx", None, None),
            P("ctx", None, None),
            P("ctx", None, None),
        ),
        out_specs=P(("req", "ctx"), None),
        check_vma=False,
    )
```

```python
import itertools
import math

import jax
import jax.numpy as jnp
from jax import lax
from jax.sharding import PartitionSpec as P

HEAD_DIM = 128


def attend_gathered(queries, span_keys, span_values, cache_keys, cache_values, length):
    token_count, column_count = queries.shape
    head_count = column_count // HEAD_DIM
    cached_rows = cache_keys.shape[0]
    block_rows = token_count + cached_rows
    scaling = 1.0 / math.sqrt(HEAD_DIM)
    key_block = jnp.concatenate([span_keys, cache_keys], 0)
    value_block = jnp.concatenate([span_values, cache_values], 0)
    piece_keys = lax.all_gather(key_block, "ctx", axis=0, tiled=True)
    piece_values = lax.all_gather(value_block, "ctx", axis=0, tiled=True)
    piece_rows = piece_keys.shape[0]
    index = jnp.arange(piece_rows, dtype=jnp.int32)
    owner = index // block_rows
    within = index % block_rows
    usable = (within < token_count) | (owner * cached_rows + within - token_count < length)
    scores = (
        jnp.einsum(
            "thd,phd->htp",
            queries.reshape(token_count, head_count, HEAD_DIM),
            piece_keys.reshape(piece_rows, head_count, HEAD_DIM),
            preferred_element_type=jnp.float32,
        )
        * scaling
    )
    scores = jnp.where(usable[None, None, :], scores, -1e30)
    peak = jnp.max(scores, axis=2, keepdims=True)
    weights = jnp.where(usable[None, None, :], jnp.exp(scores - peak), 0.0)
    total = jnp.sum(weights, axis=2)
    accum = jnp.einsum(
        "htp,phd->htd",
        weights.astype(jnp.bfloat16),
        piece_values.reshape(piece_rows, head_count, HEAD_DIM),
        preferred_element_type=jnp.float32,
    )
    return (
        (accum / total[:, :, None])
        .transpose(1, 0, 2)
        .reshape(token_count, column_count)
        .astype(jnp.bfloat16)
    )


def attend_by_head(queries, span_keys, span_values, cache_keys, cache_values, length, extra):
    token_count, column_count = queries.shape
    head_count = column_count // HEAD_DIM
    cached_rows = cache_keys.shape[0]
    ctx_count = lax.axis_size("ctx")
    local_heads = head_count // ctx_count
    width = local_heads * HEAD_DIM
    scaling = 1.0 / math.sqrt(HEAD_DIM)
    block_rows = token_count + cached_rows
    packed = jnp.concatenate(
        [queries, span_keys, cache_keys, span_values, cache_values], 0
    )
    base_rows = packed.shape[0]
    packed = jnp.concatenate([packed.reshape(base_rows, ctx_count, width), extra], 0)
    packed_rows = packed.shape[0]
    got = lax.all_to_all(packed, "ctx", split_axis=1, concat_axis=0, tiled=True)
    got = got.reshape(ctx_count, packed_rows, local_heads, HEAD_DIM)
    query_all = got[:, :token_count].reshape(ctx_count * token_count, local_heads, HEAD_DIM)
    key_all = got[:, token_count : token_count + block_rows].reshape(
        ctx_count * block_rows, local_heads, HEAD_DIM
    )
    extra_got = got[:, base_rows:]
    value_all = got[:, token_count + block_rows : base_rows].reshape(
        ctx_count * block_rows, local_heads, HEAD_DIM
    )
    piece_rows = ctx_count * block_rows
    index = jnp.arange(piece_rows, dtype=jnp.int32)
    owner = index // block_rows
    within = index % block_rows
    usable = (within < token_count) | (owner * cached_rows + within - token_count < length)
    scores = (
        jnp.einsum("thd,phd->htp", query_all, key_all, preferred_element_type=jnp.float32)
        * scaling
    )
    scores = jnp.where(usable[None, None, :], scores, -1e30)
    peak = jnp.max(scores, axis=2, keepdims=True)
    weights = jnp.where(usable[None, None, :], jnp.exp(scores - peak), 0.0)
    total = jnp.sum(weights, axis=2)
    accum = jnp.einsum(
        "htp,phd->thd",
        weights.astype(jnp.bfloat16),
        value_all,
        preferred_element_type=jnp.float32,
    )
    head_out = (accum / total.T[:, :, None]).astype(jnp.bfloat16)
    head_out = head_out.reshape(ctx_count, token_count, width)
    back = lax.all_to_all(head_out, "ctx", split_axis=0, concat_axis=0, tiled=True)
    return back.transpose(1, 0, 2).reshape(token_count, column_count), extra_got


def on_device(
    hidden_in,
    queries,
    span_keys,
    span_values,
    cache_keys,
    cache_values,
    cache_lengths,
    slot_request,
    out_weight,
    norm_gain,
    expert_ids,
    expert_gates,
    gate_proj,
    up_proj,
    down_proj,
):
    token_count, feature_width = hidden_in.shape
    column_count = queries.shape[1]
    head_count = column_count // HEAD_DIM
    ctx_count = lax.axis_size("ctx")
    slot_place = lax.axis_index("req")
    slot_count = slot_request.shape[0]
    slot_range = jnp.arange(slot_count, dtype=jnp.int32)
    request = jnp.sum(jnp.where(slot_range == slot_place, slot_request, 0))
    length = jnp.sum(jnp.where(slot_range == request, cache_lengths, 0))
    local_experts = gate_proj.shape[0]
    expert_total = local_experts * ctx_count
    gate_matrix = jnp.sum(
        jnp.where(
            expert_ids[:, :, None] == jnp.arange(expert_total, dtype=jnp.int32)[None, None, :],
            expert_gates[:, :, None],
            0.0,
        ),
        axis=1,
    )
    first_expert = lax.axis_index("ctx") * local_experts
    if head_count % ctx_count == 0:
        width = column_count // ctx_count
        high = lax.reduce_precision(gate_matrix, exponent_bits=8, mantissa_bits=7)
        rest = gate_matrix - high
        middle = lax.reduce_precision(rest, exponent_bits=8, mantissa_bits=7)
        low = rest - middle
        parts = jnp.stack([high, middle, low], -1).astype(jnp.bfloat16)
        parts = parts.reshape(token_count, ctx_count, local_experts * 3)
        parts = parts.transpose(1, 0, 2).reshape(ctx_count, -1)
        part_len = parts.shape[1]
        part_rows = -(-part_len // width)
        parts = jnp.pad(parts, ((0, 0), (0, part_rows * width - part_len)))
        parts = parts.reshape(ctx_count, part_rows, width).transpose(1, 0, 2)
        attended, parts_got = attend_by_head(
            queries, span_keys, span_values, cache_keys, cache_values, length, parts
        )
        parts_got = parts_got.reshape(ctx_count, part_rows * width)[:, :part_len]
        parts_got = parts_got.reshape(ctx_count * token_count, local_experts, 3).astype(
            jnp.float32
        )
        local_gates = (parts_got[:, :, 0] + parts_got[:, :, 1]) + parts_got[:, :, 2]
    else:
        attended = attend_gathered(
            queries, span_keys, span_values, cache_keys, cache_values, length
        )
        local_gates = lax.all_gather(
            lax.dynamic_slice_in_dim(gate_matrix, first_expert, local_experts, 1),
            "ctx",
            axis=0,
            tiled=True,
        )
    residual = hidden_in.astype(jnp.float32) + jnp.dot(
        attended, out_weight, preferred_element_type=jnp.float32
    )
    mean_square = jnp.mean(residual * residual, axis=1, keepdims=True)
    normed = (residual * lax.rsqrt(mean_square + 1e-06) * norm_gain).astype(jnp.bfloat16)

    def experts_on(rows, gates):
        moe = None
        for j in range(local_experts):
            gate_val = jnp.dot(rows, gate_proj[j], preferred_element_type=jnp.float32)
            up_val = jnp.dot(rows, up_proj[j], preferred_element_type=jnp.float32)
            activated = (jax.nn.silu(gate_val) * up_val).astype(jnp.bfloat16)
            activated = lax.optimization_barrier(activated)
            produced = jnp.dot(
                activated, down_proj[j], preferred_element_type=jnp.float32
            ).astype(jnp.bfloat16)
            term = gates[:, j : j + 1] * produced.astype(jnp.float32)
            moe = term if moe is None else moe + term
        return moe

    if ctx_count & (ctx_count - 1) == 0 and ctx_count > 1 and token_count % 4 == 0:
        me = lax.axis_index("ctx")
        stream_rows = token_count // 4
        gate_blocks = local_gates.reshape(ctx_count, token_count, local_experts)
        orders = xor_orders(ctx_count)
        moe_pieces = []
        earlier = None
        for group in range(2):
            firsts = [(2 * group + s) * stream_rows for s in range(2)]
            inputs = [normed[f : f + stream_rows] for f in firsts]
            if earlier is not None:
                inputs, _ = lax.optimization_barrier((inputs, earlier))
            helds = gather_xor(inputs, orders, ctx_count)
            earlier = helds
            gates = []
            for first, order in zip(firsts, orders):
                sources = jnp.array(relative_masks(order), jnp.int32) ^ me
                gates.append(
                    jnp.take(
                        gate_blocks[:, first : first + stream_rows], sources, axis=0
                    ).reshape(ctx_count * stream_rows, local_experts)
                )
            rows = jnp.concatenate(
                [held.reshape(ctx_count * stream_rows, feature_width) for held in helds], 0
            )
            part = experts_on(rows, jnp.concatenate(gates, 0))
            part = part.reshape(2, ctx_count, stream_rows, feature_width)
            moe_pieces.extend(reduce_xor([part[0], part[1]], orders, ctx_count))
        moe_rows = jnp.concatenate(moe_pieces, 0)
    else:
        normed_all = lax.all_gather(normed, "ctx", axis=0, tiled=True)
        moe = experts_on(normed_all, local_gates)
        moe_rows = lax.psum_scatter(
            moe.astype(jnp.bfloat16), "ctx", scatter_dimension=0, tiled=True
        ).astype(jnp.float32)
    final = (residual + moe_rows).astype(jnp.bfloat16)

    return route_to_request(final, slot_request)


def xor_orders(ctx_count):
    bits = ctx_count.bit_length() - 1
    first = list(range(bits - 1, -1, -1))
    second = list(first)
    if bits >= 3:
        second[0], second[1] = second[1], second[0]
    return [first, second]


def relative_masks(order):
    return [
        sum(((f >> step) & 1) << bit for step, bit in enumerate(order))
        for f in range(1 << len(order))
    ]


def swap(rows, mask, ctx_count):
    return lax.ppermute(rows, "ctx", [(c, c ^ mask) for c in range(ctx_count)])


def gather_xor(rows_list, orders, ctx_count):
    helds = [rows[None] for rows in rows_list]
    for step in range(len(orders[0])):
        helds = [
            jnp.concatenate([held, swap(held, 1 << order[step], ctx_count)], 0)
            for held, order in zip(helds, orders)
        ]
        helds = list(lax.optimization_barrier(tuple(helds)))
    return helds


def reduce_xor(parts, orders, ctx_count):
    totals = parts
    for step in reversed(range(len(orders[0]))):
        half = totals[0].shape[0] // 2
        sents = [
            swap(total[half:].astype(jnp.bfloat16), 1 << order[step], ctx_count)
            for total, order in zip(totals, orders)
        ]
        totals = [total[:half] + sent.astype(jnp.float32) for total, sent in zip(totals, sents)]
        totals = list(lax.optimization_barrier(tuple(totals)))
    return [total[0] for total in totals]


def route_to_request(final, slot_request):
    slot_count = slot_request.shape[0]
    token_count = final.shape[0]
    slot_range = jnp.arange(slot_count, dtype=jnp.int32)
    if slot_count <= 4:
        orders = list(itertools.permutations(range(slot_count)))
        table = jnp.array(orders, jnp.int32)
        match = jnp.all(table == slot_request[None, :], axis=1)
        choice = jnp.sum(jnp.where(match, jnp.arange(len(orders), dtype=jnp.int32), 0))

        def mover(order):
            pairs = [(g, order[g]) for g in range(slot_count)]
            if all(a == b for a, b in pairs):
                return lambda rows: rows
            return lambda rows: lax.ppermute(rows, "req", pairs)

        return lax.switch(choice, [mover(order) for order in orders], final)
    slot_place = lax.axis_index("req")
    source_slot = jnp.sum(jnp.where(slot_request == slot_place, slot_range, 0))
    piece = lax.all_gather(final, "req", axis=0, tiled=True)
    piece_rows = piece.shape[0]
    offset = source_slot * token_count
    inside = (offset >= 0) & (offset + token_count <= piece_rows)
    portion = lax.dynamic_slice_in_dim(
        piece, jnp.clip(offset, 0, piece_rows - token_count), token_count, 0
    )
    return jnp.where(inside, portion, jnp.zeros_like(final))


def solution(mesh):
    return jax.shard_map(
        on_device,
        mesh=mesh,
        in_specs=(
            P(("req", "ctx"), None),
            P(("req", "ctx"), None),
            P(("req", "ctx"), None),
            P(("req", "ctx"), None),
            P(("req", "ctx"), None),
            P(("req", "ctx"), None),
            P(),
            P(),
            P(),
            P(),
            P(("req", "ctx"), None),
            P(("req", "ctx"), None),
            P("ctx", None, None),
            P("ctx", None, None),
            P("ctx", None, None),
        ),
        out_specs=P(("req", "ctx"), None),
        check_vma=False,
    )
```

```python
import itertools
import math

import jax
import jax.numpy as jnp
from jax import lax
from jax.sharding import PartitionSpec as P

HEAD_DIM = 128


def attend_gathered(queries, span_keys, span_values, cache_keys, cache_values, length):
    token_count, column_count = queries.shape
    head_count = column_count // HEAD_DIM
    cached_rows = cache_keys.shape[0]
    block_rows = token_count + cached_rows
    scaling = 1.0 / math.sqrt(HEAD_DIM)
    key_block = jnp.concatenate([span_keys, cache_keys], 0)
    value_block = jnp.concatenate([span_values, cache_values], 0)
    piece_keys = lax.all_gather(key_block, "ctx", axis=0, tiled=True)
    piece_values = lax.all_gather(value_block, "ctx", axis=0, tiled=True)
    piece_rows = piece_keys.shape[0]
    index = jnp.arange(piece_rows, dtype=jnp.int32)
    owner = index // block_rows
    within = index % block_rows
    usable = (within < token_count) | (owner * cached_rows + within - token_count < length)
    scores = (
        jnp.einsum(
            "thd,phd->htp",
            queries.reshape(token_count, head_count, HEAD_DIM),
            piece_keys.reshape(piece_rows, head_count, HEAD_DIM),
            preferred_element_type=jnp.float32,
        )
        * scaling
    )
    scores = jnp.where(usable[None, None, :], scores, -1e30)
    peak = jnp.max(scores, axis=2, keepdims=True)
    weights = jnp.where(usable[None, None, :], jnp.exp(scores - peak), 0.0)
    total = jnp.sum(weights, axis=2)
    accum = jnp.einsum(
        "htp,phd->htd",
        weights.astype(jnp.bfloat16),
        piece_values.reshape(piece_rows, head_count, HEAD_DIM),
        preferred_element_type=jnp.float32,
    )
    return (
        (accum / total[:, :, None])
        .transpose(1, 0, 2)
        .reshape(token_count, column_count)
        .astype(jnp.bfloat16)
    )


def attend_by_head(queries, span_keys, span_values, cache_keys, cache_values, length, extra):
    token_count, column_count = queries.shape
    head_count = column_count // HEAD_DIM
    cached_rows = cache_keys.shape[0]
    ctx_count = lax.axis_size("ctx")
    local_heads = head_count // ctx_count
    width = local_heads * HEAD_DIM
    scaling = 1.0 / math.sqrt(HEAD_DIM)
    block_rows = token_count + cached_rows
    sources = [queries, span_keys, cache_keys, span_values, cache_values]
    base_rows = sum(x.shape[0] for x in sources)
    packed = jnp.concatenate(
        [x.reshape(x.shape[0], ctx_count, width).transpose(1, 0, 2) for x in sources]
        + [extra],
        1,
    )
    packed_rows = packed.shape[1]
    got = lax.all_to_all(packed, "ctx", split_axis=0, concat_axis=0, tiled=True)
    got = got.reshape(ctx_count, packed_rows, local_heads, HEAD_DIM)
    query_all = got[:, :token_count].reshape(ctx_count * token_count, local_heads, HEAD_DIM)
    key_all = got[:, token_count : token_count + block_rows].reshape(
        ctx_count * block_rows, local_heads, HEAD_DIM
    )
    extra_got = got[:, base_rows:]
    value_all = got[:, token_count + block_rows : base_rows].reshape(
        ctx_count * block_rows, local_heads, HEAD_DIM
    )
    piece_rows = ctx_count * block_rows
    index = jnp.arange(piece_rows, dtype=jnp.int32)
    owner = index // block_rows
    within = index % block_rows
    usable = (within < token_count) | (owner * cached_rows + within - token_count < length)
    scores = (
        jnp.einsum("thd,phd->htp", query_all, key_all, preferred_element_type=jnp.float32)
        * scaling
    )
    scores = jnp.where(usable[None, None, :], scores, -1e30)
    peak = jnp.max(scores, axis=2, keepdims=True)
    weights = jnp.where(usable[None, None, :], jnp.exp(scores - peak), 0.0)
    total = jnp.sum(weights, axis=2)
    accum = jnp.einsum(
        "htp,phd->thd",
        weights.astype(jnp.bfloat16),
        value_all,
        preferred_element_type=jnp.float32,
    )
    head_out = (accum / total.T[:, :, None]).astype(jnp.bfloat16)
    head_out = head_out.reshape(ctx_count, token_count, width)
    back = lax.all_to_all(head_out, "ctx", split_axis=0, concat_axis=0, tiled=True)
    return back.transpose(1, 0, 2).reshape(token_count, column_count), extra_got


def on_device(
    hidden_in,
    queries,
    span_keys,
    span_values,
    cache_keys,
    cache_values,
    cache_lengths,
    slot_request,
    out_weight,
    norm_gain,
    expert_ids,
    expert_gates,
    gate_proj,
    up_proj,
    down_proj,
):
    token_count, feature_width = hidden_in.shape
    column_count = queries.shape[1]
    head_count = column_count // HEAD_DIM
    ctx_count = lax.axis_size("ctx")
    slot_place = lax.axis_index("req")
    slot_count = slot_request.shape[0]
    slot_range = jnp.arange(slot_count, dtype=jnp.int32)
    request = jnp.sum(jnp.where(slot_range == slot_place, slot_request, 0))
    length = jnp.sum(jnp.where(slot_range == request, cache_lengths, 0))
    local_experts = gate_proj.shape[0]
    expert_total = local_experts * ctx_count
    gate_matrix = jnp.sum(
        jnp.where(
            expert_ids[:, :, None] == jnp.arange(expert_total, dtype=jnp.int32)[None, None, :],
            expert_gates[:, :, None],
            0.0,
        ),
        axis=1,
    )
    first_expert = lax.axis_index("ctx") * local_experts
    if head_count % ctx_count == 0:
        width = column_count // ctx_count
        high = lax.reduce_precision(gate_matrix, exponent_bits=8, mantissa_bits=7)
        rest = gate_matrix - high
        middle = lax.reduce_precision(rest, exponent_bits=8, mantissa_bits=7)
        low = rest - middle
        parts = jnp.stack([high, middle, low], 0).astype(jnp.bfloat16)
        parts = parts.reshape(3, token_count, ctx_count, local_experts)
        parts = parts.transpose(2, 0, 3, 1).reshape(ctx_count, -1)
        part_len = parts.shape[1]
        part_rows = -(-part_len // width)
        parts = jnp.pad(parts, ((0, 0), (0, part_rows * width - part_len)))
        parts = parts.reshape(ctx_count, part_rows, width)
        attended, parts_got = attend_by_head(
            queries, span_keys, span_values, cache_keys, cache_values, length, parts
        )
        parts_got = parts_got.reshape(ctx_count, part_rows * width)[:, :part_len]
        parts_got = parts_got.reshape(ctx_count, 3, local_experts, token_count).astype(
            jnp.float32
        )
        local_gates = (
            (parts_got[:, 0] + parts_got[:, 1]) + parts_got[:, 2]
        ).transpose(1, 0, 2)
    else:
        attended = attend_gathered(
            queries, span_keys, span_values, cache_keys, cache_values, length
        )
        local_gates = lax.all_gather(
            lax.dynamic_slice_in_dim(gate_matrix, first_expert, local_experts, 1).T,
            "ctx",
            axis=1,
            tiled=True,
        ).reshape(local_experts, ctx_count, token_count)
    residual = hidden_in.astype(jnp.float32) + jnp.dot(
        attended, out_weight, preferred_element_type=jnp.float32
    )
    mean_square = jnp.mean(residual * residual, axis=1, keepdims=True)
    normed = (residual * lax.rsqrt(mean_square + 1e-06) * norm_gain).astype(jnp.bfloat16)

    def experts_on(rows, gates):
        moe = None
        for j in range(local_experts):
            gate_val = jnp.dot(rows, gate_proj[j], preferred_element_type=jnp.float32)
            up_val = jnp.dot(rows, up_proj[j], preferred_element_type=jnp.float32)
            activated = (jax.nn.silu(gate_val) * up_val).astype(jnp.bfloat16)
            activated = lax.optimization_barrier(activated)
            produced = jnp.dot(
                activated, down_proj[j], preferred_element_type=jnp.float32
            ).astype(jnp.bfloat16)
            term = gates[j][:, None] * produced.astype(jnp.float32)
            moe = term if moe is None else moe + term
        return moe

    if ctx_count & (ctx_count - 1) == 0 and ctx_count > 1 and token_count % 4 == 0:
        me = lax.axis_index("ctx")
        stream_rows = token_count // 4
        orders = xor_orders(ctx_count)
        moe_pieces = []
        earlier = None
        for group in range(2):
            firsts = [(2 * group + s) * stream_rows for s in range(2)]
            inputs = [normed[f : f + stream_rows] for f in firsts]
            if earlier is not None:
                inputs, _ = lax.optimization_barrier((inputs, earlier))
            helds = gather_xor(inputs, orders, ctx_count)
            earlier = helds
            gates = []
            for first, order in zip(firsts, orders):
                sources = jnp.array(relative_masks(order), jnp.int32) ^ me
                gates.append(
                    jnp.take(
                        local_gates[:, :, first : first + stream_rows], sources, axis=1
                    ).reshape(local_experts, ctx_count * stream_rows)
                )
            rows = jnp.concatenate(
                [held.reshape(ctx_count * stream_rows, feature_width) for held in helds], 0
            )
            part = experts_on(rows, jnp.concatenate(gates, 1))
            part = part.reshape(2, ctx_count, stream_rows, feature_width)
            moe_pieces.extend(reduce_xor([part[0], part[1]], orders, ctx_count))
        moe_rows = jnp.concatenate(moe_pieces, 0)
    else:
        normed_all = lax.all_gather(normed, "ctx", axis=0, tiled=True)
        moe = experts_on(normed_all, local_gates.reshape(local_experts, -1))
        moe_rows = lax.psum_scatter(
            moe.astype(jnp.bfloat16), "ctx", scatter_dimension=0, tiled=True
        ).astype(jnp.float32)
    final = (residual + moe_rows).astype(jnp.bfloat16)

    return route_to_request(final, slot_request)


def xor_orders(ctx_count):
    bits = ctx_count.bit_length() - 1
    first = list(range(bits - 1, -1, -1))
    second = list(first)
    if bits >= 3:
        second[0], second[1] = second[1], second[0]
    return [first, second]


def relative_masks(order):
    return [
        sum(((f >> step) & 1) << bit for step, bit in enumerate(order))
        for f in range(1 << len(order))
    ]


def swap(rows, mask, ctx_count):
    return lax.ppermute(rows, "ctx", [(c, c ^ mask) for c in range(ctx_count)])


def gather_xor(rows_list, orders, ctx_count):
    helds = [rows[None] for rows in rows_list]
    for step in range(len(orders[0])):
        helds = [
            jnp.concatenate([held, swap(held, 1 << order[step], ctx_count)], 0)
            for held, order in zip(helds, orders)
        ]
        helds = list(lax.optimization_barrier(tuple(helds)))
    return helds


def reduce_xor(parts, orders, ctx_count):
    totals = parts
    for step in reversed(range(len(orders[0]))):
        half = totals[0].shape[0] // 2
        sents = [
            swap(total[half:].astype(jnp.bfloat16), 1 << order[step], ctx_count)
            for total, order in zip(totals, orders)
        ]
        totals = [total[:half] + sent.astype(jnp.float32) for total, sent in zip(totals, sents)]
        totals = list(lax.optimization_barrier(tuple(totals)))
    return [total[0] for total in totals]


def route_to_request(final, slot_request):
    slot_count = slot_request.shape[0]
    token_count = final.shape[0]
    slot_range = jnp.arange(slot_count, dtype=jnp.int32)
    if slot_count <= 4:
        orders = list(itertools.permutations(range(slot_count)))
        table = jnp.array(orders, jnp.int32)
        match = jnp.all(table == slot_request[None, :], axis=1)
        choice = jnp.sum(jnp.where(match, jnp.arange(len(orders), dtype=jnp.int32), 0))

        def mover(order):
            pairs = [(g, order[g]) for g in range(slot_count)]
            if all(a == b for a, b in pairs):
                return lambda rows: rows
            return lambda rows: lax.ppermute(rows, "req", pairs)

        return lax.switch(choice, [mover(order) for order in orders], final)
    slot_place = lax.axis_index("req")
    source_slot = jnp.sum(jnp.where(slot_request == slot_place, slot_range, 0))
    piece = lax.all_gather(final, "req", axis=0, tiled=True)
    piece_rows = piece.shape[0]
    offset = source_slot * token_count
    inside = (offset >= 0) & (offset + token_count <= piece_rows)
    portion = lax.dynamic_slice_in_dim(
        piece, jnp.clip(offset, 0, piece_rows - token_count), token_count, 0
    )
    return jnp.where(inside, portion, jnp.zeros_like(final))


def solution(mesh):
    return jax.shard_map(
        on_device,
        mesh=mesh,
        in_specs=(
            P(("req", "ctx"), None),
            P(("req", "ctx"), None),
            P(("req", "ctx"), None),
            P(("req", "ctx"), None),
            P(("req", "ctx"), None),
            P(("req", "ctx"), None),
            P(),
            P(),
            P(),
            P(),
            P(("req", "ctx"), None),
            P(("req", "ctx"), None),
            P("ctx", None, None),
            P("ctx", None, None),
            P("ctx", None, None),
        ),
        out_specs=P(("req", "ctx"), None),
        check_vma=False,
    )
```

```python
import itertools
import math

import jax
import jax.numpy as jnp
from jax import lax
from jax.sharding import PartitionSpec as P

HEAD_DIM = 128


def attend_gathered(queries, span_keys, span_values, cache_keys, cache_values, length):
    token_count, column_count = queries.shape
    head_count = column_count // HEAD_DIM
    cached_rows = cache_keys.shape[0]
    block_rows = token_count + cached_rows
    scaling = 1.0 / math.sqrt(HEAD_DIM)
    key_block = jnp.concatenate([span_keys, cache_keys], 0)
    value_block = jnp.concatenate([span_values, cache_values], 0)
    piece_keys = lax.all_gather(key_block, "ctx", axis=0, tiled=True)
    piece_values = lax.all_gather(value_block, "ctx", axis=0, tiled=True)
    piece_rows = piece_keys.shape[0]
    index = jnp.arange(piece_rows, dtype=jnp.int32)
    owner = index // block_rows
    within = index % block_rows
    usable = (within < token_count) | (owner * cached_rows + within - token_count < length)
    scores = (
        jnp.einsum(
            "thd,phd->htp",
            queries.reshape(token_count, head_count, HEAD_DIM),
            piece_keys.reshape(piece_rows, head_count, HEAD_DIM),
            preferred_element_type=jnp.float32,
        )
        * scaling
    )
    scores = jnp.where(usable[None, None, :], scores, -1e30)
    peak = jnp.max(scores, axis=2, keepdims=True)
    weights = jnp.where(usable[None, None, :], jnp.exp(scores - peak), 0.0)
    total = jnp.sum(weights, axis=2)
    accum = jnp.einsum(
        "htp,phd->htd",
        weights.astype(jnp.bfloat16),
        piece_values.reshape(piece_rows, head_count, HEAD_DIM),
        preferred_element_type=jnp.float32,
    )
    return (
        (accum / total[:, :, None])
        .transpose(1, 0, 2)
        .reshape(token_count, column_count)
        .astype(jnp.bfloat16)
    )


def attend_by_head(queries, span_keys, span_values, cache_keys, cache_values, length, extra):
    token_count, column_count = queries.shape
    head_count = column_count // HEAD_DIM
    cached_rows = cache_keys.shape[0]
    ctx_count = lax.axis_size("ctx")
    local_heads = head_count // ctx_count
    width = local_heads * HEAD_DIM
    scaling = 1.0 / math.sqrt(HEAD_DIM)
    block_rows = token_count + cached_rows
    sources = [queries, span_keys, cache_keys, span_values, cache_values]
    base_rows = sum(x.shape[0] for x in sources)
    packed = jnp.concatenate(
        [x.reshape(x.shape[0], ctx_count, width).transpose(1, 0, 2) for x in sources]
        + [extra],
        1,
    )
    packed_rows = packed.shape[1]
    got = lax.all_to_all(packed, "ctx", split_axis=0, concat_axis=0, tiled=True)
    got = got.reshape(ctx_count, packed_rows, local_heads, HEAD_DIM)
    query_all = got[:, :token_count].reshape(ctx_count * token_count, local_heads, HEAD_DIM)
    key_all = got[:, token_count : token_count + block_rows].reshape(
        ctx_count * block_rows, local_heads, HEAD_DIM
    )
    extra_got = got[:, base_rows:]
    value_all = got[:, token_count + block_rows : base_rows].reshape(
        ctx_count * block_rows, local_heads, HEAD_DIM
    )
    piece_rows = ctx_count * block_rows
    index = jnp.arange(piece_rows, dtype=jnp.int32)
    owner = index // block_rows
    within = index % block_rows
    usable = (within < token_count) | (owner * cached_rows + within - token_count < length)
    scores = (
        jnp.einsum("thd,phd->htp", query_all, key_all, preferred_element_type=jnp.float32)
        * scaling
    )
    scores = jnp.where(usable[None, None, :], scores, -1e30)
    peak = jnp.max(scores, axis=2, keepdims=True)
    weights = jnp.where(usable[None, None, :], jnp.exp(scores - peak), 0.0)
    total = jnp.sum(weights, axis=2)
    accum = jnp.einsum(
        "htp,phd->thd",
        weights.astype(jnp.bfloat16),
        value_all,
        preferred_element_type=jnp.float32,
    )
    head_out = (accum / total.T[:, :, None]).astype(jnp.bfloat16)
    head_out = head_out.reshape(ctx_count, token_count, width)
    back = lax.all_to_all(head_out, "ctx", split_axis=0, concat_axis=0, tiled=True)
    return back.transpose(1, 0, 2).reshape(token_count, column_count), extra_got


def on_device(
    hidden_in,
    queries,
    span_keys,
    span_values,
    cache_keys,
    cache_values,
    cache_lengths,
    slot_request,
    out_weight,
    norm_gain,
    expert_ids,
    expert_gates,
    gate_proj,
    up_proj,
    down_proj,
):
    token_count, feature_width = hidden_in.shape
    column_count = queries.shape[1]
    head_count = column_count // HEAD_DIM
    ctx_count = lax.axis_size("ctx")
    slot_place = lax.axis_index("req")
    slot_count = slot_request.shape[0]
    slot_range = jnp.arange(slot_count, dtype=jnp.int32)
    request = jnp.sum(jnp.where(slot_range == slot_place, slot_request, 0))
    length = jnp.sum(jnp.where(slot_range == request, cache_lengths, 0))
    local_experts = gate_proj.shape[0]
    expert_total = local_experts * ctx_count
    gate_matrix = jnp.sum(
        jnp.where(
            expert_ids[:, :, None] == jnp.arange(expert_total, dtype=jnp.int32)[None, None, :],
            expert_gates[:, :, None],
            0.0,
        ),
        axis=1,
    )
    first_expert = lax.axis_index("ctx") * local_experts
    if head_count % ctx_count == 0:
        width = column_count // ctx_count
        high = lax.reduce_precision(gate_matrix, exponent_bits=8, mantissa_bits=7)
        rest = gate_matrix - high
        middle = lax.reduce_precision(rest, exponent_bits=8, mantissa_bits=7)
        low = rest - middle
        parts = jnp.stack([high, middle, low], 0).astype(jnp.bfloat16)
        parts = parts.reshape(3, token_count, ctx_count, local_experts)
        parts = parts.transpose(2, 0, 3, 1).reshape(ctx_count, -1)
        part_len = parts.shape[1]
        part_rows = -(-part_len // width)
        parts = jnp.pad(parts, ((0, 0), (0, part_rows * width - part_len)))
        parts = parts.reshape(ctx_count, part_rows, width)
        attended, parts_got = attend_by_head(
            queries, span_keys, span_values, cache_keys, cache_values, length, parts
        )
        parts_got = parts_got.reshape(ctx_count, part_rows * width)[:, :part_len]
        parts_got = parts_got.reshape(ctx_count, 3, local_experts, token_count).astype(
            jnp.float32
        )
        local_gates = (
            (parts_got[:, 0] + parts_got[:, 1]) + parts_got[:, 2]
        ).transpose(1, 0, 2)
    else:
        attended = attend_gathered(
            queries, span_keys, span_values, cache_keys, cache_values, length
        )
        local_gates = lax.all_gather(
            lax.dynamic_slice_in_dim(gate_matrix, first_expert, local_experts, 1).T,
            "ctx",
            axis=1,
            tiled=True,
        ).reshape(local_experts, ctx_count, token_count)
    residual = hidden_in.astype(jnp.float32) + jnp.dot(
        attended, out_weight, preferred_element_type=jnp.float32
    )
    mean_square = jnp.mean(residual * residual, axis=1, keepdims=True)
    normed = (residual * lax.rsqrt(mean_square + 1e-06) * norm_gain).astype(jnp.bfloat16)

    def experts_on(rows, gates):
        moe = None
        for j in range(local_experts):
            gate_val = jnp.dot(rows, gate_proj[j], preferred_element_type=jnp.float32)
            up_val = jnp.dot(rows, up_proj[j], preferred_element_type=jnp.float32)
            activated = (jax.nn.silu(gate_val) * up_val).astype(jnp.bfloat16)
            activated = lax.optimization_barrier(activated)
            produced = jnp.dot(
                activated, down_proj[j], preferred_element_type=jnp.float32
            ).astype(jnp.bfloat16)
            term = gates[j][:, None] * produced.astype(jnp.float32)
            moe = term if moe is None else moe + term
        return moe

    if ctx_count & (ctx_count - 1) == 0 and ctx_count > 1 and token_count % 4 == 0:
        me = lax.axis_index("ctx")
        stream_rows = token_count // 4
        orders = xor_orders(ctx_count)
        moe_pieces = []
        earlier = None
        for group in range(2):
            firsts = [(2 * group + s) * stream_rows for s in range(2)]
            inputs = [normed[f : f + stream_rows] for f in firsts]
            if earlier is not None:
                inputs, _ = lax.optimization_barrier((inputs, earlier))
            helds = gather_xor(inputs, orders, ctx_count)
            earlier = helds
            gates = []
            for first, order in zip(firsts, orders):
                sources = jnp.array(relative_masks(order), jnp.int32) ^ me
                gates.append(
                    jnp.take(
                        local_gates[:, :, first : first + stream_rows], sources, axis=1
                    ).reshape(local_experts, ctx_count * stream_rows)
                )
            rows = jnp.concatenate(
                [held.reshape(ctx_count * stream_rows, feature_width) for held in helds], 0
            )
            part = experts_on(rows, jnp.concatenate(gates, 1))
            part = part.reshape(2, ctx_count, stream_rows, feature_width)
            moe_group = jnp.concatenate(reduce_xor([part[0], part[1]], orders, ctx_count), 0)
            final_group = (
                residual[firsts[0] : firsts[0] + 2 * stream_rows] + moe_group
            ).astype(jnp.bfloat16)
            moe_pieces.append(route_to_request(final_group, slot_request))
        return jnp.concatenate(moe_pieces, 0)
    else:
        normed_all = lax.all_gather(normed, "ctx", axis=0, tiled=True)
        moe = experts_on(normed_all, local_gates.reshape(local_experts, -1))
        moe_rows = lax.psum_scatter(
            moe.astype(jnp.bfloat16), "ctx", scatter_dimension=0, tiled=True
        ).astype(jnp.float32)
    final = (residual + moe_rows).astype(jnp.bfloat16)

    return route_to_request(final, slot_request)


def xor_orders(ctx_count):
    bits = ctx_count.bit_length() - 1
    first = list(range(bits - 1, -1, -1))
    second = list(first)
    if bits >= 3:
        second[0], second[1] = second[1], second[0]
    return [first, second]


def relative_masks(order):
    return [
        sum(((f >> step) & 1) << bit for step, bit in enumerate(order))
        for f in range(1 << len(order))
    ]


def swap(rows, mask, ctx_count):
    return lax.ppermute(rows, "ctx", [(c, c ^ mask) for c in range(ctx_count)])


def gather_xor(rows_list, orders, ctx_count):
    helds = [rows[None] for rows in rows_list]
    for step in range(len(orders[0])):
        masks = [1 << order[step] for order in orders]
        if all(mask == masks[0] for mask in masks):
            got = swap(jnp.stack(helds), masks[0], ctx_count)
            gots = [got[i] for i in range(len(helds))]
        else:
            gots = [swap(held, mask, ctx_count) for held, mask in zip(helds, masks)]
        helds = [jnp.concatenate([held, got], 0) for held, got in zip(helds, gots)]
        helds = list(lax.optimization_barrier(tuple(helds)))
    return helds


def reduce_xor(parts, orders, ctx_count):
    totals = parts
    for step in reversed(range(len(orders[0]))):
        half = totals[0].shape[0] // 2
        masks = [1 << order[step] for order in orders]
        outgoing = [total[half:].astype(jnp.bfloat16) for total in totals]
        if all(mask == masks[0] for mask in masks):
            sent = swap(jnp.stack(outgoing), masks[0], ctx_count)
            sents = [sent[i] for i in range(len(outgoing))]
        else:
            sents = [swap(out, mask, ctx_count) for out, mask in zip(outgoing, masks)]
        totals = [total[:half] + sent.astype(jnp.float32) for total, sent in zip(totals, sents)]
        totals = list(lax.optimization_barrier(tuple(totals)))
    return [total[0] for total in totals]


def route_to_request(final, slot_request):
    slot_count = slot_request.shape[0]
    token_count = final.shape[0]
    slot_range = jnp.arange(slot_count, dtype=jnp.int32)
    if slot_count <= 4:
        orders = list(itertools.permutations(range(slot_count)))
        table = jnp.array(orders, jnp.int32)
        match = jnp.all(table == slot_request[None, :], axis=1)
        choice = jnp.sum(jnp.where(match, jnp.arange(len(orders), dtype=jnp.int32), 0))

        def mover(order):
            pairs = [(g, order[g]) for g in range(slot_count)]
            if all(a == b for a, b in pairs):
                return lambda rows: rows
            return lambda rows: lax.ppermute(rows, "req", pairs)

        return lax.switch(choice, [mover(order) for order in orders], final)
    slot_place = lax.axis_index("req")
    source_slot = jnp.sum(jnp.where(slot_request == slot_place, slot_range, 0))
    piece = lax.all_gather(final, "req", axis=0, tiled=True)
    piece_rows = piece.shape[0]
    offset = source_slot * token_count
    inside = (offset >= 0) & (offset + token_count <= piece_rows)
    portion = lax.dynamic_slice_in_dim(
        piece, jnp.clip(offset, 0, piece_rows - token_count), token_count, 0
    )
    return jnp.where(inside, portion, jnp.zeros_like(final))


def solution(mesh):
    return jax.shard_map(
        on_device,
        mesh=mesh,
        in_specs=(
            P(("req", "ctx"), None),
            P(("req", "ctx"), None),
            P(("req", "ctx"), None),
            P(("req", "ctx"), None),
            P(("req", "ctx"), None),
            P(("req", "ctx"), None),
            P(),
            P(),
            P(),
            P(),
            P(("req", "ctx"), None),
            P(("req", "ctx"), None),
            P("ctx", None, None),
            P("ctx", None, None),
            P("ctx", None, None),
        ),
        out_specs=P(("req", "ctx"), None),
        check_vma=False,
    )
```

```python
import itertools
import math

import jax
import jax.numpy as jnp
from jax import lax
from jax.sharding import PartitionSpec as P

HEAD_DIM = 128


def attend_gathered(queries, span_keys, span_values, cache_keys, cache_values, length):
    token_count, column_count = queries.shape
    head_count = column_count // HEAD_DIM
    cached_rows = cache_keys.shape[0]
    block_rows = token_count + cached_rows
    scaling = 1.0 / math.sqrt(HEAD_DIM)
    key_block = jnp.concatenate([span_keys, cache_keys], 0)
    value_block = jnp.concatenate([span_values, cache_values], 0)
    piece_keys = lax.all_gather(key_block, "ctx", axis=0, tiled=True)
    piece_values = lax.all_gather(value_block, "ctx", axis=0, tiled=True)
    piece_rows = piece_keys.shape[0]
    index = jnp.arange(piece_rows, dtype=jnp.int32)
    owner = index // block_rows
    within = index % block_rows
    usable = (within < token_count) | (owner * cached_rows + within - token_count < length)
    scores = (
        jnp.einsum(
            "thd,phd->htp",
            queries.reshape(token_count, head_count, HEAD_DIM),
            piece_keys.reshape(piece_rows, head_count, HEAD_DIM),
            preferred_element_type=jnp.float32,
        )
        * scaling
    )
    scores = jnp.where(usable[None, None, :], scores, -1e30)
    peak = jnp.max(scores, axis=2, keepdims=True)
    weights = jnp.where(usable[None, None, :], jnp.exp(scores - peak), 0.0)
    total = jnp.sum(weights, axis=2)
    accum = jnp.einsum(
        "htp,phd->htd",
        weights.astype(jnp.bfloat16),
        piece_values.reshape(piece_rows, head_count, HEAD_DIM),
        preferred_element_type=jnp.float32,
    )
    return (
        (accum / total[:, :, None])
        .transpose(1, 0, 2)
        .reshape(token_count, column_count)
        .astype(jnp.bfloat16)
    )


def attend_by_head(queries, span_keys, span_values, cache_keys, cache_values, length, extra):
    token_count, column_count = queries.shape
    head_count = column_count // HEAD_DIM
    cached_rows = cache_keys.shape[0]
    ctx_count = lax.axis_size("ctx")
    local_heads = head_count // ctx_count
    width = local_heads * HEAD_DIM
    scaling = 1.0 / math.sqrt(HEAD_DIM)
    block_rows = token_count + cached_rows
    sources = [queries, span_keys, cache_keys, span_values, cache_values]
    base_rows = sum(x.shape[0] for x in sources)
    packed = jnp.concatenate(
        [x.reshape(x.shape[0], ctx_count, width).transpose(1, 0, 2) for x in sources]
        + [extra],
        1,
    )
    packed_rows = packed.shape[1]
    got = lax.all_to_all(packed, "ctx", split_axis=0, concat_axis=0, tiled=True)
    got = got.reshape(ctx_count, packed_rows, local_heads, HEAD_DIM)
    query_all = got[:, :token_count].reshape(ctx_count * token_count, local_heads, HEAD_DIM)
    key_all = got[:, token_count : token_count + block_rows].reshape(
        ctx_count * block_rows, local_heads, HEAD_DIM
    )
    extra_got = got[:, base_rows:]
    value_all = got[:, token_count + block_rows : base_rows].reshape(
        ctx_count * block_rows, local_heads, HEAD_DIM
    )
    piece_rows = ctx_count * block_rows
    index = jnp.arange(piece_rows, dtype=jnp.int32)
    owner = index // block_rows
    within = index % block_rows
    usable = (within < token_count) | (owner * cached_rows + within - token_count < length)
    scores = (
        jnp.einsum("thd,phd->htp", query_all, key_all, preferred_element_type=jnp.float32)
        * scaling
    )
    scores = jnp.where(usable[None, None, :], scores, -1e30)
    peak = jnp.max(scores, axis=2, keepdims=True)
    weights = jnp.where(usable[None, None, :], jnp.exp(scores - peak), 0.0)
    total = jnp.sum(weights, axis=2)
    accum = jnp.einsum(
        "htp,phd->thd",
        weights.astype(jnp.bfloat16),
        value_all,
        preferred_element_type=jnp.float32,
    )
    head_out = (accum / total.T[:, :, None]).astype(jnp.bfloat16)
    head_out = head_out.reshape(ctx_count, token_count, width)
    back = lax.all_to_all(head_out, "ctx", split_axis=0, concat_axis=0, tiled=True)
    return back.transpose(1, 0, 2).reshape(token_count, column_count), extra_got


def on_device(
    hidden_in,
    queries,
    span_keys,
    span_values,
    cache_keys,
    cache_values,
    cache_lengths,
    slot_request,
    out_weight,
    norm_gain,
    expert_ids,
    expert_gates,
    gate_proj,
    up_proj,
    down_proj,
):
    token_count, feature_width = hidden_in.shape
    column_count = queries.shape[1]
    head_count = column_count // HEAD_DIM
    ctx_count = lax.axis_size("ctx")
    slot_place = lax.axis_index("req")
    slot_count = slot_request.shape[0]
    slot_range = jnp.arange(slot_count, dtype=jnp.int32)
    request = jnp.sum(jnp.where(slot_range == slot_place, slot_request, 0))
    length = jnp.sum(jnp.where(slot_range == request, cache_lengths, 0))
    local_experts = gate_proj.shape[0]
    expert_total = local_experts * ctx_count
    gate_matrix = jnp.sum(
        jnp.where(
            expert_ids[:, :, None] == jnp.arange(expert_total, dtype=jnp.int32)[None, None, :],
            expert_gates[:, :, None],
            0.0,
        ),
        axis=1,
    )
    first_expert = lax.axis_index("ctx") * local_experts
    if head_count % ctx_count == 0:
        width = column_count // ctx_count
        high = lax.reduce_precision(gate_matrix, exponent_bits=8, mantissa_bits=7)
        rest = gate_matrix - high
        middle = lax.reduce_precision(rest, exponent_bits=8, mantissa_bits=7)
        low = rest - middle
        parts = jnp.stack([high, middle, low], 0).astype(jnp.bfloat16)
        parts = parts.reshape(3, token_count, ctx_count, local_experts)
        parts = parts.transpose(2, 0, 3, 1).reshape(ctx_count, -1)
        part_len = parts.shape[1]
        part_rows = -(-part_len // width)
        parts = jnp.pad(parts, ((0, 0), (0, part_rows * width - part_len)))
        parts = parts.reshape(ctx_count, part_rows, width)
        attended, parts_got = attend_by_head(
            queries, span_keys, span_values, cache_keys, cache_values, length, parts
        )
        parts_got = parts_got.reshape(ctx_count, part_rows * width)[:, :part_len]
        parts_got = parts_got.reshape(ctx_count, 3, local_experts, token_count).astype(
            jnp.float32
        )
        local_gates = (
            (parts_got[:, 0] + parts_got[:, 1]) + parts_got[:, 2]
        ).transpose(1, 0, 2)
    else:
        attended = attend_gathered(
            queries, span_keys, span_values, cache_keys, cache_values, length
        )
        local_gates = lax.all_gather(
            lax.dynamic_slice_in_dim(gate_matrix, first_expert, local_experts, 1).T,
            "ctx",
            axis=1,
            tiled=True,
        ).reshape(local_experts, ctx_count, token_count)
    residual = hidden_in.astype(jnp.float32) + jnp.dot(
        attended, out_weight, preferred_element_type=jnp.float32
    )
    mean_square = jnp.mean(residual * residual, axis=1, keepdims=True)
    normed = (residual * lax.rsqrt(mean_square + 1e-06) * norm_gain).astype(jnp.bfloat16)

    def experts_on(rows, gates):
        moe = None
        for j in range(local_experts):
            gate_val = jnp.dot(rows, gate_proj[j], preferred_element_type=jnp.float32)
            up_val = jnp.dot(rows, up_proj[j], preferred_element_type=jnp.float32)
            activated = (jax.nn.silu(gate_val) * up_val).astype(jnp.bfloat16)
            activated = lax.optimization_barrier(activated)
            produced = jnp.dot(
                activated, down_proj[j], preferred_element_type=jnp.float32
            ).astype(jnp.bfloat16)
            term = gates[j][:, None] * produced.astype(jnp.float32)
            moe = term if moe is None else moe + term
        return moe

    if ctx_count & (ctx_count - 1) == 0 and ctx_count > 1 and token_count % 4 == 0:
        me = lax.axis_index("ctx")
        stream_rows = token_count // 4
        orders = xor_orders(ctx_count)
        moe_pieces = []
        earlier = None
        for group in range(2):
            firsts = [(2 * group + s) * stream_rows for s in range(2)]
            inputs = [normed[f : f + stream_rows] for f in firsts]
            if earlier is not None:
                inputs, _ = lax.optimization_barrier((inputs, earlier))
            helds = gather_xor(inputs, orders, ctx_count)
            earlier = helds
            gates = []
            for first, order in zip(firsts, orders):
                sources = jnp.array(relative_masks(order), jnp.int32) ^ me
                gates.append(
                    jnp.take(
                        local_gates[:, :, first : first + stream_rows], sources, axis=1
                    ).reshape(local_experts, ctx_count * stream_rows)
                )
            rows = jnp.concatenate(
                [held.reshape(ctx_count * stream_rows, feature_width) for held in helds], 0
            )
            part = experts_on(rows, jnp.concatenate(gates, 1))
            part = part.reshape(2, ctx_count, stream_rows, feature_width)
            moe_pieces.extend(reduce_xor([part[0], part[1]], orders, ctx_count))
        moe_rows = jnp.concatenate(moe_pieces, 0)
    else:
        normed_all = lax.all_gather(normed, "ctx", axis=0, tiled=True)
        moe = experts_on(normed_all, local_gates.reshape(local_experts, -1))
        moe_rows = lax.psum_scatter(
            moe.astype(jnp.bfloat16), "ctx", scatter_dimension=0, tiled=True
        ).astype(jnp.float32)
    final = (residual + moe_rows).astype(jnp.bfloat16)

    return route_to_request(final, slot_request)


def xor_orders(ctx_count):
    bits = ctx_count.bit_length() - 1
    first = list(range(bits - 1, -1, -1))
    second = list(first)
    if bits >= 3:
        second[0], second[1] = second[1], second[0]
    return [first, second]


def relative_masks(order):
    return [
        sum(((f >> step) & 1) << bit for step, bit in enumerate(order))
        for f in range(1 << len(order))
    ]


def swap(rows, mask, ctx_count):
    return lax.ppermute(rows, "ctx", [(c, c ^ mask) for c in range(ctx_count)])


def gather_xor(rows_list, orders, ctx_count):
    helds = [rows[None] for rows in rows_list]
    for step in range(len(orders[0])):
        masks = [1 << order[step] for order in orders]
        if all(mask == masks[0] for mask in masks):
            got = swap(jnp.stack(helds), masks[0], ctx_count)
            gots = [got[i] for i in range(len(helds))]
        else:
            gots = [swap(held, mask, ctx_count) for held, mask in zip(helds, masks)]
        helds = [jnp.concatenate([held, got], 0) for held, got in zip(helds, gots)]
        helds = list(lax.optimization_barrier(tuple(helds)))
    return helds


def reduce_xor(parts, orders, ctx_count):
    totals = parts
    for step in reversed(range(len(orders[0]))):
        half = totals[0].shape[0] // 2
        masks = [1 << order[step] for order in orders]
        outgoing = [total[half:].astype(jnp.bfloat16) for total in totals]
        if all(mask == masks[0] for mask in masks):
            sent = swap(jnp.stack(outgoing), masks[0], ctx_count)
            sents = [sent[i] for i in range(len(outgoing))]
        else:
            sents = [swap(out, mask, ctx_count) for out, mask in zip(outgoing, masks)]
        totals = [total[:half] + sent.astype(jnp.float32) for total, sent in zip(totals, sents)]
        totals = list(lax.optimization_barrier(tuple(totals)))
    return [total[0] for total in totals]


def route_to_request(final, slot_request):
    slot_count = slot_request.shape[0]
    token_count = final.shape[0]
    slot_range = jnp.arange(slot_count, dtype=jnp.int32)
    if slot_count <= 4:
        orders = list(itertools.permutations(range(slot_count)))
        table = jnp.array(orders, jnp.int32)
        match = jnp.all(table == slot_request[None, :], axis=1)
        choice = jnp.sum(jnp.where(match, jnp.arange(len(orders), dtype=jnp.int32), 0))

        def mover(order):
            pairs = [(g, order[g]) for g in range(slot_count)]
            if all(a == b for a, b in pairs):
                return lambda rows: rows
            return lambda rows: lax.ppermute(rows, "req", pairs)

        return lax.switch(choice, [mover(order) for order in orders], final)
    slot_place = lax.axis_index("req")
    source_slot = jnp.sum(jnp.where(slot_request == slot_place, slot_range, 0))
    piece = lax.all_gather(final, "req", axis=0, tiled=True)
    piece_rows = piece.shape[0]
    offset = source_slot * token_count
    inside = (offset >= 0) & (offset + token_count <= piece_rows)
    portion = lax.dynamic_slice_in_dim(
        piece, jnp.clip(offset, 0, piece_rows - token_count), token_count, 0
    )
    return jnp.where(inside, portion, jnp.zeros_like(final))


def solution(mesh):
    return jax.shard_map(
        on_device,
        mesh=mesh,
        in_specs=(
            P(("req", "ctx"), None),
            P(("req", "ctx"), None),
            P(("req", "ctx"), None),
            P(("req", "ctx"), None),
            P(("req", "ctx"), None),
            P(("req", "ctx"), None),
            P(),
            P(),
            P(),
            P(),
            P(("req", "ctx"), None),
            P(("req", "ctx"), None),
            P("ctx", None, None),
            P("ctx", None, None),
            P("ctx", None, None),
        ),
        out_specs=P(("req", "ctx"), None),
        check_vma=False,
    )
```

```python
import itertools
import math

import jax
import jax.numpy as jnp
from jax import lax
from jax.sharding import PartitionSpec as P

HEAD_DIM = 128


def attend_gathered(queries, span_keys, span_values, cache_keys, cache_values, length):
    token_count, column_count = queries.shape
    head_count = column_count // HEAD_DIM
    cached_rows = cache_keys.shape[0]
    block_rows = token_count + cached_rows
    scaling = 1.0 / math.sqrt(HEAD_DIM)
    key_block = jnp.concatenate([span_keys, cache_keys], 0)
    value_block = jnp.concatenate([span_values, cache_values], 0)
    piece_keys = lax.all_gather(key_block, "ctx", axis=0, tiled=True)
    piece_values = lax.all_gather(value_block, "ctx", axis=0, tiled=True)
    piece_rows = piece_keys.shape[0]
    index = jnp.arange(piece_rows, dtype=jnp.int32)
    owner = index // block_rows
    within = index % block_rows
    usable = (within < token_count) | (owner * cached_rows + within - token_count < length)
    scores = (
        jnp.einsum(
            "thd,phd->htp",
            queries.reshape(token_count, head_count, HEAD_DIM),
            piece_keys.reshape(piece_rows, head_count, HEAD_DIM),
            preferred_element_type=jnp.float32,
        )
        * scaling
    )
    scores = jnp.where(usable[None, None, :], scores, -1e30)
    peak = jnp.max(scores, axis=2, keepdims=True)
    weights = jnp.where(usable[None, None, :], jnp.exp(scores - peak), 0.0)
    total = jnp.sum(weights, axis=2)
    accum = jnp.einsum(
        "htp,phd->htd",
        weights.astype(jnp.bfloat16),
        piece_values.reshape(piece_rows, head_count, HEAD_DIM),
        preferred_element_type=jnp.float32,
    )
    return (
        (accum / total[:, :, None])
        .transpose(1, 0, 2)
        .reshape(token_count, column_count)
        .astype(jnp.bfloat16)
    )


def attend_by_head(queries, span_keys, span_values, cache_keys, cache_values, length, extra):
    token_count, column_count = queries.shape
    head_count = column_count // HEAD_DIM
    cached_rows = cache_keys.shape[0]
    ctx_count = lax.axis_size("ctx")
    local_heads = head_count // ctx_count
    width = local_heads * HEAD_DIM
    scaling = 1.0 / math.sqrt(HEAD_DIM)
    block_rows = token_count + cached_rows
    sources = [queries, span_keys, cache_keys, span_values, cache_values]
    base_rows = sum(x.shape[0] for x in sources)
    packed = jnp.concatenate(
        [x.reshape(x.shape[0], ctx_count, width).transpose(1, 0, 2) for x in sources]
        + [extra],
        1,
    )
    packed_rows = packed.shape[1]
    got = lax.all_to_all(packed, "ctx", split_axis=0, concat_axis=0, tiled=True)
    got = got.reshape(ctx_count, packed_rows, local_heads, HEAD_DIM)
    query_all = got[:, :token_count].reshape(ctx_count * token_count, local_heads, HEAD_DIM)
    key_all = got[:, token_count : token_count + block_rows].reshape(
        ctx_count * block_rows, local_heads, HEAD_DIM
    )
    extra_got = got[:, base_rows:]
    value_all = got[:, token_count + block_rows : base_rows].reshape(
        ctx_count * block_rows, local_heads, HEAD_DIM
    )
    piece_rows = ctx_count * block_rows
    index = jnp.arange(piece_rows, dtype=jnp.int32)
    owner = index // block_rows
    within = index % block_rows
    usable = (within < token_count) | (owner * cached_rows + within - token_count < length)
    scores = (
        jnp.einsum("thd,phd->htp", query_all, key_all, preferred_element_type=jnp.float32)
        * scaling
    )
    scores = jnp.where(usable[None, None, :], scores, -1e30)
    peak = jnp.max(scores, axis=2, keepdims=True)
    weights = jnp.where(usable[None, None, :], jnp.exp(scores - peak), 0.0)
    total = jnp.sum(weights, axis=2)
    accum = jnp.einsum(
        "htp,phd->thd",
        weights.astype(jnp.bfloat16),
        value_all,
        preferred_element_type=jnp.float32,
    )
    head_out = (accum / total.T[:, :, None]).astype(jnp.bfloat16)
    head_out = head_out.reshape(ctx_count, token_count, width)
    back = lax.all_to_all(head_out, "ctx", split_axis=0, concat_axis=0, tiled=True)
    return back.transpose(1, 0, 2).reshape(token_count, column_count), extra_got


def on_device(
    hidden_in,
    queries,
    span_keys,
    span_values,
    cache_keys,
    cache_values,
    cache_lengths,
    slot_request,
    out_weight,
    norm_gain,
    expert_ids,
    expert_gates,
    gate_proj,
    up_proj,
    down_proj,
):
    token_count, feature_width = hidden_in.shape
    column_count = queries.shape[1]
    head_count = column_count // HEAD_DIM
    ctx_count = lax.axis_size("ctx")
    slot_place = lax.axis_index("req")
    slot_count = slot_request.shape[0]
    slot_range = jnp.arange(slot_count, dtype=jnp.int32)
    request = jnp.sum(jnp.where(slot_range == slot_place, slot_request, 0))
    length = jnp.sum(jnp.where(slot_range == request, cache_lengths, 0))
    local_experts = gate_proj.shape[0]
    expert_total = local_experts * ctx_count
    gate_matrix = jnp.sum(
        jnp.where(
            expert_ids[:, :, None] == jnp.arange(expert_total, dtype=jnp.int32)[None, None, :],
            expert_gates[:, :, None],
            0.0,
        ),
        axis=1,
    )
    first_expert = lax.axis_index("ctx") * local_experts
    if head_count % ctx_count == 0:
        width = column_count // ctx_count
        high = lax.reduce_precision(gate_matrix, exponent_bits=8, mantissa_bits=7)
        rest = gate_matrix - high
        middle = lax.reduce_precision(rest, exponent_bits=8, mantissa_bits=7)
        low = rest - middle
        parts = jnp.stack([high, middle, low], 0).astype(jnp.bfloat16)
        parts = parts.reshape(3, token_count, ctx_count, local_experts)
        parts = parts.transpose(2, 0, 3, 1).reshape(ctx_count, -1)
        part_len = parts.shape[1]
        part_rows = -(-part_len // width)
        parts = jnp.pad(parts, ((0, 0), (0, part_rows * width - part_len)))
        parts = parts.reshape(ctx_count, part_rows, width)
        attended, parts_got = attend_by_head(
            queries, span_keys, span_values, cache_keys, cache_values, length, parts
        )
        parts_got = parts_got.reshape(ctx_count, part_rows * width)[:, :part_len]
        parts_got = parts_got.reshape(ctx_count, 3, local_experts, token_count).astype(
            jnp.float32
        )
        local_gates = (
            (parts_got[:, 0] + parts_got[:, 1]) + parts_got[:, 2]
        ).transpose(1, 0, 2)
    else:
        attended = attend_gathered(
            queries, span_keys, span_values, cache_keys, cache_values, length
        )
        local_gates = lax.all_gather(
            lax.dynamic_slice_in_dim(gate_matrix, first_expert, local_experts, 1).T,
            "ctx",
            axis=1,
            tiled=True,
        ).reshape(local_experts, ctx_count, token_count)
    residual = hidden_in.astype(jnp.float32) + jnp.dot(
        attended, out_weight, preferred_element_type=jnp.float32
    )
    mean_square = jnp.mean(residual * residual, axis=1, keepdims=True)
    normed = (residual * lax.rsqrt(mean_square + 1e-06) * norm_gain).astype(jnp.bfloat16)

    def experts_on(rows, gates):
        moe = None
        for j in range(local_experts):
            gate_val = jnp.dot(rows, gate_proj[j], preferred_element_type=jnp.float32)
            up_val = jnp.dot(rows, up_proj[j], preferred_element_type=jnp.float32)
            activated = (jax.nn.silu(gate_val) * up_val).astype(jnp.bfloat16)
            activated = lax.optimization_barrier(activated)
            produced = jnp.dot(
                activated, down_proj[j], preferred_element_type=jnp.float32
            ).astype(jnp.bfloat16)
            term = gates[j][:, None] * produced.astype(jnp.float32)
            moe = term if moe is None else moe + term
        return moe

    if ctx_count & (ctx_count - 1) == 0 and ctx_count > 1 and token_count % 4 == 0:
        me = lax.axis_index("ctx")
        stream_rows = token_count // 4
        orders = xor_orders(ctx_count)
        moe_pieces = []
        earlier = None
        pending = None
        steps = len(orders[0])
        for group in range(2):
            firsts = [(2 * group + s) * stream_rows for s in range(2)]
            inputs = [normed[f : f + stream_rows] for f in firsts]
            if earlier is not None:
                inputs, _ = lax.optimization_barrier((inputs, earlier))
            helds = gather_xor(inputs, orders, ctx_count)
            earlier = helds
            gates = []
            for first, order in zip(firsts, orders):
                sources = jnp.array(relative_masks(order), jnp.int32) ^ me
                gates.append(
                    jnp.take(
                        local_gates[:, :, first : first + stream_rows], sources, axis=1
                    ).reshape(local_experts, ctx_count * stream_rows)
                )
            rows = jnp.concatenate(
                [held.reshape(ctx_count * stream_rows, feature_width) for held in helds], 0
            )
            if pending is not None:
                rows, pending = lax.optimization_barrier((rows, pending))
                moe_pieces.extend(reduce_xor(pending, orders, ctx_count, steps - 1))
            part = experts_on(rows, jnp.concatenate(gates, 1))
            part = part.reshape(2, ctx_count, stream_rows, feature_width)
            pending = reduce_xor([part[0], part[1]], orders, ctx_count, steps, steps - 1)
        moe_pieces.extend(reduce_xor(pending, orders, ctx_count, steps - 1))
        moe_rows = jnp.concatenate(moe_pieces, 0)
    else:
        normed_all = lax.all_gather(normed, "ctx", axis=0, tiled=True)
        moe = experts_on(normed_all, local_gates.reshape(local_experts, -1))
        moe_rows = lax.psum_scatter(
            moe.astype(jnp.bfloat16), "ctx", scatter_dimension=0, tiled=True
        ).astype(jnp.float32)
    final = (residual + moe_rows).astype(jnp.bfloat16)

    return route_to_request(final, slot_request)


def xor_orders(ctx_count):
    bits = ctx_count.bit_length() - 1
    first = list(range(bits - 1, -1, -1))
    second = list(first)
    if bits >= 3:
        second[0], second[1] = second[1], second[0]
    return [first, second]


def relative_masks(order):
    return [
        sum(((f >> step) & 1) << bit for step, bit in enumerate(order))
        for f in range(1 << len(order))
    ]


def swap(rows, mask, ctx_count):
    return lax.ppermute(rows, "ctx", [(c, c ^ mask) for c in range(ctx_count)])


def gather_xor(rows_list, orders, ctx_count):
    helds = [rows[None] for rows in rows_list]
    for step in range(len(orders[0])):
        masks = [1 << order[step] for order in orders]
        if all(mask == masks[0] for mask in masks):
            got = swap(jnp.stack(helds), masks[0], ctx_count)
            gots = [got[i] for i in range(len(helds))]
        else:
            gots = [swap(held, mask, ctx_count) for held, mask in zip(helds, masks)]
        helds = [jnp.concatenate([held, got], 0) for held, got in zip(helds, gots)]
        helds = list(lax.optimization_barrier(tuple(helds)))
    return helds


def reduce_xor(parts, orders, ctx_count, start=None, stop=0):
    totals = parts
    start = len(orders[0]) if start is None else start
    for step in reversed(range(stop, start)):
        half = totals[0].shape[0] // 2
        masks = [1 << order[step] for order in orders]
        outgoing = [total[half:].astype(jnp.bfloat16) for total in totals]
        if all(mask == masks[0] for mask in masks):
            sent = swap(jnp.stack(outgoing), masks[0], ctx_count)
            sents = [sent[i] for i in range(len(outgoing))]
        else:
            sents = [swap(out, mask, ctx_count) for out, mask in zip(outgoing, masks)]
        totals = [total[:half] + sent.astype(jnp.float32) for total, sent in zip(totals, sents)]
        totals = list(lax.optimization_barrier(tuple(totals)))
    if stop > 0:
        return totals
    return [total[0] for total in totals]


def route_to_request(final, slot_request):
    slot_count = slot_request.shape[0]
    token_count = final.shape[0]
    slot_range = jnp.arange(slot_count, dtype=jnp.int32)
    if slot_count <= 4:
        orders = list(itertools.permutations(range(slot_count)))
        table = jnp.array(orders, jnp.int32)
        match = jnp.all(table == slot_request[None, :], axis=1)
        choice = jnp.sum(jnp.where(match, jnp.arange(len(orders), dtype=jnp.int32), 0))

        def mover(order):
            pairs = [(g, order[g]) for g in range(slot_count)]
            if all(a == b for a, b in pairs):
                return lambda rows: rows
            return lambda rows: lax.ppermute(rows, "req", pairs)

        return lax.switch(choice, [mover(order) for order in orders], final)
    slot_place = lax.axis_index("req")
    source_slot = jnp.sum(jnp.where(slot_request == slot_place, slot_range, 0))
    piece = lax.all_gather(final, "req", axis=0, tiled=True)
    piece_rows = piece.shape[0]
    offset = source_slot * token_count
    inside = (offset >= 0) & (offset + token_count <= piece_rows)
    portion = lax.dynamic_slice_in_dim(
        piece, jnp.clip(offset, 0, piece_rows - token_count), token_count, 0
    )
    return jnp.where(inside, portion, jnp.zeros_like(final))


def solution(mesh):
    return jax.shard_map(
        on_device,
        mesh=mesh,
        in_specs=(
            P(("req", "ctx"), None),
            P(("req", "ctx"), None),
            P(("req", "ctx"), None),
            P(("req", "ctx"), None),
            P(("req", "ctx"), None),
            P(("req", "ctx"), None),
            P(),
            P(),
            P(),
            P(),
            P(("req", "ctx"), None),
            P(("req", "ctx"), None),
            P("ctx", None, None),
            P("ctx", None, None),
            P("ctx", None, None),
        ),
        out_specs=P(("req", "ctx"), None),
        check_vma=False,
    )
```

```python
import itertools
import math

import jax
import jax.numpy as jnp
from jax import lax
from jax.experimental import pallas as pl
from jax.experimental.pallas import tpu as pltpu
from jax.sharding import PartitionSpec as P

HEAD_DIM = 128


def attend_gathered(queries, span_keys, span_values, cache_keys, cache_values, length):
    token_count, column_count = queries.shape
    head_count = column_count // HEAD_DIM
    cached_rows = cache_keys.shape[0]
    block_rows = token_count + cached_rows
    scaling = 1.0 / math.sqrt(HEAD_DIM)
    key_block = jnp.concatenate([span_keys, cache_keys], 0)
    value_block = jnp.concatenate([span_values, cache_values], 0)
    piece_keys = lax.all_gather(key_block, "ctx", axis=0, tiled=True)
    piece_values = lax.all_gather(value_block, "ctx", axis=0, tiled=True)
    piece_rows = piece_keys.shape[0]
    index = jnp.arange(piece_rows, dtype=jnp.int32)
    owner = index // block_rows
    within = index % block_rows
    usable = (within < token_count) | (owner * cached_rows + within - token_count < length)
    scores = (
        jnp.einsum(
            "thd,phd->htp",
            queries.reshape(token_count, head_count, HEAD_DIM),
            piece_keys.reshape(piece_rows, head_count, HEAD_DIM),
            preferred_element_type=jnp.float32,
        )
        * scaling
    )
    scores = jnp.where(usable[None, None, :], scores, -1e30)
    peak = jnp.max(scores, axis=2, keepdims=True)
    weights = jnp.where(usable[None, None, :], jnp.exp(scores - peak), 0.0)
    total = jnp.sum(weights, axis=2)
    accum = jnp.einsum(
        "htp,phd->htd",
        weights.astype(jnp.bfloat16),
        piece_values.reshape(piece_rows, head_count, HEAD_DIM),
        preferred_element_type=jnp.float32,
    )
    return (
        (accum / total[:, :, None])
        .transpose(1, 0, 2)
        .reshape(token_count, column_count)
        .astype(jnp.bfloat16)
    )


def pack_by_destination(sources, extra, width):
    ctx_count = extra.shape[0]
    counts = [x.shape[0] for x in sources] + [extra.shape[1]]
    offsets = [sum(counts[:i]) for i in range(len(counts))]
    total_rows = sum(counts)

    def body(*refs):
        out_ref = refs[-1]
        for i, ref in enumerate(refs[:-2]):
            out_ref[0, offsets[i] : offsets[i] + counts[i], :] = ref[...]
        out_ref[0, offsets[-1] :, :] = refs[-2][0]

    in_specs = [pl.BlockSpec((x.shape[0], width), lambda c: (0, c)) for x in sources]
    in_specs.append(pl.BlockSpec((1, extra.shape[1], width), lambda c: (c, 0, 0)))
    moved = 2 * total_rows * width * ctx_count * extra.dtype.itemsize
    return pl.pallas_call(
        body,
        grid=(ctx_count,),
        in_specs=in_specs,
        out_specs=pl.BlockSpec((1, total_rows, width), lambda c: (c, 0, 0)),
        out_shape=jax.ShapeDtypeStruct((ctx_count, total_rows, width), extra.dtype),
        cost_estimate=pl.CostEstimate(flops=0, transcendentals=0, bytes_accessed=moved),
    )(*sources, extra)


def attend_by_head(queries, span_keys, span_values, cache_keys, cache_values, length, extra):
    token_count, column_count = queries.shape
    head_count = column_count // HEAD_DIM
    cached_rows = cache_keys.shape[0]
    ctx_count = lax.axis_size("ctx")
    local_heads = head_count // ctx_count
    width = local_heads * HEAD_DIM
    scaling = 1.0 / math.sqrt(HEAD_DIM)
    block_rows = token_count + cached_rows
    sources = [queries, span_keys, cache_keys, span_values, cache_values]
    base_rows = sum(x.shape[0] for x in sources)
    packed = pack_by_destination(sources, extra, width)
    packed_rows = packed.shape[1]
    got = lax.all_to_all(packed, "ctx", split_axis=0, concat_axis=0, tiled=True)
    got = got.reshape(ctx_count, packed_rows, local_heads, HEAD_DIM)
    query_all = got[:, :token_count].reshape(ctx_count * token_count, local_heads, HEAD_DIM)
    key_all = got[:, token_count : token_count + block_rows].reshape(
        ctx_count * block_rows, local_heads, HEAD_DIM
    )
    extra_got = got[:, base_rows:]
    value_all = got[:, token_count + block_rows : base_rows].reshape(
        ctx_count * block_rows, local_heads, HEAD_DIM
    )
    piece_rows = ctx_count * block_rows
    index = jnp.arange(piece_rows, dtype=jnp.int32)
    owner = index // block_rows
    within = index % block_rows
    usable = (within < token_count) | (owner * cached_rows + within - token_count < length)
    scores = (
        jnp.einsum("thd,phd->htp", query_all, key_all, preferred_element_type=jnp.float32)
        * scaling
    )
    scores = jnp.where(usable[None, None, :], scores, -1e30)
    peak = jnp.max(scores, axis=2, keepdims=True)
    weights = jnp.where(usable[None, None, :], jnp.exp(scores - peak), 0.0)
    total = jnp.sum(weights, axis=2)
    accum = jnp.einsum(
        "htp,phd->thd",
        weights.astype(jnp.bfloat16),
        value_all,
        preferred_element_type=jnp.float32,
    )
    head_out = (accum / total.T[:, :, None]).astype(jnp.bfloat16)
    head_out = head_out.reshape(ctx_count, token_count, width)
    back = lax.all_to_all(head_out, "ctx", split_axis=0, concat_axis=0, tiled=True)
    return back.transpose(1, 0, 2).reshape(token_count, column_count), extra_got


def on_device(
    hidden_in,
    queries,
    span_keys,
    span_values,
    cache_keys,
    cache_values,
    cache_lengths,
    slot_request,
    out_weight,
    norm_gain,
    expert_ids,
    expert_gates,
    gate_proj,
    up_proj,
    down_proj,
):
    token_count, feature_width = hidden_in.shape
    column_count = queries.shape[1]
    head_count = column_count // HEAD_DIM
    ctx_count = lax.axis_size("ctx")
    slot_place = lax.axis_index("req")
    slot_count = slot_request.shape[0]
    slot_range = jnp.arange(slot_count, dtype=jnp.int32)
    request = jnp.sum(jnp.where(slot_range == slot_place, slot_request, 0))
    length = jnp.sum(jnp.where(slot_range == request, cache_lengths, 0))
    local_experts = gate_proj.shape[0]
    expert_total = local_experts * ctx_count
    gate_matrix = jnp.sum(
        jnp.where(
            expert_ids[:, :, None] == jnp.arange(expert_total, dtype=jnp.int32)[None, None, :],
            expert_gates[:, :, None],
            0.0,
        ),
        axis=1,
    )
    first_expert = lax.axis_index("ctx") * local_experts
    if head_count % ctx_count == 0:
        width = column_count // ctx_count
        high = lax.reduce_precision(gate_matrix, exponent_bits=8, mantissa_bits=7)
        rest = gate_matrix - high
        middle = lax.reduce_precision(rest, exponent_bits=8, mantissa_bits=7)
        low = rest - middle
        parts = jnp.stack([high, middle, low], 0).astype(jnp.bfloat16)
        parts = parts.reshape(3, token_count, ctx_count, local_experts)
        parts = parts.transpose(2, 0, 3, 1).reshape(ctx_count, -1)
        part_len = parts.shape[1]
        part_rows = -(-part_len // width)
        parts = jnp.pad(parts, ((0, 0), (0, part_rows * width - part_len)))
        parts = parts.reshape(ctx_count, part_rows, width)
        attended, parts_got = attend_by_head(
            queries, span_keys, span_values, cache_keys, cache_values, length, parts
        )
        parts_got = parts_got.reshape(ctx_count, part_rows * width)[:, :part_len]
        parts_got = parts_got.reshape(ctx_count, 3, local_experts, token_count).astype(
            jnp.float32
        )
        local_gates = (
            (parts_got[:, 0] + parts_got[:, 1]) + parts_got[:, 2]
        ).transpose(1, 0, 2)
    else:
        attended = attend_gathered(
            queries, span_keys, span_values, cache_keys, cache_values, length
        )
        local_gates = lax.all_gather(
            lax.dynamic_slice_in_dim(gate_matrix, first_expert, local_experts, 1).T,
            "ctx",
            axis=1,
            tiled=True,
        ).reshape(local_experts, ctx_count, token_count)
    residual = hidden_in.astype(jnp.float32) + jnp.dot(
        attended, out_weight, preferred_element_type=jnp.float32
    )
    mean_square = jnp.mean(residual * residual, axis=1, keepdims=True)
    normed = (residual * lax.rsqrt(mean_square + 1e-06) * norm_gain).astype(jnp.bfloat16)

    def experts_on(rows, gates):
        moe = None
        for j in range(local_experts):
            gate_val = jnp.dot(rows, gate_proj[j], preferred_element_type=jnp.float32)
            up_val = jnp.dot(rows, up_proj[j], preferred_element_type=jnp.float32)
            activated = (jax.nn.silu(gate_val) * up_val).astype(jnp.bfloat16)
            activated = lax.optimization_barrier(activated)
            produced = jnp.dot(
                activated, down_proj[j], preferred_element_type=jnp.float32
            ).astype(jnp.bfloat16)
            term = gates[j][:, None] * produced.astype(jnp.float32)
            moe = term if moe is None else moe + term
        return moe

    if ctx_count & (ctx_count - 1) == 0 and ctx_count > 1 and token_count % 4 == 0:
        me = lax.axis_index("ctx")
        stream_rows = token_count // 4
        orders = xor_orders(ctx_count)
        moe_pieces = []
        earlier = None
        pending = None
        steps = len(orders[0])
        for group in range(2):
            firsts = [(2 * group + s) * stream_rows for s in range(2)]
            inputs = [normed[f : f + stream_rows] for f in firsts]
            if earlier is not None:
                inputs, _ = lax.optimization_barrier((inputs, earlier))
            helds = gather_xor(inputs, orders, ctx_count)
            earlier = helds
            gates = []
            for first, order in zip(firsts, orders):
                sources = jnp.array(relative_masks(order), jnp.int32) ^ me
                gates.append(
                    jnp.take(
                        local_gates[:, :, first : first + stream_rows], sources, axis=1
                    ).reshape(local_experts, ctx_count * stream_rows)
                )
            rows = jnp.concatenate(
                [held.reshape(ctx_count * stream_rows, feature_width) for held in helds], 0
            )
            if pending is not None:
                rows, pending = lax.optimization_barrier((rows, pending))
                moe_pieces.extend(reduce_xor(pending, orders, ctx_count, steps - 1))
            part = experts_on(rows, jnp.concatenate(gates, 1))
            part = part.reshape(2, ctx_count, stream_rows, feature_width)
            pending = reduce_xor([part[0], part[1]], orders, ctx_count, steps, steps - 1)
        moe_pieces.extend(reduce_xor(pending, orders, ctx_count, steps - 1))
        moe_rows = jnp.concatenate(moe_pieces, 0)
    else:
        normed_all = lax.all_gather(normed, "ctx", axis=0, tiled=True)
        moe = experts_on(normed_all, local_gates.reshape(local_experts, -1))
        moe_rows = lax.psum_scatter(
            moe.astype(jnp.bfloat16), "ctx", scatter_dimension=0, tiled=True
        ).astype(jnp.float32)
    final = (residual + moe_rows).astype(jnp.bfloat16)

    return route_to_request(final, slot_request)


def xor_orders(ctx_count):
    bits = ctx_count.bit_length() - 1
    first = list(range(bits - 1, -1, -1))
    second = list(first)
    if bits >= 3:
        second[0], second[1] = second[1], second[0]
    return [first, second]


def relative_masks(order):
    return [
        sum(((f >> step) & 1) << bit for step, bit in enumerate(order))
        for f in range(1 << len(order))
    ]


def swap(rows, mask, ctx_count):
    return lax.ppermute(rows, "ctx", [(c, c ^ mask) for c in range(ctx_count)])


def gather_xor(rows_list, orders, ctx_count):
    helds = [rows[None] for rows in rows_list]
    for step in range(len(orders[0])):
        masks = [1 << order[step] for order in orders]
        if all(mask == masks[0] for mask in masks):
            got = swap(jnp.stack(helds), masks[0], ctx_count)
            gots = [got[i] for i in range(len(helds))]
        else:
            gots = [swap(held, mask, ctx_count) for held, mask in zip(helds, masks)]
        helds = [jnp.concatenate([held, got], 0) for held, got in zip(helds, gots)]
        helds = list(lax.optimization_barrier(tuple(helds)))
    return helds


def reduce_xor(parts, orders, ctx_count, start=None, stop=0):
    totals = parts
    start = len(orders[0]) if start is None else start
    for step in reversed(range(stop, start)):
        half = totals[0].shape[0] // 2
        masks = [1 << order[step] for order in orders]
        outgoing = [total[half:].astype(jnp.bfloat16) for total in totals]
        if all(mask == masks[0] for mask in masks):
            sent = swap(jnp.stack(outgoing), masks[0], ctx_count)
            sents = [sent[i] for i in range(len(outgoing))]
        else:
            sents = [swap(out, mask, ctx_count) for out, mask in zip(outgoing, masks)]
        totals = [total[:half] + sent.astype(jnp.float32) for total, sent in zip(totals, sents)]
        totals = list(lax.optimization_barrier(tuple(totals)))
    if stop > 0:
        return totals
    return [total[0] for total in totals]


def route_to_request(final, slot_request):
    slot_count = slot_request.shape[0]
    token_count = final.shape[0]
    slot_range = jnp.arange(slot_count, dtype=jnp.int32)
    if slot_count <= 4:
        orders = list(itertools.permutations(range(slot_count)))
        table = jnp.array(orders, jnp.int32)
        match = jnp.all(table == slot_request[None, :], axis=1)
        choice = jnp.sum(jnp.where(match, jnp.arange(len(orders), dtype=jnp.int32), 0))

        def mover(order):
            pairs = [(g, order[g]) for g in range(slot_count)]
            if all(a == b for a, b in pairs):
                return lambda rows: rows
            return lambda rows: lax.ppermute(rows, "req", pairs)

        return lax.switch(choice, [mover(order) for order in orders], final)
    slot_place = lax.axis_index("req")
    source_slot = jnp.sum(jnp.where(slot_request == slot_place, slot_range, 0))
    piece = lax.all_gather(final, "req", axis=0, tiled=True)
    piece_rows = piece.shape[0]
    offset = source_slot * token_count
    inside = (offset >= 0) & (offset + token_count <= piece_rows)
    portion = lax.dynamic_slice_in_dim(
        piece, jnp.clip(offset, 0, piece_rows - token_count), token_count, 0
    )
    return jnp.where(inside, portion, jnp.zeros_like(final))


def solution(mesh):
    return jax.shard_map(
        on_device,
        mesh=mesh,
        in_specs=(
            P(("req", "ctx"), None),
            P(("req", "ctx"), None),
            P(("req", "ctx"), None),
            P(("req", "ctx"), None),
            P(("req", "ctx"), None),
            P(("req", "ctx"), None),
            P(),
            P(),
            P(),
            P(),
            P(("req", "ctx"), None),
            P(("req", "ctx"), None),
            P("ctx", None, None),
            P("ctx", None, None),
            P("ctx", None, None),
        ),
        out_specs=P(("req", "ctx"), None),
        check_vma=False,
    )
```

```python
import itertools
import math

import jax
import jax.numpy as jnp
from jax import lax
from jax.experimental import pallas as pl
from jax.experimental.pallas import tpu as pltpu
from jax.sharding import PartitionSpec as P

HEAD_DIM = 128


def attend_gathered(queries, span_keys, span_values, cache_keys, cache_values, length):
    token_count, column_count = queries.shape
    head_count = column_count // HEAD_DIM
    cached_rows = cache_keys.shape[0]
    block_rows = token_count + cached_rows
    scaling = 1.0 / math.sqrt(HEAD_DIM)
    key_block = jnp.concatenate([span_keys, cache_keys], 0)
    value_block = jnp.concatenate([span_values, cache_values], 0)
    piece_keys = lax.all_gather(key_block, "ctx", axis=0, tiled=True)
    piece_values = lax.all_gather(value_block, "ctx", axis=0, tiled=True)
    piece_rows = piece_keys.shape[0]
    index = jnp.arange(piece_rows, dtype=jnp.int32)
    owner = index // block_rows
    within = index % block_rows
    usable = (within < token_count) | (owner * cached_rows + within - token_count < length)
    scores = (
        jnp.einsum(
            "thd,phd->htp",
            queries.reshape(token_count, head_count, HEAD_DIM),
            piece_keys.reshape(piece_rows, head_count, HEAD_DIM),
            preferred_element_type=jnp.float32,
        )
        * scaling
    )
    scores = jnp.where(usable[None, None, :], scores, -1e30)
    peak = jnp.max(scores, axis=2, keepdims=True)
    weights = jnp.where(usable[None, None, :], jnp.exp(scores - peak), 0.0)
    total = jnp.sum(weights, axis=2)
    accum = jnp.einsum(
        "htp,phd->htd",
        weights.astype(jnp.bfloat16),
        piece_values.reshape(piece_rows, head_count, HEAD_DIM),
        preferred_element_type=jnp.float32,
    )
    return (
        (accum / total[:, :, None])
        .transpose(1, 0, 2)
        .reshape(token_count, column_count)
        .astype(jnp.bfloat16)
    )


def pack_by_destination(sources, extra, width):
    ctx_count = extra.shape[0]
    counts = [x.shape[0] for x in sources] + [extra.shape[1]]
    offsets = [sum(counts[:i]) for i in range(len(counts))]
    total_rows = sum(counts)

    def body(*refs):
        out_ref = refs[-1]
        for i, ref in enumerate(refs[:-2]):
            out_ref[0, offsets[i] : offsets[i] + counts[i], :] = ref[...]
        out_ref[0, offsets[-1] :, :] = refs[-2][0]

    in_specs = [pl.BlockSpec((x.shape[0], width), lambda c: (0, c)) for x in sources]
    in_specs.append(pl.BlockSpec((1, extra.shape[1], width), lambda c: (c, 0, 0)))
    moved = 2 * total_rows * width * ctx_count * extra.dtype.itemsize
    return pl.pallas_call(
        body,
        grid=(ctx_count,),
        in_specs=in_specs,
        out_specs=pl.BlockSpec((1, total_rows, width), lambda c: (c, 0, 0)),
        out_shape=jax.ShapeDtypeStruct((ctx_count, total_rows, width), extra.dtype),
        cost_estimate=pl.CostEstimate(flops=0, transcendentals=0, bytes_accessed=moved),
    )(*sources, extra)


def attend_by_head(
    queries, span_keys, span_values, cache_keys, cache_values, length, extra, companion
):
    token_count, column_count = queries.shape
    head_count = column_count // HEAD_DIM
    cached_rows = cache_keys.shape[0]
    ctx_count = lax.axis_size("ctx")
    local_heads = head_count // ctx_count
    width = local_heads * HEAD_DIM
    scaling = 1.0 / math.sqrt(HEAD_DIM)
    block_rows = token_count + cached_rows
    sources = [queries, span_keys, cache_keys, span_values, cache_values]
    base_rows = sum(x.shape[0] for x in sources)
    packed = pack_by_destination(sources, extra, width)
    packed_rows = packed.shape[1]
    got = lax.all_to_all(packed, "ctx", split_axis=0, concat_axis=0, tiled=True)
    got, companion = lax.optimization_barrier((got, companion))
    got = got.reshape(ctx_count, packed_rows, local_heads, HEAD_DIM)
    query_all = got[:, :token_count].reshape(ctx_count * token_count, local_heads, HEAD_DIM)
    key_all = got[:, token_count : token_count + block_rows].reshape(
        ctx_count * block_rows, local_heads, HEAD_DIM
    )
    extra_got = got[:, base_rows:]
    value_all = got[:, token_count + block_rows : base_rows].reshape(
        ctx_count * block_rows, local_heads, HEAD_DIM
    )
    piece_rows = ctx_count * block_rows
    index = jnp.arange(piece_rows, dtype=jnp.int32)
    owner = index // block_rows
    within = index % block_rows
    usable = (within < token_count) | (owner * cached_rows + within - token_count < length)
    scores = (
        jnp.einsum("thd,phd->htp", query_all, key_all, preferred_element_type=jnp.float32)
        * scaling
    )
    scores = jnp.where(usable[None, None, :], scores, -1e30)
    peak = jnp.max(scores, axis=2, keepdims=True)
    weights = jnp.where(usable[None, None, :], jnp.exp(scores - peak), 0.0)
    total = jnp.sum(weights, axis=2)
    accum = jnp.einsum(
        "htp,phd->thd",
        weights.astype(jnp.bfloat16),
        value_all,
        preferred_element_type=jnp.float32,
    )
    head_out = (accum / total.T[:, :, None]).astype(jnp.bfloat16)
    head_out = head_out.reshape(ctx_count, token_count, width)
    back = lax.all_to_all(head_out, "ctx", split_axis=0, concat_axis=0, tiled=True)
    return back.transpose(1, 0, 2).reshape(token_count, column_count), extra_got, companion


def on_device(
    hidden_in,
    queries,
    span_keys,
    span_values,
    cache_keys,
    cache_values,
    cache_lengths,
    slot_request,
    out_weight,
    norm_gain,
    expert_ids,
    expert_gates,
    gate_proj,
    up_proj,
    down_proj,
):
    token_count, feature_width = hidden_in.shape
    column_count = queries.shape[1]
    head_count = column_count // HEAD_DIM
    ctx_count = lax.axis_size("ctx")
    slot_place = lax.axis_index("req")
    slot_count = slot_request.shape[0]
    slot_range = jnp.arange(slot_count, dtype=jnp.int32)
    request = jnp.sum(jnp.where(slot_range == slot_place, slot_request, 0))
    length = jnp.sum(jnp.where(slot_range == request, cache_lengths, 0))
    local_experts = gate_proj.shape[0]
    expert_total = local_experts * ctx_count
    gate_matrix = jnp.sum(
        jnp.where(
            expert_ids[:, :, None] == jnp.arange(expert_total, dtype=jnp.int32)[None, None, :],
            expert_gates[:, :, None],
            0.0,
        ),
        axis=1,
    )
    first_expert = lax.axis_index("ctx") * local_experts
    if head_count % ctx_count == 0:
        width = column_count // ctx_count
        high = lax.reduce_precision(gate_matrix, exponent_bits=8, mantissa_bits=7)
        rest = gate_matrix - high
        middle = lax.reduce_precision(rest, exponent_bits=8, mantissa_bits=7)
        low = rest - middle
        parts = jnp.stack([high, middle, low], 0).astype(jnp.bfloat16)
        parts = parts.reshape(3, token_count, ctx_count, local_experts)
        parts = parts.transpose(2, 0, 3, 1).reshape(ctx_count, -1)
        part_len = parts.shape[1]
        part_rows = -(-part_len // width)
        parts = jnp.pad(parts, ((0, 0), (0, part_rows * width - part_len)))
        parts = parts.reshape(ctx_count, part_rows, width)
        hidden_in = route_to_request(hidden_in, slot_request)
        attended, parts_got, hidden_in = attend_by_head(
            queries, span_keys, span_values, cache_keys, cache_values, length, parts, hidden_in
        )
        carried = jnp.concatenate([attended, parts_got.reshape(-1, column_count)], 0)
        carried = route_to_request(carried, slot_request)
        attended = carried[:token_count]
        parts_got = carried[token_count:]
        routed = True
        parts_got = parts_got.reshape(ctx_count, part_rows * width)[:, :part_len]
        parts_got = parts_got.reshape(ctx_count, 3, local_experts, token_count).astype(
            jnp.float32
        )
        local_gates = (
            (parts_got[:, 0] + parts_got[:, 1]) + parts_got[:, 2]
        ).transpose(1, 0, 2)
    else:
        routed = False
        attended = attend_gathered(
            queries, span_keys, span_values, cache_keys, cache_values, length
        )
        local_gates = lax.all_gather(
            lax.dynamic_slice_in_dim(gate_matrix, first_expert, local_experts, 1).T,
            "ctx",
            axis=1,
            tiled=True,
        ).reshape(local_experts, ctx_count, token_count)
    residual = hidden_in.astype(jnp.float32) + jnp.dot(
        attended, out_weight, preferred_element_type=jnp.float32
    )
    mean_square = jnp.mean(residual * residual, axis=1, keepdims=True)
    normed = (residual * lax.rsqrt(mean_square + 1e-06) * norm_gain).astype(jnp.bfloat16)

    def experts_on(rows, gates):
        moe = None
        for j in range(local_experts):
            gate_val = jnp.dot(rows, gate_proj[j], preferred_element_type=jnp.float32)
            up_val = jnp.dot(rows, up_proj[j], preferred_element_type=jnp.float32)
            activated = (jax.nn.silu(gate_val) * up_val).astype(jnp.bfloat16)
            activated = lax.optimization_barrier(activated)
            produced = jnp.dot(
                activated, down_proj[j], preferred_element_type=jnp.float32
            ).astype(jnp.bfloat16)
            term = gates[j][:, None] * produced.astype(jnp.float32)
            moe = term if moe is None else moe + term
        return moe

    if ctx_count & (ctx_count - 1) == 0 and ctx_count > 1 and token_count % 4 == 0:
        me = lax.axis_index("ctx")
        stream_rows = token_count // 4
        orders = xor_orders(ctx_count)
        moe_pieces = []
        earlier = None
        pending = None
        steps = len(orders[0])
        for group in range(2):
            firsts = [(2 * group + s) * stream_rows for s in range(2)]
            inputs = [normed[f : f + stream_rows] for f in firsts]
            if earlier is not None:
                inputs, _ = lax.optimization_barrier((inputs, earlier))
            helds = gather_xor(inputs, orders, ctx_count)
            earlier = helds
            gates = []
            for first, order in zip(firsts, orders):
                sources = jnp.array(relative_masks(order), jnp.int32) ^ me
                gates.append(
                    jnp.take(
                        local_gates[:, :, first : first + stream_rows], sources, axis=1
                    ).reshape(local_experts, ctx_count * stream_rows)
                )
            rows = jnp.concatenate(
                [held.reshape(ctx_count * stream_rows, feature_width) for held in helds], 0
            )
            if pending is not None:
                rows, pending = lax.optimization_barrier((rows, pending))
                moe_pieces.extend(reduce_xor(pending, orders, ctx_count, steps - 1))
            part = experts_on(rows, jnp.concatenate(gates, 1))
            part = part.reshape(2, ctx_count, stream_rows, feature_width)
            pending = reduce_xor([part[0], part[1]], orders, ctx_count, steps, steps - 1)
        moe_pieces.extend(reduce_xor(pending, orders, ctx_count, steps - 1))
        moe_rows = jnp.concatenate(moe_pieces, 0)
    else:
        normed_all = lax.all_gather(normed, "ctx", axis=0, tiled=True)
        moe = experts_on(normed_all, local_gates.reshape(local_experts, -1))
        moe_rows = lax.psum_scatter(
            moe.astype(jnp.bfloat16), "ctx", scatter_dimension=0, tiled=True
        ).astype(jnp.float32)
    final = (residual + moe_rows).astype(jnp.bfloat16)

    if routed:
        return final
    return route_to_request(final, slot_request)


def xor_orders(ctx_count):
    bits = ctx_count.bit_length() - 1
    first = list(range(bits - 1, -1, -1))
    second = list(first)
    if bits >= 3:
        second[0], second[1] = second[1], second[0]
    return [first, second]


def relative_masks(order):
    return [
        sum(((f >> step) & 1) << bit for step, bit in enumerate(order))
        for f in range(1 << len(order))
    ]


def swap(rows, mask, ctx_count):
    return lax.ppermute(rows, "ctx", [(c, c ^ mask) for c in range(ctx_count)])


def gather_xor(rows_list, orders, ctx_count):
    helds = [rows[None] for rows in rows_list]
    for step in range(len(orders[0])):
        masks = [1 << order[step] for order in orders]
        if all(mask == masks[0] for mask in masks):
            got = swap(jnp.stack(helds), masks[0], ctx_count)
            gots = [got[i] for i in range(len(helds))]
        else:
            gots = [swap(held, mask, ctx_count) for held, mask in zip(helds, masks)]
        helds = [jnp.concatenate([held, got], 0) for held, got in zip(helds, gots)]
        helds = list(lax.optimization_barrier(tuple(helds)))
    return helds


def reduce_xor(parts, orders, ctx_count, start=None, stop=0):
    totals = parts
    start = len(orders[0]) if start is None else start
    for step in reversed(range(stop, start)):
        half = totals[0].shape[0] // 2
        masks = [1 << order[step] for order in orders]
        outgoing = [total[half:].astype(jnp.bfloat16) for total in totals]
        if all(mask == masks[0] for mask in masks):
            sent = swap(jnp.stack(outgoing), masks[0], ctx_count)
            sents = [sent[i] for i in range(len(outgoing))]
        else:
            sents = [swap(out, mask, ctx_count) for out, mask in zip(outgoing, masks)]
        totals = [total[:half] + sent.astype(jnp.float32) for total, sent in zip(totals, sents)]
        totals = list(lax.optimization_barrier(tuple(totals)))
    if stop > 0:
        return totals
    return [total[0] for total in totals]


def route_to_request(final, slot_request):
    slot_count = slot_request.shape[0]
    token_count = final.shape[0]
    slot_range = jnp.arange(slot_count, dtype=jnp.int32)
    if slot_count <= 4:
        orders = list(itertools.permutations(range(slot_count)))
        table = jnp.array(orders, jnp.int32)
        match = jnp.all(table == slot_request[None, :], axis=1)
        choice = jnp.sum(jnp.where(match, jnp.arange(len(orders), dtype=jnp.int32), 0))

        def mover(order):
            pairs = [(g, order[g]) for g in range(slot_count)]
            if all(a == b for a, b in pairs):
                return lambda rows: rows
            return lambda rows: lax.ppermute(rows, "req", pairs)

        return lax.switch(choice, [mover(order) for order in orders], final)
    slot_place = lax.axis_index("req")
    source_slot = jnp.sum(jnp.where(slot_request == slot_place, slot_range, 0))
    piece = lax.all_gather(final, "req", axis=0, tiled=True)
    piece_rows = piece.shape[0]
    offset = source_slot * token_count
    inside = (offset >= 0) & (offset + token_count <= piece_rows)
    portion = lax.dynamic_slice_in_dim(
        piece, jnp.clip(offset, 0, piece_rows - token_count), token_count, 0
    )
    return jnp.where(inside, portion, jnp.zeros_like(final))


def solution(mesh):
    return jax.shard_map(
        on_device,
        mesh=mesh,
        in_specs=(
            P(("req", "ctx"), None),
            P(("req", "ctx"), None),
            P(("req", "ctx"), None),
            P(("req", "ctx"), None),
            P(("req", "ctx"), None),
            P(("req", "ctx"), None),
            P(),
            P(),
            P(),
            P(),
            P(("req", "ctx"), None),
            P(("req", "ctx"), None),
            P("ctx", None, None),
            P("ctx", None, None),
            P("ctx", None, None),
        ),
        out_specs=P(("req", "ctx"), None),
        check_vma=False,
    )
```

```python
import itertools
import math

import jax
import jax.numpy as jnp
from jax import lax
from jax.experimental import pallas as pl
from jax.experimental.pallas import tpu as pltpu
from jax.sharding import PartitionSpec as P

HEAD_DIM = 128


def attend_gathered(queries, span_keys, span_values, cache_keys, cache_values, length):
    token_count, column_count = queries.shape
    head_count = column_count // HEAD_DIM
    cached_rows = cache_keys.shape[0]
    block_rows = token_count + cached_rows
    scaling = 1.0 / math.sqrt(HEAD_DIM)
    key_block = jnp.concatenate([span_keys, cache_keys], 0)
    value_block = jnp.concatenate([span_values, cache_values], 0)
    piece_keys = lax.all_gather(key_block, "ctx", axis=0, tiled=True)
    piece_values = lax.all_gather(value_block, "ctx", axis=0, tiled=True)
    piece_rows = piece_keys.shape[0]
    index = jnp.arange(piece_rows, dtype=jnp.int32)
    owner = index // block_rows
    within = index % block_rows
    usable = (within < token_count) | (owner * cached_rows + within - token_count < length)
    scores = (
        jnp.einsum(
            "thd,phd->htp",
            queries.reshape(token_count, head_count, HEAD_DIM),
            piece_keys.reshape(piece_rows, head_count, HEAD_DIM),
            preferred_element_type=jnp.float32,
        )
        * scaling
    )
    scores = jnp.where(usable[None, None, :], scores, -1e30)
    peak = jnp.max(scores, axis=2, keepdims=True)
    weights = jnp.where(usable[None, None, :], jnp.exp(scores - peak), 0.0)
    total = jnp.sum(weights, axis=2)
    accum = jnp.einsum(
        "htp,phd->htd",
        weights.astype(jnp.bfloat16),
        piece_values.reshape(piece_rows, head_count, HEAD_DIM),
        preferred_element_type=jnp.float32,
    )
    return (
        (accum / total[:, :, None])
        .transpose(1, 0, 2)
        .reshape(token_count, column_count)
        .astype(jnp.bfloat16)
    )


def pack_by_destination(sources, extra, width):
    ctx_count = extra.shape[0]
    counts = [x.shape[0] for x in sources] + [extra.shape[1]]
    offsets = [sum(counts[:i]) for i in range(len(counts))]
    total_rows = sum(counts)

    def body(*refs):
        out_ref = refs[-1]

        def one(c, carry):
            columns = pl.ds(pl.multiple_of(c * width, width), width)
            for i, ref in enumerate(refs[:-2]):
                out_ref[c, offsets[i] : offsets[i] + counts[i], :] = ref[:, columns]
            out_ref[c, offsets[-1] :, :] = refs[-2][c]
            return carry

        lax.fori_loop(0, ctx_count, one, 0)

    moved = 2 * total_rows * width * ctx_count * extra.dtype.itemsize
    vmem = pl.BlockSpec(memory_space=pltpu.VMEM)
    return pl.pallas_call(
        body,
        in_specs=[vmem] * (len(sources) + 1),
        out_specs=vmem,
        out_shape=jax.ShapeDtypeStruct((ctx_count, total_rows, width), extra.dtype),
        cost_estimate=pl.CostEstimate(flops=0, transcendentals=0, bytes_accessed=moved),
    )(*sources, extra)


def attend_by_head(
    queries, span_keys, span_values, cache_keys, cache_values, length, extra, companion
):
    token_count, column_count = queries.shape
    head_count = column_count // HEAD_DIM
    cached_rows = cache_keys.shape[0]
    ctx_count = lax.axis_size("ctx")
    local_heads = head_count // ctx_count
    width = local_heads * HEAD_DIM
    scaling = 1.0 / math.sqrt(HEAD_DIM)
    block_rows = token_count + cached_rows
    sources = [queries, span_keys, cache_keys, span_values, cache_values]
    base_rows = sum(x.shape[0] for x in sources)
    packed = pack_by_destination(sources, extra, width)
    packed_rows = packed.shape[1]
    got = lax.all_to_all(packed, "ctx", split_axis=0, concat_axis=0, tiled=True)
    got, companion = lax.optimization_barrier((got, companion))
    got = got.reshape(ctx_count, packed_rows, local_heads, HEAD_DIM)
    query_all = got[:, :token_count].reshape(ctx_count * token_count, local_heads, HEAD_DIM)
    key_all = got[:, token_count : token_count + block_rows].reshape(
        ctx_count * block_rows, local_heads, HEAD_DIM
    )
    extra_got = got[:, base_rows:]
    value_all = got[:, token_count + block_rows : base_rows].reshape(
        ctx_count * block_rows, local_heads, HEAD_DIM
    )
    piece_rows = ctx_count * block_rows
    index = jnp.arange(piece_rows, dtype=jnp.int32)
    owner = index // block_rows
    within = index % block_rows
    usable = (within < token_count) | (owner * cached_rows + within - token_count < length)
    scores = (
        jnp.einsum("thd,phd->htp", query_all, key_all, preferred_element_type=jnp.float32)
        * scaling
    )
    scores = jnp.where(usable[None, None, :], scores, -1e30)
    peak = jnp.max(scores, axis=2, keepdims=True)
    weights = jnp.where(usable[None, None, :], jnp.exp(scores - peak), 0.0)
    total = jnp.sum(weights, axis=2)
    accum = jnp.einsum(
        "htp,phd->thd",
        weights.astype(jnp.bfloat16),
        value_all,
        preferred_element_type=jnp.float32,
    )
    head_out = (accum / total.T[:, :, None]).astype(jnp.bfloat16)
    head_out = head_out.reshape(ctx_count, token_count, width)
    back = lax.all_to_all(head_out, "ctx", split_axis=0, concat_axis=0, tiled=True)
    return back.transpose(1, 0, 2).reshape(token_count, column_count), extra_got, companion


def on_device(
    hidden_in,
    queries,
    span_keys,
    span_values,
    cache_keys,
    cache_values,
    cache_lengths,
    slot_request,
    out_weight,
    norm_gain,
    expert_ids,
    expert_gates,
    gate_proj,
    up_proj,
    down_proj,
):
    token_count, feature_width = hidden_in.shape
    column_count = queries.shape[1]
    head_count = column_count // HEAD_DIM
    ctx_count = lax.axis_size("ctx")
    slot_place = lax.axis_index("req")
    slot_count = slot_request.shape[0]
    slot_range = jnp.arange(slot_count, dtype=jnp.int32)
    request = jnp.sum(jnp.where(slot_range == slot_place, slot_request, 0))
    length = jnp.sum(jnp.where(slot_range == request, cache_lengths, 0))
    local_experts = gate_proj.shape[0]
    expert_total = local_experts * ctx_count
    gate_matrix = jnp.sum(
        jnp.where(
            expert_ids[:, :, None] == jnp.arange(expert_total, dtype=jnp.int32)[None, None, :],
            expert_gates[:, :, None],
            0.0,
        ),
        axis=1,
    )
    first_expert = lax.axis_index("ctx") * local_experts
    if head_count % ctx_count == 0:
        width = column_count // ctx_count
        high = lax.reduce_precision(gate_matrix, exponent_bits=8, mantissa_bits=7)
        rest = gate_matrix - high
        middle = lax.reduce_precision(rest, exponent_bits=8, mantissa_bits=7)
        low = rest - middle
        parts = jnp.stack([high, middle, low], 0).astype(jnp.bfloat16)
        parts = parts.reshape(3, token_count, ctx_count, local_experts)
        parts = parts.transpose(2, 0, 3, 1).reshape(ctx_count, -1)
        part_len = parts.shape[1]
        part_rows = -(-part_len // width)
        parts = jnp.pad(parts, ((0, 0), (0, part_rows * width - part_len)))
        parts = parts.reshape(ctx_count, part_rows, width)
        hidden_in = route_to_request(hidden_in, slot_request)
        attended, parts_got, hidden_in = attend_by_head(
            queries, span_keys, span_values, cache_keys, cache_values, length, parts, hidden_in
        )
        carried = jnp.concatenate([attended, parts_got.reshape(-1, column_count)], 0)
        carried = route_to_request(carried, slot_request)
        attended = carried[:token_count]
        parts_got = carried[token_count:]
        routed = True
        parts_got = parts_got.reshape(ctx_count, part_rows * width)[:, :part_len]
        parts_got = parts_got.reshape(ctx_count, 3, local_experts, token_count).astype(
            jnp.float32
        )
        local_gates = (
            (parts_got[:, 0] + parts_got[:, 1]) + parts_got[:, 2]
        ).transpose(1, 0, 2)
    else:
        routed = False
        attended = attend_gathered(
            queries, span_keys, span_values, cache_keys, cache_values, length
        )
        local_gates = lax.all_gather(
            lax.dynamic_slice_in_dim(gate_matrix, first_expert, local_experts, 1).T,
            "ctx",
            axis=1,
            tiled=True,
        ).reshape(local_experts, ctx_count, token_count)
    residual = hidden_in.astype(jnp.float32) + jnp.dot(
        attended, out_weight, preferred_element_type=jnp.float32
    )
    mean_square = jnp.mean(residual * residual, axis=1, keepdims=True)
    normed = (residual * lax.rsqrt(mean_square + 1e-06) * norm_gain).astype(jnp.bfloat16)

    def experts_on(rows, gates):
        moe = None
        for j in range(local_experts):
            gate_val = jnp.dot(rows, gate_proj[j], preferred_element_type=jnp.float32)
            up_val = jnp.dot(rows, up_proj[j], preferred_element_type=jnp.float32)
            activated = (jax.nn.silu(gate_val) * up_val).astype(jnp.bfloat16)
            activated = lax.optimization_barrier(activated)
            produced = jnp.dot(
                activated, down_proj[j], preferred_element_type=jnp.float32
            ).astype(jnp.bfloat16)
            term = gates[j][:, None] * produced.astype(jnp.float32)
            moe = term if moe is None else moe + term
        return moe

    if ctx_count & (ctx_count - 1) == 0 and ctx_count > 1 and token_count % 4 == 0:
        me = lax.axis_index("ctx")
        stream_rows = token_count // 4
        orders = xor_orders(ctx_count)
        moe_pieces = []
        earlier = None
        pending = None
        steps = len(orders[0])
        for group in range(2):
            firsts = [(2 * group + s) * stream_rows for s in range(2)]
            inputs = [normed[f : f + stream_rows] for f in firsts]
            if earlier is not None:
                inputs, _ = lax.optimization_barrier((inputs, earlier))
            helds = gather_xor(inputs, orders, ctx_count)
            earlier = helds
            gates = []
            for first, order in zip(firsts, orders):
                sources = jnp.array(relative_masks(order), jnp.int32) ^ me
                gates.append(
                    jnp.take(
                        local_gates[:, :, first : first + stream_rows], sources, axis=1
                    ).reshape(local_experts, ctx_count * stream_rows)
                )
            rows = jnp.concatenate(
                [held.reshape(ctx_count * stream_rows, feature_width) for held in helds], 0
            )
            if pending is not None:
                rows, pending = lax.optimization_barrier((rows, pending))
                moe_pieces.extend(reduce_xor(pending, orders, ctx_count, steps - 1))
            part = experts_on(rows, jnp.concatenate(gates, 1))
            part = part.reshape(2, ctx_count, stream_rows, feature_width)
            pending = reduce_xor([part[0], part[1]], orders, ctx_count, steps, steps - 1)
        moe_pieces.extend(reduce_xor(pending, orders, ctx_count, steps - 1))
        moe_rows = jnp.concatenate(moe_pieces, 0)
    else:
        normed_all = lax.all_gather(normed, "ctx", axis=0, tiled=True)
        moe = experts_on(normed_all, local_gates.reshape(local_experts, -1))
        moe_rows = lax.psum_scatter(
            moe.astype(jnp.bfloat16), "ctx", scatter_dimension=0, tiled=True
        ).astype(jnp.float32)
    final = (residual + moe_rows).astype(jnp.bfloat16)

    if routed:
        return final
    return route_to_request(final, slot_request)


def xor_orders(ctx_count):
    bits = ctx_count.bit_length() - 1
    first = list(range(bits - 1, -1, -1))
    second = list(first)
    if bits >= 3:
        second[0], second[1] = second[1], second[0]
    return [first, second]


def relative_masks(order):
    return [
        sum(((f >> step) & 1) << bit for step, bit in enumerate(order))
        for f in range(1 << len(order))
    ]


def swap(rows, mask, ctx_count):
    return lax.ppermute(rows, "ctx", [(c, c ^ mask) for c in range(ctx_count)])


def gather_xor(rows_list, orders, ctx_count):
    helds = [rows[None] for rows in rows_list]
    for step in range(len(orders[0])):
        masks = [1 << order[step] for order in orders]
        if all(mask == masks[0] for mask in masks):
            got = swap(jnp.stack(helds), masks[0], ctx_count)
            gots = [got[i] for i in range(len(helds))]
        else:
            gots = [swap(held, mask, ctx_count) for held, mask in zip(helds, masks)]
        helds = [jnp.concatenate([held, got], 0) for held, got in zip(helds, gots)]
        helds = list(lax.optimization_barrier(tuple(helds)))
    return helds


def reduce_xor(parts, orders, ctx_count, start=None, stop=0):
    totals = parts
    start = len(orders[0]) if start is None else start
    for step in reversed(range(stop, start)):
        half = totals[0].shape[0] // 2
        masks = [1 << order[step] for order in orders]
        outgoing = [total[half:].astype(jnp.bfloat16) for total in totals]
        if all(mask == masks[0] for mask in masks):
            sent = swap(jnp.stack(outgoing), masks[0], ctx_count)
            sents = [sent[i] for i in range(len(outgoing))]
        else:
            sents = [swap(out, mask, ctx_count) for out, mask in zip(outgoing, masks)]
        totals = [total[:half] + sent.astype(jnp.float32) for total, sent in zip(totals, sents)]
        totals = list(lax.optimization_barrier(tuple(totals)))
    if stop > 0:
        return totals
    return [total[0] for total in totals]


def route_to_request(final, slot_request):
    slot_count = slot_request.shape[0]
    token_count = final.shape[0]
    slot_range = jnp.arange(slot_count, dtype=jnp.int32)
    if slot_count <= 4:
        orders = list(itertools.permutations(range(slot_count)))
        table = jnp.array(orders, jnp.int32)
        match = jnp.all(table == slot_request[None, :], axis=1)
        choice = jnp.sum(jnp.where(match, jnp.arange(len(orders), dtype=jnp.int32), 0))

        def mover(order):
            pairs = [(g, order[g]) for g in range(slot_count)]
            if all(a == b for a, b in pairs):
                return lambda rows: rows
            return lambda rows: lax.ppermute(rows, "req", pairs)

        return lax.switch(choice, [mover(order) for order in orders], final)
    slot_place = lax.axis_index("req")
    source_slot = jnp.sum(jnp.where(slot_request == slot_place, slot_range, 0))
    piece = lax.all_gather(final, "req", axis=0, tiled=True)
    piece_rows = piece.shape[0]
    offset = source_slot * token_count
    inside = (offset >= 0) & (offset + token_count <= piece_rows)
    portion = lax.dynamic_slice_in_dim(
        piece, jnp.clip(offset, 0, piece_rows - token_count), token_count, 0
    )
    return jnp.where(inside, portion, jnp.zeros_like(final))


def solution(mesh):
    return jax.shard_map(
        on_device,
        mesh=mesh,
        in_specs=(
            P(("req", "ctx"), None),
            P(("req", "ctx"), None),
            P(("req", "ctx"), None),
            P(("req", "ctx"), None),
            P(("req", "ctx"), None),
            P(("req", "ctx"), None),
            P(),
            P(),
            P(),
            P(),
            P(("req", "ctx"), None),
            P(("req", "ctx"), None),
            P("ctx", None, None),
            P("ctx", None, None),
            P("ctx", None, None),
        ),
        out_specs=P(("req", "ctx"), None),
        check_vma=False,
    )
```

```python
import itertools
import math

import jax
import jax.numpy as jnp
from jax import lax
from jax.experimental import pallas as pl
from jax.experimental.pallas import tpu as pltpu
from jax.sharding import PartitionSpec as P

HEAD_DIM = 128


def attend_gathered(queries, span_keys, span_values, cache_keys, cache_values, length):
    token_count, column_count = queries.shape
    head_count = column_count // HEAD_DIM
    cached_rows = cache_keys.shape[0]
    block_rows = token_count + cached_rows
    scaling = 1.0 / math.sqrt(HEAD_DIM)
    key_block = jnp.concatenate([span_keys, cache_keys], 0)
    value_block = jnp.concatenate([span_values, cache_values], 0)
    piece_keys = lax.all_gather(key_block, "ctx", axis=0, tiled=True)
    piece_values = lax.all_gather(value_block, "ctx", axis=0, tiled=True)
    piece_rows = piece_keys.shape[0]
    index = jnp.arange(piece_rows, dtype=jnp.int32)
    owner = index // block_rows
    within = index % block_rows
    usable = (within < token_count) | (owner * cached_rows + within - token_count < length)
    scores = (
        jnp.einsum(
            "thd,phd->htp",
            queries.reshape(token_count, head_count, HEAD_DIM),
            piece_keys.reshape(piece_rows, head_count, HEAD_DIM),
            preferred_element_type=jnp.float32,
        )
        * scaling
    )
    scores = jnp.where(usable[None, None, :], scores, -1e30)
    peak = jnp.max(scores, axis=2, keepdims=True)
    weights = jnp.where(usable[None, None, :], jnp.exp(scores - peak), 0.0)
    total = jnp.sum(weights, axis=2)
    accum = jnp.einsum(
        "htp,phd->htd",
        weights.astype(jnp.bfloat16),
        piece_values.reshape(piece_rows, head_count, HEAD_DIM),
        preferred_element_type=jnp.float32,
    )
    return (
        (accum / total[:, :, None])
        .transpose(1, 0, 2)
        .reshape(token_count, column_count)
        .astype(jnp.bfloat16)
    )


def pack_by_destination(sources, extra, width):
    ctx_count = extra.shape[0]
    counts = [x.shape[0] for x in sources] + [extra.shape[1]]
    offsets = [sum(counts[:i]) for i in range(len(counts))]
    total_rows = sum(counts)

    def body(*refs):
        out_ref = refs[-1]

        def one(c, carry):
            columns = pl.ds(pl.multiple_of(c * width, width), width)
            for i, ref in enumerate(refs[:-2]):
                out_ref[c, offsets[i] : offsets[i] + counts[i], :] = ref[:, columns]
            out_ref[c, offsets[-1] :, :] = refs[-2][c]
            return carry

        lax.fori_loop(0, ctx_count, one, 0)

    moved = 2 * total_rows * width * ctx_count * extra.dtype.itemsize
    vmem = pl.BlockSpec(memory_space=pltpu.VMEM)
    return pl.pallas_call(
        body,
        in_specs=[vmem] * (len(sources) + 1),
        out_specs=vmem,
        out_shape=jax.ShapeDtypeStruct((ctx_count, total_rows, width), extra.dtype),
        cost_estimate=pl.CostEstimate(flops=0, transcendentals=0, bytes_accessed=moved),
    )(*sources, extra)


def attend_one_head(query, key, value, usable_row):
    rows, depth = query.shape
    keys = key.shape[0]
    block = 256 if rows % 256 == 0 else rows
    scaling = 1.0 / math.sqrt(HEAD_DIM)

    def body(q_ref, k_ref, v_ref, m_ref, o_ref):
        scores = (
            lax.dot_general(
                q_ref[...],
                k_ref[...],
                (((1,), (1,)), ((), ())),
                preferred_element_type=jnp.float32,
            )
            * scaling
        )
        usable = m_ref[...] != 0
        scores = jnp.where(usable, scores, -1e30)
        peak = jnp.max(scores, axis=1, keepdims=True)
        weights = jnp.where(usable, jnp.exp(scores - peak), 0.0)
        total = jnp.sum(weights, axis=1, keepdims=True)
        accum = jnp.dot(
            weights.astype(jnp.bfloat16), v_ref[...], preferred_element_type=jnp.float32
        )
        o_ref[...] = (accum / total).astype(o_ref.dtype)

    return pl.pallas_call(
        body,
        grid=(rows // block,),
        in_specs=[
            pl.BlockSpec((block, depth), lambda i: (i, 0)),
            pl.BlockSpec((keys, depth), lambda i: (0, 0)),
            pl.BlockSpec((keys, depth), lambda i: (0, 0)),
            pl.BlockSpec((1, keys), lambda i: (0, 0)),
        ],
        out_specs=pl.BlockSpec((block, depth), lambda i: (i, 0)),
        out_shape=jax.ShapeDtypeStruct((rows, depth), query.dtype),
        cost_estimate=pl.CostEstimate(
            flops=4 * rows * keys * depth,
            transcendentals=rows * keys,
            bytes_accessed=2 * (2 * rows * depth + 2 * keys * depth) + 4 * keys,
        ),
    )(query, key, value, usable_row)


def attend_by_head(
    queries, span_keys, span_values, cache_keys, cache_values, length, extra, companion
):
    token_count, column_count = queries.shape
    head_count = column_count // HEAD_DIM
    cached_rows = cache_keys.shape[0]
    ctx_count = lax.axis_size("ctx")
    local_heads = head_count // ctx_count
    width = local_heads * HEAD_DIM
    scaling = 1.0 / math.sqrt(HEAD_DIM)
    block_rows = token_count + cached_rows
    sources = [queries, span_keys, cache_keys, span_values, cache_values]
    base_rows = sum(x.shape[0] for x in sources)
    packed = pack_by_destination(sources, extra, width)
    packed_rows = packed.shape[1]
    got = lax.all_to_all(packed, "ctx", split_axis=0, concat_axis=0, tiled=True)
    got, companion = lax.optimization_barrier((got, companion))
    got = got.reshape(ctx_count, packed_rows, local_heads, HEAD_DIM)
    query_all = got[:, :token_count].reshape(ctx_count * token_count, local_heads, HEAD_DIM)
    key_all = got[:, token_count : token_count + block_rows].reshape(
        ctx_count * block_rows, local_heads, HEAD_DIM
    )
    extra_got = got[:, base_rows:]
    value_all = got[:, token_count + block_rows : base_rows].reshape(
        ctx_count * block_rows, local_heads, HEAD_DIM
    )
    piece_rows = ctx_count * block_rows
    index = jnp.arange(piece_rows, dtype=jnp.int32)
    owner = index // block_rows
    within = index % block_rows
    usable = (within < token_count) | (owner * cached_rows + within - token_count < length)
    usable_row = usable.astype(jnp.int32)[None, :]
    head_out = jnp.stack(
        [
            attend_one_head(query_all[:, h], key_all[:, h], value_all[:, h], usable_row)
            for h in range(local_heads)
        ],
        1,
    )
    head_out = head_out.reshape(ctx_count, token_count, width)
    back = lax.all_to_all(head_out, "ctx", split_axis=0, concat_axis=0, tiled=True)
    return back.transpose(1, 0, 2).reshape(token_count, column_count), extra_got, companion


def on_device(
    hidden_in,
    queries,
    span_keys,
    span_values,
    cache_keys,
    cache_values,
    cache_lengths,
    slot_request,
    out_weight,
    norm_gain,
    expert_ids,
    expert_gates,
    gate_proj,
    up_proj,
    down_proj,
):
    token_count, feature_width = hidden_in.shape
    column_count = queries.shape[1]
    head_count = column_count // HEAD_DIM
    ctx_count = lax.axis_size("ctx")
    slot_place = lax.axis_index("req")
    slot_count = slot_request.shape[0]
    slot_range = jnp.arange(slot_count, dtype=jnp.int32)
    request = jnp.sum(jnp.where(slot_range == slot_place, slot_request, 0))
    length = jnp.sum(jnp.where(slot_range == request, cache_lengths, 0))
    local_experts = gate_proj.shape[0]
    expert_total = local_experts * ctx_count
    gate_matrix = jnp.sum(
        jnp.where(
            expert_ids[:, :, None] == jnp.arange(expert_total, dtype=jnp.int32)[None, None, :],
            expert_gates[:, :, None],
            0.0,
        ),
        axis=1,
    )
    first_expert = lax.axis_index("ctx") * local_experts
    if head_count % ctx_count == 0:
        width = column_count // ctx_count
        high = lax.reduce_precision(gate_matrix, exponent_bits=8, mantissa_bits=7)
        rest = gate_matrix - high
        middle = lax.reduce_precision(rest, exponent_bits=8, mantissa_bits=7)
        low = rest - middle
        parts = jnp.stack([high, middle, low], 0).astype(jnp.bfloat16)
        parts = parts.reshape(3, token_count, ctx_count, local_experts)
        parts = parts.transpose(2, 0, 3, 1).reshape(ctx_count, -1)
        part_len = parts.shape[1]
        part_rows = -(-part_len // width)
        parts = jnp.pad(parts, ((0, 0), (0, part_rows * width - part_len)))
        parts = parts.reshape(ctx_count, part_rows, width)
        hidden_in = route_to_request(hidden_in, slot_request)
        attended, parts_got, hidden_in = attend_by_head(
            queries, span_keys, span_values, cache_keys, cache_values, length, parts, hidden_in
        )
        carried = jnp.concatenate([attended, parts_got.reshape(-1, column_count)], 0)
        carried = route_to_request(carried, slot_request)
        attended = carried[:token_count]
        parts_got = carried[token_count:]
        routed = True
        parts_got = parts_got.reshape(ctx_count, part_rows * width)[:, :part_len]
        parts_got = parts_got.reshape(ctx_count, 3, local_experts, token_count).astype(
            jnp.float32
        )
        local_gates = (
            (parts_got[:, 0] + parts_got[:, 1]) + parts_got[:, 2]
        ).transpose(1, 0, 2)
    else:
        routed = False
        attended = attend_gathered(
            queries, span_keys, span_values, cache_keys, cache_values, length
        )
        local_gates = lax.all_gather(
            lax.dynamic_slice_in_dim(gate_matrix, first_expert, local_experts, 1).T,
            "ctx",
            axis=1,
            tiled=True,
        ).reshape(local_experts, ctx_count, token_count)
    residual = hidden_in.astype(jnp.float32) + jnp.dot(
        attended, out_weight, preferred_element_type=jnp.float32
    )
    mean_square = jnp.mean(residual * residual, axis=1, keepdims=True)
    normed = (residual * lax.rsqrt(mean_square + 1e-06) * norm_gain).astype(jnp.bfloat16)

    def experts_on(rows, gates):
        moe = None
        for j in range(local_experts):
            gate_val = jnp.dot(rows, gate_proj[j], preferred_element_type=jnp.float32)
            up_val = jnp.dot(rows, up_proj[j], preferred_element_type=jnp.float32)
            activated = (jax.nn.silu(gate_val) * up_val).astype(jnp.bfloat16)
            activated = lax.optimization_barrier(activated)
            produced = jnp.dot(
                activated, down_proj[j], preferred_element_type=jnp.float32
            ).astype(jnp.bfloat16)
            term = gates[j][:, None] * produced.astype(jnp.float32)
            moe = term if moe is None else moe + term
        return moe

    if ctx_count & (ctx_count - 1) == 0 and ctx_count > 1 and token_count % 4 == 0:
        me = lax.axis_index("ctx")
        stream_rows = token_count // 4
        orders = xor_orders(ctx_count)
        moe_pieces = []
        earlier = None
        pending = None
        steps = len(orders[0])
        for group in range(2):
            firsts = [(2 * group + s) * stream_rows for s in range(2)]
            inputs = [normed[f : f + stream_rows] for f in firsts]
            if earlier is not None:
                inputs, _ = lax.optimization_barrier((inputs, earlier))
            helds = gather_xor(inputs, orders, ctx_count)
            earlier = helds
            gates = []
            for first, order in zip(firsts, orders):
                sources = jnp.array(relative_masks(order), jnp.int32) ^ me
                gates.append(
                    jnp.take(
                        local_gates[:, :, first : first + stream_rows], sources, axis=1
                    ).reshape(local_experts, ctx_count * stream_rows)
                )
            rows = jnp.concatenate(
                [held.reshape(ctx_count * stream_rows, feature_width) for held in helds], 0
            )
            if pending is not None:
                rows, pending = lax.optimization_barrier((rows, pending))
                moe_pieces.extend(reduce_xor(pending, orders, ctx_count, steps - 1))
            part = experts_on(rows, jnp.concatenate(gates, 1))
            part = part.reshape(2, ctx_count, stream_rows, feature_width)
            pending = reduce_xor([part[0], part[1]], orders, ctx_count, steps, steps - 1)
        moe_pieces.extend(reduce_xor(pending, orders, ctx_count, steps - 1))
        moe_rows = jnp.concatenate(moe_pieces, 0)
    else:
        normed_all = lax.all_gather(normed, "ctx", axis=0, tiled=True)
        moe = experts_on(normed_all, local_gates.reshape(local_experts, -1))
        moe_rows = lax.psum_scatter(
            moe.astype(jnp.bfloat16), "ctx", scatter_dimension=0, tiled=True
        ).astype(jnp.float32)
    final = (residual + moe_rows).astype(jnp.bfloat16)

    if routed:
        return final
    return route_to_request(final, slot_request)


def xor_orders(ctx_count):
    bits = ctx_count.bit_length() - 1
    first = list(range(bits - 1, -1, -1))
    second = list(first)
    if bits >= 3:
        second[0], second[1] = second[1], second[0]
    return [first, second]


def relative_masks(order):
    return [
        sum(((f >> step) & 1) << bit for step, bit in enumerate(order))
        for f in range(1 << len(order))
    ]


def swap(rows, mask, ctx_count):
    return lax.ppermute(rows, "ctx", [(c, c ^ mask) for c in range(ctx_count)])


def gather_xor(rows_list, orders, ctx_count):
    helds = [rows[None] for rows in rows_list]
    for step in range(len(orders[0])):
        masks = [1 << order[step] for order in orders]
        if all(mask == masks[0] for mask in masks):
            got = swap(jnp.stack(helds), masks[0], ctx_count)
            gots = [got[i] for i in range(len(helds))]
        else:
            gots = [swap(held, mask, ctx_count) for held, mask in zip(helds, masks)]
        helds = [jnp.concatenate([held, got], 0) for held, got in zip(helds, gots)]
        helds = list(lax.optimization_barrier(tuple(helds)))
    return helds


def reduce_xor(parts, orders, ctx_count, start=None, stop=0):
    totals = parts
    start = len(orders[0]) if start is None else start
    for step in reversed(range(stop, start)):
        half = totals[0].shape[0] // 2
        masks = [1 << order[step] for order in orders]
        outgoing = [total[half:].astype(jnp.bfloat16) for total in totals]
        if all(mask == masks[0] for mask in masks):
            sent = swap(jnp.stack(outgoing), masks[0], ctx_count)
            sents = [sent[i] for i in range(len(outgoing))]
        else:
            sents = [swap(out, mask, ctx_count) for out, mask in zip(outgoing, masks)]
        totals = [total[:half] + sent.astype(jnp.float32) for total, sent in zip(totals, sents)]
        totals = list(lax.optimization_barrier(tuple(totals)))
    if stop > 0:
        return totals
    return [total[0] for total in totals]


def route_to_request(final, slot_request):
    slot_count = slot_request.shape[0]
    token_count = final.shape[0]
    slot_range = jnp.arange(slot_count, dtype=jnp.int32)
    if slot_count <= 4:
        orders = list(itertools.permutations(range(slot_count)))
        table = jnp.array(orders, jnp.int32)
        match = jnp.all(table == slot_request[None, :], axis=1)
        choice = jnp.sum(jnp.where(match, jnp.arange(len(orders), dtype=jnp.int32), 0))

        def mover(order):
            pairs = [(g, order[g]) for g in range(slot_count)]
            if all(a == b for a, b in pairs):
                return lambda rows: rows
            return lambda rows: lax.ppermute(rows, "req", pairs)

        return lax.switch(choice, [mover(order) for order in orders], final)
    slot_place = lax.axis_index("req")
    source_slot = jnp.sum(jnp.where(slot_request == slot_place, slot_range, 0))
    piece = lax.all_gather(final, "req", axis=0, tiled=True)
    piece_rows = piece.shape[0]
    offset = source_slot * token_count
    inside = (offset >= 0) & (offset + token_count <= piece_rows)
    portion = lax.dynamic_slice_in_dim(
        piece, jnp.clip(offset, 0, piece_rows - token_count), token_count, 0
    )
    return jnp.where(inside, portion, jnp.zeros_like(final))


def solution(mesh):
    return jax.shard_map(
        on_device,
        mesh=mesh,
        in_specs=(
            P(("req", "ctx"), None),
            P(("req", "ctx"), None),
            P(("req", "ctx"), None),
            P(("req", "ctx"), None),
            P(("req", "ctx"), None),
            P(("req", "ctx"), None),
            P(),
            P(),
            P(),
            P(),
            P(("req", "ctx"), None),
            P(("req", "ctx"), None),
            P("ctx", None, None),
            P("ctx", None, None),
            P("ctx", None, None),
        ),
        out_specs=P(("req", "ctx"), None),
        check_vma=False,
    )
```

```python
import itertools
import math

import jax
import jax.numpy as jnp
from jax import lax
from jax.experimental import pallas as pl
from jax.experimental.pallas import tpu as pltpu
from jax.sharding import PartitionSpec as P

HEAD_DIM = 128


def attend_gathered(queries, span_keys, span_values, cache_keys, cache_values, length):
    token_count, column_count = queries.shape
    head_count = column_count // HEAD_DIM
    cached_rows = cache_keys.shape[0]
    block_rows = token_count + cached_rows
    scaling = 1.0 / math.sqrt(HEAD_DIM)
    key_block = jnp.concatenate([span_keys, cache_keys], 0)
    value_block = jnp.concatenate([span_values, cache_values], 0)
    piece_keys = lax.all_gather(key_block, "ctx", axis=0, tiled=True)
    piece_values = lax.all_gather(value_block, "ctx", axis=0, tiled=True)
    piece_rows = piece_keys.shape[0]
    index = jnp.arange(piece_rows, dtype=jnp.int32)
    owner = index // block_rows
    within = index % block_rows
    usable = (within < token_count) | (owner * cached_rows + within - token_count < length)
    scores = (
        jnp.einsum(
            "thd,phd->htp",
            queries.reshape(token_count, head_count, HEAD_DIM),
            piece_keys.reshape(piece_rows, head_count, HEAD_DIM),
            preferred_element_type=jnp.float32,
        )
        * scaling
    )
    scores = jnp.where(usable[None, None, :], scores, -1e30)
    peak = jnp.max(scores, axis=2, keepdims=True)
    weights = jnp.where(usable[None, None, :], jnp.exp(scores - peak), 0.0)
    total = jnp.sum(weights, axis=2)
    accum = jnp.einsum(
        "htp,phd->htd",
        weights.astype(jnp.bfloat16),
        piece_values.reshape(piece_rows, head_count, HEAD_DIM),
        preferred_element_type=jnp.float32,
    )
    return (
        (accum / total[:, :, None])
        .transpose(1, 0, 2)
        .reshape(token_count, column_count)
        .astype(jnp.bfloat16)
    )


def pack_by_destination(sources, extra, width):
    ctx_count = extra.shape[0]
    counts = [x.shape[0] for x in sources] + [extra.shape[1]]
    offsets = [sum(counts[:i]) for i in range(len(counts))]
    total_rows = sum(counts)

    def body(*refs):
        out_ref = refs[-1]

        def one(c, carry):
            columns = pl.ds(pl.multiple_of(c * width, width), width)
            for i, ref in enumerate(refs[:-2]):
                out_ref[c, offsets[i] : offsets[i] + counts[i], :] = ref[:, columns]
            out_ref[c, offsets[-1] :, :] = refs[-2][c]
            return carry

        lax.fori_loop(0, ctx_count, one, 0)

    moved = 2 * total_rows * width * ctx_count * extra.dtype.itemsize
    vmem = pl.BlockSpec(memory_space=pltpu.VMEM)
    return pl.pallas_call(
        body,
        in_specs=[vmem] * (len(sources) + 1),
        out_specs=vmem,
        out_shape=jax.ShapeDtypeStruct((ctx_count, total_rows, width), extra.dtype),
        cost_estimate=pl.CostEstimate(flops=0, transcendentals=0, bytes_accessed=moved),
    )(*sources, extra)


def attend_by_head(
    queries, span_keys, span_values, cache_keys, cache_values, length, extra, companion
):
    token_count, column_count = queries.shape
    head_count = column_count // HEAD_DIM
    cached_rows = cache_keys.shape[0]
    ctx_count = lax.axis_size("ctx")
    local_heads = head_count // ctx_count
    width = local_heads * HEAD_DIM
    scaling = 1.0 / math.sqrt(HEAD_DIM)
    block_rows = token_count + cached_rows
    sources = [queries, span_keys, cache_keys, span_values, cache_values]
    base_rows = sum(x.shape[0] for x in sources)
    packed = pack_by_destination(sources, extra, width)
    packed_rows = packed.shape[1]
    got = lax.all_to_all(packed, "ctx", split_axis=0, concat_axis=0, tiled=True)
    got, companion = lax.optimization_barrier((got, companion))
    got = got.reshape(ctx_count, packed_rows, local_heads, HEAD_DIM)
    query_all = got[:, :token_count].reshape(ctx_count * token_count, local_heads, HEAD_DIM)
    key_all = got[:, token_count : token_count + block_rows].reshape(
        ctx_count * block_rows, local_heads, HEAD_DIM
    )
    extra_got = got[:, base_rows:]
    value_all = got[:, token_count + block_rows : base_rows].reshape(
        ctx_count * block_rows, local_heads, HEAD_DIM
    )
    piece_rows = ctx_count * block_rows
    index = jnp.arange(piece_rows, dtype=jnp.int32)
    owner = index // block_rows
    within = index % block_rows
    usable = (within < token_count) | (owner * cached_rows + within - token_count < length)
    scores = (
        jnp.einsum("thd,phd->htp", query_all, key_all, preferred_element_type=jnp.float32)
        * scaling
    )
    scores = jnp.where(usable[None, None, :], scores, -1e30)
    peak = jnp.max(scores, axis=2, keepdims=True)
    weights = jnp.where(usable[None, None, :], jnp.exp(scores - peak), 0.0)
    total = jnp.sum(weights, axis=2)
    accum = jnp.einsum(
        "htp,phd->thd",
        weights.astype(jnp.bfloat16),
        value_all,
        preferred_element_type=jnp.float32,
    )
    head_out = (accum / total.T[:, :, None]).astype(jnp.bfloat16)
    head_out = head_out.reshape(ctx_count, token_count, width)
    back = lax.all_to_all(head_out, "ctx", split_axis=0, concat_axis=0, tiled=True)
    return back.transpose(1, 0, 2).reshape(token_count, column_count), extra_got, companion


def on_device(
    hidden_in,
    queries,
    span_keys,
    span_values,
    cache_keys,
    cache_values,
    cache_lengths,
    slot_request,
    out_weight,
    norm_gain,
    expert_ids,
    expert_gates,
    gate_proj,
    up_proj,
    down_proj,
):
    token_count, feature_width = hidden_in.shape
    column_count = queries.shape[1]
    head_count = column_count // HEAD_DIM
    ctx_count = lax.axis_size("ctx")
    slot_place = lax.axis_index("req")
    slot_count = slot_request.shape[0]
    slot_range = jnp.arange(slot_count, dtype=jnp.int32)
    request = jnp.sum(jnp.where(slot_range == slot_place, slot_request, 0))
    length = jnp.sum(jnp.where(slot_range == request, cache_lengths, 0))
    local_experts = gate_proj.shape[0]
    expert_total = local_experts * ctx_count
    gate_matrix = jnp.sum(
        jnp.where(
            expert_ids[:, :, None] == jnp.arange(expert_total, dtype=jnp.int32)[None, None, :],
            expert_gates[:, :, None],
            0.0,
        ),
        axis=1,
    )
    first_expert = lax.axis_index("ctx") * local_experts
    if head_count % ctx_count == 0:
        width = column_count // ctx_count
        high = lax.reduce_precision(gate_matrix, exponent_bits=8, mantissa_bits=7)
        rest = gate_matrix - high
        middle = lax.reduce_precision(rest, exponent_bits=8, mantissa_bits=7)
        low = rest - middle
        parts = jnp.stack([high, middle, low], 0).astype(jnp.bfloat16)
        parts = parts.reshape(3, token_count, ctx_count, local_experts)
        parts = parts.transpose(2, 0, 3, 1).reshape(ctx_count, -1)
        part_len = parts.shape[1]
        part_rows = -(-part_len // width)
        parts = jnp.pad(parts, ((0, 0), (0, part_rows * width - part_len)))
        parts = parts.reshape(ctx_count, part_rows, width)
        hidden_in = route_to_request(hidden_in, slot_request)
        attended, parts_got, hidden_in = attend_by_head(
            queries, span_keys, span_values, cache_keys, cache_values, length, parts, hidden_in
        )
        carried = jnp.concatenate([attended, parts_got.reshape(-1, column_count)], 0)
        carried = route_to_request(carried, slot_request)
        attended = carried[:token_count]
        parts_got = carried[token_count:]
        routed = True
        parts_got = parts_got.reshape(ctx_count, part_rows * width)[:, :part_len]
        parts_got = parts_got.reshape(ctx_count, 3, local_experts, token_count).astype(
            jnp.float32
        )
        local_gates = (
            (parts_got[:, 0] + parts_got[:, 1]) + parts_got[:, 2]
        ).transpose(1, 0, 2)
    else:
        routed = False
        attended = attend_gathered(
            queries, span_keys, span_values, cache_keys, cache_values, length
        )
        local_gates = lax.all_gather(
            lax.dynamic_slice_in_dim(gate_matrix, first_expert, local_experts, 1).T,
            "ctx",
            axis=1,
            tiled=True,
        ).reshape(local_experts, ctx_count, token_count)
    residual = hidden_in.astype(jnp.float32) + jnp.dot(
        attended, out_weight, preferred_element_type=jnp.float32
    )
    mean_square = jnp.mean(residual * residual, axis=1, keepdims=True)
    normed = (residual * lax.rsqrt(mean_square + 1e-06) * norm_gain).astype(jnp.bfloat16)

    def experts_on(rows, gates):
        moe = None
        for j in range(local_experts):
            gate_val = jnp.dot(rows, gate_proj[j], preferred_element_type=jnp.float32)
            up_val = jnp.dot(rows, up_proj[j], preferred_element_type=jnp.float32)
            activated = (jax.nn.silu(gate_val) * up_val).astype(jnp.bfloat16)
            activated = lax.optimization_barrier(activated)
            produced = jnp.dot(
                activated, down_proj[j], preferred_element_type=jnp.float32
            ).astype(jnp.bfloat16)
            term = gates[j][:, None] * produced.astype(jnp.float32)
            moe = term if moe is None else moe + term
        return moe

    if ctx_count & (ctx_count - 1) == 0 and ctx_count > 1 and token_count % 4 == 0:
        me = lax.axis_index("ctx")
        group_count = 1
        stream_rows = token_count // (2 * group_count)
        orders = xor_orders(ctx_count)
        moe_pieces = []
        earlier = None
        pending = None
        steps = len(orders[0])
        for group in range(group_count):
            firsts = [(2 * group + s) * stream_rows for s in range(2)]
            inputs = [normed[f : f + stream_rows] for f in firsts]
            if earlier is not None:
                inputs, _ = lax.optimization_barrier((inputs, earlier))
            helds = gather_xor(inputs, orders, ctx_count)
            earlier = helds
            gates = []
            for first, order in zip(firsts, orders):
                sources = jnp.array(relative_masks(order), jnp.int32) ^ me
                gates.append(
                    jnp.take(
                        local_gates[:, :, first : first + stream_rows], sources, axis=1
                    ).reshape(local_experts, ctx_count * stream_rows)
                )
            rows = jnp.concatenate(
                [held.reshape(ctx_count * stream_rows, feature_width) for held in helds], 0
            )
            if pending is not None:
                rows, pending = lax.optimization_barrier((rows, pending))
                moe_pieces.extend(reduce_xor(pending, orders, ctx_count, steps - 1))
            part = experts_on(rows, jnp.concatenate(gates, 1))
            part = part.reshape(2, ctx_count, stream_rows, feature_width)
            pending = reduce_xor([part[0], part[1]], orders, ctx_count, steps, steps - 1)
        moe_pieces.extend(reduce_xor(pending, orders, ctx_count, steps - 1))
        moe_rows = jnp.concatenate(moe_pieces, 0)
    else:
        normed_all = lax.all_gather(normed, "ctx", axis=0, tiled=True)
        moe = experts_on(normed_all, local_gates.reshape(local_experts, -1))
        moe_rows = lax.psum_scatter(
            moe.astype(jnp.bfloat16), "ctx", scatter_dimension=0, tiled=True
        ).astype(jnp.float32)
    final = (residual + moe_rows).astype(jnp.bfloat16)

    if routed:
        return final
    return route_to_request(final, slot_request)


def xor_orders(ctx_count):
    bits = ctx_count.bit_length() - 1
    first = list(range(bits - 1, -1, -1))
    second = list(first)
    if bits >= 3:
        second[0], second[1] = second[1], second[0]
    return [first, second]


def relative_masks(order):
    return [
        sum(((f >> step) & 1) << bit for step, bit in enumerate(order))
        for f in range(1 << len(order))
    ]


def swap(rows, mask, ctx_count):
    return lax.ppermute(rows, "ctx", [(c, c ^ mask) for c in range(ctx_count)])


def gather_xor(rows_list, orders, ctx_count):
    helds = [rows[None] for rows in rows_list]
    for step in range(len(orders[0])):
        masks = [1 << order[step] for order in orders]
        if all(mask == masks[0] for mask in masks):
            got = swap(jnp.stack(helds), masks[0], ctx_count)
            gots = [got[i] for i in range(len(helds))]
        else:
            gots = [swap(held, mask, ctx_count) for held, mask in zip(helds, masks)]
        helds = [jnp.concatenate([held, got], 0) for held, got in zip(helds, gots)]
        helds = list(lax.optimization_barrier(tuple(helds)))
    return helds


def reduce_xor(parts, orders, ctx_count, start=None, stop=0):
    totals = parts
    start = len(orders[0]) if start is None else start
    for step in reversed(range(stop, start)):
        half = totals[0].shape[0] // 2
        masks = [1 << order[step] for order in orders]
        outgoing = [total[half:].astype(jnp.bfloat16) for total in totals]
        if all(mask == masks[0] for mask in masks):
            sent = swap(jnp.stack(outgoing), masks[0], ctx_count)
            sents = [sent[i] for i in range(len(outgoing))]
        else:
            sents = [swap(out, mask, ctx_count) for out, mask in zip(outgoing, masks)]
        totals = [total[:half] + sent.astype(jnp.float32) for total, sent in zip(totals, sents)]
        totals = list(lax.optimization_barrier(tuple(totals)))
    if stop > 0:
        return totals
    return [total[0] for total in totals]


def route_to_request(final, slot_request):
    slot_count = slot_request.shape[0]
    token_count = final.shape[0]
    slot_range = jnp.arange(slot_count, dtype=jnp.int32)
    if slot_count <= 4:
        orders = list(itertools.permutations(range(slot_count)))
        table = jnp.array(orders, jnp.int32)
        match = jnp.all(table == slot_request[None, :], axis=1)
        choice = jnp.sum(jnp.where(match, jnp.arange(len(orders), dtype=jnp.int32), 0))

        def mover(order):
            pairs = [(g, order[g]) for g in range(slot_count)]
            if all(a == b for a, b in pairs):
                return lambda rows: rows
            return lambda rows: lax.ppermute(rows, "req", pairs)

        return lax.switch(choice, [mover(order) for order in orders], final)
    slot_place = lax.axis_index("req")
    source_slot = jnp.sum(jnp.where(slot_request == slot_place, slot_range, 0))
    piece = lax.all_gather(final, "req", axis=0, tiled=True)
    piece_rows = piece.shape[0]
    offset = source_slot * token_count
    inside = (offset >= 0) & (offset + token_count <= piece_rows)
    portion = lax.dynamic_slice_in_dim(
        piece, jnp.clip(offset, 0, piece_rows - token_count), token_count, 0
    )
    return jnp.where(inside, portion, jnp.zeros_like(final))


def solution(mesh):
    return jax.shard_map(
        on_device,
        mesh=mesh,
        in_specs=(
            P(("req", "ctx"), None),
            P(("req", "ctx"), None),
            P(("req", "ctx"), None),
            P(("req", "ctx"), None),
            P(("req", "ctx"), None),
            P(("req", "ctx"), None),
            P(),
            P(),
            P(),
            P(),
            P(("req", "ctx"), None),
            P(("req", "ctx"), None),
            P("ctx", None, None),
            P("ctx", None, None),
            P("ctx", None, None),
        ),
        out_specs=P(("req", "ctx"), None),
        check_vma=False,
    )
```

```python
import itertools
import math

import jax
import jax.numpy as jnp
from jax import lax
from jax.experimental import pallas as pl
from jax.experimental.pallas import tpu as pltpu
from jax.sharding import PartitionSpec as P

HEAD_DIM = 128


def attend_gathered(queries, span_keys, span_values, cache_keys, cache_values, length):
    token_count, column_count = queries.shape
    head_count = column_count // HEAD_DIM
    cached_rows = cache_keys.shape[0]
    block_rows = token_count + cached_rows
    scaling = 1.0 / math.sqrt(HEAD_DIM)
    key_block = jnp.concatenate([span_keys, cache_keys], 0)
    value_block = jnp.concatenate([span_values, cache_values], 0)
    piece_keys = lax.all_gather(key_block, "ctx", axis=0, tiled=True)
    piece_values = lax.all_gather(value_block, "ctx", axis=0, tiled=True)
    piece_rows = piece_keys.shape[0]
    index = jnp.arange(piece_rows, dtype=jnp.int32)
    owner = index // block_rows
    within = index % block_rows
    usable = (within < token_count) | (owner * cached_rows + within - token_count < length)
    scores = (
        jnp.einsum(
            "thd,phd->htp",
            queries.reshape(token_count, head_count, HEAD_DIM),
            piece_keys.reshape(piece_rows, head_count, HEAD_DIM),
            preferred_element_type=jnp.float32,
        )
        * scaling
    )
    scores = jnp.where(usable[None, None, :], scores, -1e30)
    peak = jnp.max(scores, axis=2, keepdims=True)
    weights = jnp.where(usable[None, None, :], jnp.exp(scores - peak), 0.0)
    total = jnp.sum(weights, axis=2)
    accum = jnp.einsum(
        "htp,phd->htd",
        weights.astype(jnp.bfloat16),
        piece_values.reshape(piece_rows, head_count, HEAD_DIM),
        preferred_element_type=jnp.float32,
    )
    return (
        (accum / total[:, :, None])
        .transpose(1, 0, 2)
        .reshape(token_count, column_count)
        .astype(jnp.bfloat16)
    )


def pack_by_destination(sources, extra, width):
    ctx_count = extra.shape[0]
    counts = [x.shape[0] for x in sources] + [extra.shape[1]]
    offsets = [sum(counts[:i]) for i in range(len(counts))]
    total_rows = sum(counts)

    def body(*refs):
        out_ref = refs[-1]

        def one(c, carry):
            columns = pl.ds(pl.multiple_of(c * width, width), width)
            for i, ref in enumerate(refs[:-2]):
                out_ref[c, offsets[i] : offsets[i] + counts[i], :] = ref[:, columns]
            out_ref[c, offsets[-1] :, :] = refs[-2][c]
            return carry

        lax.fori_loop(0, ctx_count, one, 0)

    moved = 2 * total_rows * width * ctx_count * extra.dtype.itemsize
    vmem = pl.BlockSpec(memory_space=pltpu.VMEM)
    return pl.pallas_call(
        body,
        in_specs=[vmem] * (len(sources) + 1),
        out_specs=vmem,
        out_shape=jax.ShapeDtypeStruct((ctx_count, total_rows, width), extra.dtype),
        cost_estimate=pl.CostEstimate(flops=0, transcendentals=0, bytes_accessed=moved),
    )(*sources, extra)


def attend_by_head(
    queries, span_keys, span_values, cache_keys, cache_values, length, extra, companion
):
    token_count, column_count = queries.shape
    head_count = column_count // HEAD_DIM
    cached_rows = cache_keys.shape[0]
    ctx_count = lax.axis_size("ctx")
    local_heads = head_count // ctx_count
    width = local_heads * HEAD_DIM
    scaling = 1.0 / math.sqrt(HEAD_DIM)
    block_rows = token_count + cached_rows
    sources = [queries, span_keys, cache_keys, span_values, cache_values]
    base_rows = sum(x.shape[0] for x in sources)
    packed = pack_by_destination(sources, extra, width)
    packed_rows = packed.shape[1]
    got = lax.all_to_all(packed, "ctx", split_axis=0, concat_axis=0, tiled=True)
    got, companion = lax.optimization_barrier((got, companion))
    got = got.reshape(ctx_count, packed_rows, local_heads, HEAD_DIM)
    query_all = got[:, :token_count].reshape(ctx_count * token_count, local_heads, HEAD_DIM)
    key_all = got[:, token_count : token_count + block_rows].reshape(
        ctx_count * block_rows, local_heads, HEAD_DIM
    )
    extra_got = got[:, base_rows:]
    value_all = got[:, token_count + block_rows : base_rows].reshape(
        ctx_count * block_rows, local_heads, HEAD_DIM
    )
    piece_rows = ctx_count * block_rows
    index = jnp.arange(piece_rows, dtype=jnp.int32)
    owner = index // block_rows
    within = index % block_rows
    usable = (within < token_count) | (owner * cached_rows + within - token_count < length)
    scores = (
        jnp.einsum("thd,phd->htp", query_all, key_all, preferred_element_type=jnp.float32)
        * scaling
    )
    scores = jnp.where(usable[None, None, :], scores, -1e30)
    peak = jnp.max(scores, axis=2, keepdims=True)
    weights = jnp.where(usable[None, None, :], jnp.exp(scores - peak), 0.0)
    total = jnp.sum(weights, axis=2)
    accum = jnp.einsum(
        "htp,phd->thd",
        weights.astype(jnp.bfloat16),
        value_all,
        preferred_element_type=jnp.float32,
    )
    head_out = (accum / total.T[:, :, None]).astype(jnp.bfloat16)
    head_out = head_out.reshape(ctx_count, token_count, width)
    back = lax.all_to_all(head_out, "ctx", split_axis=0, concat_axis=0, tiled=True)
    return back.transpose(1, 0, 2).reshape(token_count, column_count), extra_got, companion


def on_device(
    hidden_in,
    queries,
    span_keys,
    span_values,
    cache_keys,
    cache_values,
    cache_lengths,
    slot_request,
    out_weight,
    norm_gain,
    expert_ids,
    expert_gates,
    gate_proj,
    up_proj,
    down_proj,
):
    token_count, feature_width = hidden_in.shape
    column_count = queries.shape[1]
    head_count = column_count // HEAD_DIM
    ctx_count = lax.axis_size("ctx")
    slot_place = lax.axis_index("req")
    slot_count = slot_request.shape[0]
    slot_range = jnp.arange(slot_count, dtype=jnp.int32)
    request = jnp.sum(jnp.where(slot_range == slot_place, slot_request, 0))
    length = jnp.sum(jnp.where(slot_range == request, cache_lengths, 0))
    local_experts = gate_proj.shape[0]
    expert_total = local_experts * ctx_count
    gate_matrix = jnp.sum(
        jnp.where(
            expert_ids[:, :, None] == jnp.arange(expert_total, dtype=jnp.int32)[None, None, :],
            expert_gates[:, :, None],
            0.0,
        ),
        axis=1,
    )
    first_expert = lax.axis_index("ctx") * local_experts
    if head_count % ctx_count == 0:
        width = column_count // ctx_count
        high = lax.reduce_precision(gate_matrix, exponent_bits=8, mantissa_bits=7)
        rest = gate_matrix - high
        middle = lax.reduce_precision(rest, exponent_bits=8, mantissa_bits=7)
        low = rest - middle
        parts = jnp.stack([high, middle, low], 0).astype(jnp.bfloat16)
        parts = parts.reshape(3, token_count, ctx_count, local_experts)
        parts = parts.transpose(2, 0, 3, 1).reshape(ctx_count, -1)
        part_len = parts.shape[1]
        part_rows = -(-part_len // width)
        parts = jnp.pad(parts, ((0, 0), (0, part_rows * width - part_len)))
        parts = parts.reshape(ctx_count, part_rows, width)
        hidden_in = route_to_request(hidden_in, slot_request)
        attended, parts_got, hidden_in = attend_by_head(
            queries, span_keys, span_values, cache_keys, cache_values, length, parts, hidden_in
        )
        carried = jnp.concatenate([attended, parts_got.reshape(-1, column_count)], 0)
        carried = route_to_request(carried, slot_request)
        attended = carried[:token_count]
        parts_got = carried[token_count:]
        routed = True
        parts_got = parts_got.reshape(ctx_count, part_rows * width)[:, :part_len]
        parts_got = parts_got.reshape(ctx_count, 3, local_experts, token_count).astype(
            jnp.float32
        )
        local_gates = (
            (parts_got[:, 0] + parts_got[:, 1]) + parts_got[:, 2]
        ).transpose(1, 0, 2)
    else:
        routed = False
        attended = attend_gathered(
            queries, span_keys, span_values, cache_keys, cache_values, length
        )
        local_gates = lax.all_gather(
            lax.dynamic_slice_in_dim(gate_matrix, first_expert, local_experts, 1).T,
            "ctx",
            axis=1,
            tiled=True,
        ).reshape(local_experts, ctx_count, token_count)
    residual = hidden_in.astype(jnp.float32) + jnp.dot(
        attended, out_weight, preferred_element_type=jnp.float32
    )
    mean_square = jnp.mean(residual * residual, axis=1, keepdims=True)
    normed = (residual * lax.rsqrt(mean_square + 1e-06) * norm_gain).astype(jnp.bfloat16)

    def experts_on(rows, gates):
        moe = None
        for j in range(local_experts):
            gate_val = jnp.dot(rows, gate_proj[j], preferred_element_type=jnp.float32)
            up_val = jnp.dot(rows, up_proj[j], preferred_element_type=jnp.float32)
            activated = (jax.nn.silu(gate_val) * up_val).astype(jnp.bfloat16)
            activated = lax.optimization_barrier(activated)
            produced = jnp.dot(
                activated, down_proj[j], preferred_element_type=jnp.float32
            ).astype(jnp.bfloat16)
            term = gates[j][:, None] * produced.astype(jnp.float32)
            moe = term if moe is None else moe + term
        return moe

    if ctx_count & (ctx_count - 1) == 0 and ctx_count > 1 and token_count % 4 == 0:
        me = lax.axis_index("ctx")
        stream_rows = token_count // 2
        orders = xor_orders(ctx_count)
        steps = len(orders[0])
        firsts = [s * stream_rows for s in range(2)]
        inputs = [normed[f : f + stream_rows] for f in firsts]
        helds = gather_xor(inputs, [order[:-1] for order in orders], ctx_count)
        last_mask = 1 << orders[0][-1]
        arrived = swap(jnp.stack(helds), last_mask, ctx_count)
        half_blocks = ctx_count // 2
        gates_own, gates_arrived = [], []
        for first, order in zip(firsts, orders):
            sources = jnp.array(relative_masks(order), jnp.int32) ^ me
            gates = jnp.take(local_gates[:, :, first : first + stream_rows], sources, axis=1)
            gates_own.append(gates[:, :half_blocks].reshape(local_experts, -1))
            gates_arrived.append(gates[:, half_blocks:].reshape(local_experts, -1))
        half_rows = half_blocks * stream_rows
        own_part = experts_on(
            jnp.concatenate([held.reshape(half_rows, feature_width) for held in helds], 0),
            jnp.concatenate(gates_own, 1),
        )
        arrived_part = experts_on(
            arrived.reshape(2 * half_rows, feature_width), jnp.concatenate(gates_arrived, 1)
        )
        returned = swap(arrived_part.astype(jnp.bfloat16), last_mask, ctx_count)
        totals = own_part + returned.astype(jnp.float32)
        totals = totals.reshape(2, half_blocks, stream_rows, feature_width)
        totals = list(lax.optimization_barrier((totals[0], totals[1])))
        moe_pieces = reduce_xor(totals, orders, ctx_count, steps - 1)
        moe_rows = jnp.concatenate(moe_pieces, 0)
    else:
        normed_all = lax.all_gather(normed, "ctx", axis=0, tiled=True)
        moe = experts_on(normed_all, local_gates.reshape(local_experts, -1))
        moe_rows = lax.psum_scatter(
            moe.astype(jnp.bfloat16), "ctx", scatter_dimension=0, tiled=True
        ).astype(jnp.float32)
    final = (residual + moe_rows).astype(jnp.bfloat16)

    if routed:
        return final
    return route_to_request(final, slot_request)


def xor_orders(ctx_count):
    bits = ctx_count.bit_length() - 1
    first = list(range(bits - 1, -1, -1))
    second = list(first)
    if bits >= 3:
        second[0], second[1] = second[1], second[0]
    return [first, second]


def relative_masks(order):
    return [
        sum(((f >> step) & 1) << bit for step, bit in enumerate(order))
        for f in range(1 << len(order))
    ]


def swap(rows, mask, ctx_count):
    return lax.ppermute(rows, "ctx", [(c, c ^ mask) for c in range(ctx_count)])


def gather_xor(rows_list, orders, ctx_count):
    helds = [rows[None] for rows in rows_list]
    for step in range(len(orders[0])):
        masks = [1 << order[step] for order in orders]
        if all(mask == masks[0] for mask in masks):
            got = swap(jnp.stack(helds), masks[0], ctx_count)
            gots = [got[i] for i in range(len(helds))]
        else:
            gots = [swap(held, mask, ctx_count) for held, mask in zip(helds, masks)]
        helds = [jnp.concatenate([held, got], 0) for held, got in zip(helds, gots)]
        helds = list(lax.optimization_barrier(tuple(helds)))
    return helds


def reduce_xor(parts, orders, ctx_count, start=None, stop=0):
    totals = parts
    start = len(orders[0]) if start is None else start
    for step in reversed(range(stop, start)):
        half = totals[0].shape[0] // 2
        masks = [1 << order[step] for order in orders]
        outgoing = [total[half:].astype(jnp.bfloat16) for total in totals]
        if all(mask == masks[0] for mask in masks):
            sent = swap(jnp.stack(outgoing), masks[0], ctx_count)
            sents = [sent[i] for i in range(len(outgoing))]
        else:
            sents = [swap(out, mask, ctx_count) for out, mask in zip(outgoing, masks)]
        totals = [total[:half] + sent.astype(jnp.float32) for total, sent in zip(totals, sents)]
        totals = list(lax.optimization_barrier(tuple(totals)))
    if stop > 0:
        return totals
    return [total[0] for total in totals]


def route_to_request(final, slot_request):
    slot_count = slot_request.shape[0]
    token_count = final.shape[0]
    slot_range = jnp.arange(slot_count, dtype=jnp.int32)
    if slot_count <= 4:
        orders = list(itertools.permutations(range(slot_count)))
        table = jnp.array(orders, jnp.int32)
        match = jnp.all(table == slot_request[None, :], axis=1)
        choice = jnp.sum(jnp.where(match, jnp.arange(len(orders), dtype=jnp.int32), 0))

        def mover(order):
            pairs = [(g, order[g]) for g in range(slot_count)]
            if all(a == b for a, b in pairs):
                return lambda rows: rows
            return lambda rows: lax.ppermute(rows, "req", pairs)

        return lax.switch(choice, [mover(order) for order in orders], final)
    slot_place = lax.axis_index("req")
    source_slot = jnp.sum(jnp.where(slot_request == slot_place, slot_range, 0))
    piece = lax.all_gather(final, "req", axis=0, tiled=True)
    piece_rows = piece.shape[0]
    offset = source_slot * token_count
    inside = (offset >= 0) & (offset + token_count <= piece_rows)
    portion = lax.dynamic_slice_in_dim(
        piece, jnp.clip(offset, 0, piece_rows - token_count), token_count, 0
    )
    return jnp.where(inside, portion, jnp.zeros_like(final))


def solution(mesh):
    return jax.shard_map(
        on_device,
        mesh=mesh,
        in_specs=(
            P(("req", "ctx"), None),
            P(("req", "ctx"), None),
            P(("req", "ctx"), None),
            P(("req", "ctx"), None),
            P(("req", "ctx"), None),
            P(("req", "ctx"), None),
            P(),
            P(),
            P(),
            P(),
            P(("req", "ctx"), None),
            P(("req", "ctx"), None),
            P("ctx", None, None),
            P("ctx", None, None),
            P("ctx", None, None),
        ),
        out_specs=P(("req", "ctx"), None),
        check_vma=False,
    )
```

```python
import itertools
import math

import jax
import jax.numpy as jnp
from jax import lax
from jax.experimental import pallas as pl
from jax.experimental.pallas import tpu as pltpu
from jax.sharding import PartitionSpec as P

HEAD_DIM = 128


def attend_gathered(queries, span_keys, span_values, cache_keys, cache_values, length):
    token_count, column_count = queries.shape
    head_count = column_count // HEAD_DIM
    cached_rows = cache_keys.shape[0]
    block_rows = token_count + cached_rows
    scaling = 1.0 / math.sqrt(HEAD_DIM)
    key_block = jnp.concatenate([span_keys, cache_keys], 0)
    value_block = jnp.concatenate([span_values, cache_values], 0)
    piece_keys = lax.all_gather(key_block, "ctx", axis=0, tiled=True)
    piece_values = lax.all_gather(value_block, "ctx", axis=0, tiled=True)
    piece_rows = piece_keys.shape[0]
    index = jnp.arange(piece_rows, dtype=jnp.int32)
    owner = index // block_rows
    within = index % block_rows
    usable = (within < token_count) | (owner * cached_rows + within - token_count < length)
    scores = (
        jnp.einsum(
            "thd,phd->htp",
            queries.reshape(token_count, head_count, HEAD_DIM),
            piece_keys.reshape(piece_rows, head_count, HEAD_DIM),
            preferred_element_type=jnp.float32,
        )
        * scaling
    )
    scores = jnp.where(usable[None, None, :], scores, -1e30)
    peak = jnp.max(scores, axis=2, keepdims=True)
    weights = jnp.where(usable[None, None, :], jnp.exp(scores - peak), 0.0)
    total = jnp.sum(weights, axis=2)
    accum = jnp.einsum(
        "htp,phd->htd",
        weights.astype(jnp.bfloat16),
        piece_values.reshape(piece_rows, head_count, HEAD_DIM),
        preferred_element_type=jnp.float32,
    )
    return (
        (accum / total[:, :, None])
        .transpose(1, 0, 2)
        .reshape(token_count, column_count)
        .astype(jnp.bfloat16)
    )


def pack_by_destination(sources, extra, width):
    ctx_count = extra.shape[0]
    counts = [x.shape[0] for x in sources] + [extra.shape[1]]
    offsets = [sum(counts[:i]) for i in range(len(counts))]
    total_rows = sum(counts)

    def body(*refs):
        out_ref = refs[-1]

        def one(c, carry):
            columns = pl.ds(pl.multiple_of(c * width, width), width)
            for i, ref in enumerate(refs[:-2]):
                out_ref[c, offsets[i] : offsets[i] + counts[i], :] = ref[:, columns]
            out_ref[c, offsets[-1] :, :] = refs[-2][c]
            return carry

        lax.fori_loop(0, ctx_count, one, 0)

    moved = 2 * total_rows * width * ctx_count * extra.dtype.itemsize
    vmem = pl.BlockSpec(memory_space=pltpu.VMEM)
    return pl.pallas_call(
        body,
        in_specs=[vmem] * (len(sources) + 1),
        out_specs=vmem,
        out_shape=jax.ShapeDtypeStruct((ctx_count, total_rows, width), extra.dtype),
        cost_estimate=pl.CostEstimate(flops=0, transcendentals=0, bytes_accessed=moved),
    )(*sources, extra)


def attend_by_head(
    queries, span_keys, span_values, cache_keys, cache_values, length, extra, companion
):
    token_count, column_count = queries.shape
    head_count = column_count // HEAD_DIM
    cached_rows = cache_keys.shape[0]
    ctx_count = lax.axis_size("ctx")
    local_heads = head_count // ctx_count
    width = local_heads * HEAD_DIM
    scaling = 1.0 / math.sqrt(HEAD_DIM)
    block_rows = token_count + cached_rows
    sources = [queries, span_keys, cache_keys, span_values, cache_values]
    base_rows = sum(x.shape[0] for x in sources)
    packed = pack_by_destination(sources, extra, width)
    packed_rows = packed.shape[1]
    got = lax.all_to_all(packed, "ctx", split_axis=0, concat_axis=0, tiled=True)
    got, companion = lax.optimization_barrier((got, companion))
    got = got.reshape(ctx_count, packed_rows, local_heads, HEAD_DIM)
    query_all = got[:, :token_count].reshape(ctx_count * token_count, local_heads, HEAD_DIM)
    key_all = got[:, token_count : token_count + block_rows].reshape(
        ctx_count * block_rows, local_heads, HEAD_DIM
    )
    extra_got = got[:, base_rows:]
    value_all = got[:, token_count + block_rows : base_rows].reshape(
        ctx_count * block_rows, local_heads, HEAD_DIM
    )
    piece_rows = ctx_count * block_rows
    index = jnp.arange(piece_rows, dtype=jnp.int32)
    owner = index // block_rows
    within = index % block_rows
    usable = (within < token_count) | (owner * cached_rows + within - token_count < length)
    scores = (
        jnp.einsum("thd,phd->htp", query_all, key_all, preferred_element_type=jnp.float32)
        * scaling
    )
    scores = jnp.where(usable[None, None, :], scores, -1e30)
    peak = jnp.max(scores, axis=2, keepdims=True)
    weights = jnp.where(usable[None, None, :], jnp.exp(scores - peak), 0.0)
    total = jnp.sum(weights, axis=2)
    accum = jnp.einsum(
        "htp,phd->thd",
        weights.astype(jnp.bfloat16),
        value_all,
        preferred_element_type=jnp.float32,
    )
    head_out = (accum / total.T[:, :, None]).astype(jnp.bfloat16)
    head_out = head_out.reshape(ctx_count, token_count, width)
    back = lax.all_to_all(head_out, "ctx", split_axis=0, concat_axis=0, tiled=True)
    return back.transpose(1, 0, 2).reshape(token_count, column_count), extra_got, companion


def on_device(
    hidden_in,
    queries,
    span_keys,
    span_values,
    cache_keys,
    cache_values,
    cache_lengths,
    slot_request,
    out_weight,
    norm_gain,
    expert_ids,
    expert_gates,
    gate_proj,
    up_proj,
    down_proj,
):
    token_count, feature_width = hidden_in.shape
    column_count = queries.shape[1]
    head_count = column_count // HEAD_DIM
    ctx_count = lax.axis_size("ctx")
    slot_place = lax.axis_index("req")
    slot_count = slot_request.shape[0]
    slot_range = jnp.arange(slot_count, dtype=jnp.int32)
    request = jnp.sum(jnp.where(slot_range == slot_place, slot_request, 0))
    length = jnp.sum(jnp.where(slot_range == request, cache_lengths, 0))
    local_experts = gate_proj.shape[0]
    expert_total = local_experts * ctx_count
    gate_matrix = jnp.sum(
        jnp.where(
            expert_ids[:, :, None] == jnp.arange(expert_total, dtype=jnp.int32)[None, None, :],
            expert_gates[:, :, None],
            0.0,
        ),
        axis=1,
    )
    first_expert = lax.axis_index("ctx") * local_experts
    if head_count % ctx_count == 0:
        width = column_count // ctx_count
        high = lax.reduce_precision(gate_matrix, exponent_bits=8, mantissa_bits=7)
        rest = gate_matrix - high
        middle = lax.reduce_precision(rest, exponent_bits=8, mantissa_bits=7)
        low = rest - middle
        parts = jnp.stack([high, middle, low], 0).astype(jnp.bfloat16)
        parts = parts.reshape(3, token_count, ctx_count, local_experts)
        parts = parts.transpose(2, 0, 3, 1).reshape(ctx_count, -1)
        part_len = parts.shape[1]
        part_rows = -(-part_len // width)
        parts = jnp.pad(parts, ((0, 0), (0, part_rows * width - part_len)))
        parts = parts.reshape(ctx_count, part_rows, width)
        hidden_in = route_to_request(hidden_in, slot_request)
        attended, parts_got, hidden_in = attend_by_head(
            queries, span_keys, span_values, cache_keys, cache_values, length, parts, hidden_in
        )
        carried = jnp.concatenate([attended, parts_got.reshape(-1, column_count)], 0)
        carried = route_to_request(carried, slot_request)
        attended = carried[:token_count]
        parts_got = carried[token_count:]
        routed = True
        parts_got = parts_got.reshape(ctx_count, part_rows * width)[:, :part_len]
        parts_got = parts_got.reshape(ctx_count, 3, local_experts, token_count).astype(
            jnp.float32
        )
        local_gates = (
            (parts_got[:, 0] + parts_got[:, 1]) + parts_got[:, 2]
        ).transpose(1, 0, 2)
    else:
        routed = False
        attended = attend_gathered(
            queries, span_keys, span_values, cache_keys, cache_values, length
        )
        local_gates = lax.all_gather(
            lax.dynamic_slice_in_dim(gate_matrix, first_expert, local_experts, 1).T,
            "ctx",
            axis=1,
            tiled=True,
        ).reshape(local_experts, ctx_count, token_count)
    residual = hidden_in.astype(jnp.float32) + jnp.dot(
        attended, out_weight, preferred_element_type=jnp.float32
    )
    mean_square = jnp.mean(residual * residual, axis=1, keepdims=True)
    normed = (residual * lax.rsqrt(mean_square + 1e-06) * norm_gain).astype(jnp.bfloat16)

    def experts_on(rows, gates):
        moe = None
        for j in range(local_experts):
            gate_val = jnp.dot(rows, gate_proj[j], preferred_element_type=jnp.float32)
            up_val = jnp.dot(rows, up_proj[j], preferred_element_type=jnp.float32)
            activated = (jax.nn.silu(gate_val) * up_val).astype(jnp.bfloat16)
            activated = lax.optimization_barrier(activated)
            produced = jnp.dot(
                activated, down_proj[j], preferred_element_type=jnp.float32
            ).astype(jnp.bfloat16)
            term = gates[j][:, None] * produced.astype(jnp.float32)
            moe = term if moe is None else moe + term
        return moe

    if ctx_count & (ctx_count - 1) == 0 and ctx_count > 1 and token_count % 4 == 0:
        me = lax.axis_index("ctx")
        stream_rows = token_count // 2
        orders = xor_orders(ctx_count)
        steps = len(orders[0])
        firsts = [s * stream_rows for s in range(2)]
        inputs = [normed[f : f + stream_rows] for f in firsts]
        helds = gather_xor(inputs, [order[:-1] for order in orders], ctx_count)
        last_mask = 1 << orders[0][-1]
        held = jnp.stack(helds)
        arrived = swap(held, last_mask, ctx_count)
        half_blocks = ctx_count // 2
        gates_own, gates_arrived = [], []
        for first, order in zip(firsts, orders):
            sources = jnp.array(relative_masks(order), jnp.int32) ^ me
            gates = jnp.take(local_gates[:, :, first : first + stream_rows], sources, axis=1)
            gates_own.append(gates[:, :half_blocks].reshape(local_experts, -1))
            gates_arrived.append(gates[:, half_blocks:].reshape(local_experts, -1))
        rows = jnp.concatenate([held, arrived], 0).reshape(-1, feature_width)
        part = experts_on(rows, jnp.concatenate(gates_own + gates_arrived, 1))
        part = part.reshape(2, 2, half_blocks, stream_rows, feature_width)
        returned = swap(part[1].astype(jnp.bfloat16), last_mask, ctx_count)
        totals = part[0] + returned.astype(jnp.float32)
        totals = list(lax.optimization_barrier((totals[0], totals[1])))
        moe_pieces = reduce_xor(totals, orders, ctx_count, steps - 1)
        moe_rows = jnp.concatenate(moe_pieces, 0)
    else:
        normed_all = lax.all_gather(normed, "ctx", axis=0, tiled=True)
        moe = experts_on(normed_all, local_gates.reshape(local_experts, -1))
        moe_rows = lax.psum_scatter(
            moe.astype(jnp.bfloat16), "ctx", scatter_dimension=0, tiled=True
        ).astype(jnp.float32)
    final = (residual + moe_rows).astype(jnp.bfloat16)

    if routed:
        return final
    return route_to_request(final, slot_request)


def xor_orders(ctx_count):
    bits = ctx_count.bit_length() - 1
    first = list(range(bits - 1, -1, -1))
    second = list(first)
    if bits >= 3:
        second[0], second[1] = second[1], second[0]
    return [first, second]


def relative_masks(order):
    return [
        sum(((f >> step) & 1) << bit for step, bit in enumerate(order))
        for f in range(1 << len(order))
    ]


def swap(rows, mask, ctx_count):
    return lax.ppermute(rows, "ctx", [(c, c ^ mask) for c in range(ctx_count)])


def gather_xor(rows_list, orders, ctx_count):
    helds = [rows[None] for rows in rows_list]
    for step in range(len(orders[0])):
        masks = [1 << order[step] for order in orders]
        if all(mask == masks[0] for mask in masks):
            got = swap(jnp.stack(helds), masks[0], ctx_count)
            gots = [got[i] for i in range(len(helds))]
        else:
            gots = [swap(held, mask, ctx_count) for held, mask in zip(helds, masks)]
        helds = [jnp.concatenate([held, got], 0) for held, got in zip(helds, gots)]
        helds = list(lax.optimization_barrier(tuple(helds)))
    return helds


def reduce_xor(parts, orders, ctx_count, start=None, stop=0):
    totals = parts
    start = len(orders[0]) if start is None else start
    for step in reversed(range(stop, start)):
        half = totals[0].shape[0] // 2
        masks = [1 << order[step] for order in orders]
        outgoing = [total[half:].astype(jnp.bfloat16) for total in totals]
        if all(mask == masks[0] for mask in masks):
            sent = swap(jnp.stack(outgoing), masks[0], ctx_count)
            sents = [sent[i] for i in range(len(outgoing))]
        else:
            sents = [swap(out, mask, ctx_count) for out, mask in zip(outgoing, masks)]
        totals = [total[:half] + sent.astype(jnp.float32) for total, sent in zip(totals, sents)]
        totals = list(lax.optimization_barrier(tuple(totals)))
    if stop > 0:
        return totals
    return [total[0] for total in totals]


def route_to_request(final, slot_request):
    slot_count = slot_request.shape[0]
    token_count = final.shape[0]
    slot_range = jnp.arange(slot_count, dtype=jnp.int32)
    if slot_count <= 4:
        orders = list(itertools.permutations(range(slot_count)))
        table = jnp.array(orders, jnp.int32)
        match = jnp.all(table == slot_request[None, :], axis=1)
        choice = jnp.sum(jnp.where(match, jnp.arange(len(orders), dtype=jnp.int32), 0))

        def mover(order):
            pairs = [(g, order[g]) for g in range(slot_count)]
            if all(a == b for a, b in pairs):
                return lambda rows: rows
            return lambda rows: lax.ppermute(rows, "req", pairs)

        return lax.switch(choice, [mover(order) for order in orders], final)
    slot_place = lax.axis_index("req")
    source_slot = jnp.sum(jnp.where(slot_request == slot_place, slot_range, 0))
    piece = lax.all_gather(final, "req", axis=0, tiled=True)
    piece_rows = piece.shape[0]
    offset = source_slot * token_count
    inside = (offset >= 0) & (offset + token_count <= piece_rows)
    portion = lax.dynamic_slice_in_dim(
        piece, jnp.clip(offset, 0, piece_rows - token_count), token_count, 0
    )
    return jnp.where(inside, portion, jnp.zeros_like(final))


def solution(mesh):
    return jax.shard_map(
        on_device,
        mesh=mesh,
        in_specs=(
            P(("req", "ctx"), None),
            P(("req", "ctx"), None),
            P(("req", "ctx"), None),
            P(("req", "ctx"), None),
            P(("req", "ctx"), None),
            P(("req", "ctx"), None),
            P(),
            P(),
            P(),
            P(),
            P(("req", "ctx"), None),
            P(("req", "ctx"), None),
            P("ctx", None, None),
            P("ctx", None, None),
            P("ctx", None, None),
        ),
        out_specs=P(("req", "ctx"), None),
        check_vma=False,
    )
```
